512 devices in a mesh: seq: 64 (over x, z), tp: 8 (over y, core).
Axes of the slice: x: 4, y: 4, z: 16, core: 2. Of those that a mesh axis runs over, the one named last changes fastest.
Arguments:
- hidden_in: bfloat16 [8192, 2048], P('seq', 'tp'), may hold values from -3 to 3
- norm_gain: float32 [2048], replicated, may hold values from 0.1 to 1.9
- w_query: bfloat16 [2048, 2048], P(None, 'tp'), may hold values from -0.125 to 0.125
- w_key: bfloat16 [2048, 1024], P(None, 'tp'), may hold values from -0.125 to 0.125
- w_value: bfloat16 [2048, 1024], P(None, 'tp'), may hold values from -0.125 to 0.125
- w_headgate: bfloat16 [2048, 16], P(None, 'tp'), may hold values from -0.125 to 0.125
- w_out: bfloat16 [2048, 2048], P('tp'), may hold values from -0.125 to 0.125
- q_gain: float32 [128], replicated, may hold values from 1.5 to 4
- k_gain: float32 [128], replicated, may hold values from 0.1 to 1.9
- cache_keys: bfloat16 [2, 8192, 1024], P(None, 'seq', 'tp'), as said below
- cache_values: bfloat16 [2, 8192, 1024], P(None, 'seq', 'tp'), may hold values from -6 to 6
- cached_len: int32 [8], replicated, may hold values from 0 to 8192, as said below
- group_of: int32 [8], replicated, may hold values from 0 to 1, as said below
Outputs:
- layer_out: bfloat16 [8192, 2048], P('seq', 'tp')
The draws below stay inside these ranges and needn't reach their ends.
Inputs may be any that keep to these rules, and one draw needn't show every extreme that they name: `cache_keys`: keys of the cached positions, of order one and larger. `cached_len`: some request attends to all 8192 cached positions of its prompt, and some to none. `group_of`: every shared prompt is used by some request.
All inputs are finite; a program needn't handle non-finite values.
Results may differ from the reference program's by a relative error of at most 0.018.
Values may be sent and summed in bfloat16 or wider, within the bound.
No kernel may reach another device: no remote copies, remote signals or barrier semaphores. Data moves between devices by JAX's collectives and lax.ppermute only.
A program may use at most 64 MiB of HBM per device.

```python
import math
import jax
import jax.numpy as jnp
from jax import lax

D = 2048
HEADS = 16
KV_HEADS = 8
HEAD_DIM = 128
SPAN = 1024
CACHE = 8192
GROUPS = 2
TOK_DEV = 128
TOKENS = 8192
REQ = 8


def draw_cache_keys(key, part):
    first_key = jax.random.fold_in(jax.random.fold_in(key, 11), 0)
    drawn = jax.random.normal(first_key, (GROUPS, CACHE, KV_HEADS * HEAD_DIM), jnp.float32)
    return drawn.astype(jnp.bfloat16)


def draw_cached_len(key, part):
    first_key, second_key = jax.random.split(jax.random.fold_in(key, 23))
    drawn = jax.random.randint(first_key, (3, REQ), 0, CACHE + 1, jnp.int32)
    lengths = jnp.min(drawn, 0)
    order = jax.random.permutation(second_key, REQ)
    return lengths.at[order[0]].set(CACHE).at[order[1]].set(0)


def draw_group_of(key, part):
    first_key, second_key = jax.random.split(jax.random.fold_in(key, 37))
    chosen = jax.random.randint(first_key, (REQ,), 0, GROUPS, jnp.int32)
    order = jax.random.permutation(second_key, REQ)
    return chosen.at[order[:GROUPS]].set(jnp.arange(GROUPS, dtype=jnp.int32))


def shard_levels(own_key, dims, shards, low, largest):
    level = 1.0
    for axis_at, parts in shards:
        heights = jax.random.uniform(jax.random.fold_in(jax.random.fold_in(own_key, 6), axis_at), (parts,), jnp.float32, low / len(shards), largest / len(shards))
        level = level * jnp.repeat(jnp.exp(heights), dims[axis_at] // parts).reshape((-1,) + (1,) * (len(dims) - 1 - axis_at))
    return level


def scatter_about(stream_key, dims, width, bound, shards=(), kind=jnp.bfloat16):
    values = width * jax.random.normal(stream_key, dims, jnp.float32)
    if shards:
        values = values * shard_levels(stream_key, dims, shards, -0.22, 0.18)
    return jnp.clip(values, -bound, bound).astype(kind)


def setup_inputs(seed: int = 0) -> dict:
    keys = jax.random.split(jax.random.key(seed), 14)
    return {
        "hidden_in": scatter_about(keys[0], (TOKENS, D), 0.5, 3.0, ((0, 64), (1, 8))),
        "norm_gain": jnp.clip(1.0 + 0.18 * jax.random.normal(keys[1], (D,), jnp.float32), 0.1, 1.9),
        "w_query": scatter_about(keys[2], (D, HEADS * HEAD_DIM), D ** -0.5, 0.125, ((1, 8),)),
        "w_key": scatter_about(keys[3], (D, KV_HEADS * HEAD_DIM), D ** -0.5, 0.125, ((1, 8),)),
        "w_value": scatter_about(keys[4], (D, KV_HEADS * HEAD_DIM), D ** -0.5, 0.125, ((1, 8),)),
        "w_headgate": scatter_about(keys[5], (D, HEADS), D ** -0.5, 0.125, ((1, 8),)),
        "w_out": scatter_about(keys[6], (HEADS * HEAD_DIM, D), (HEADS * HEAD_DIM) ** -0.5, 0.125, ((0, 8),)),
        "q_gain": jnp.clip(jnp.exp(jax.random.uniform(keys[7], (HEAD_DIM,), jnp.float32, math.log(1.5), math.log(4.0))), 1.5, 4.0),
        "k_gain": jnp.clip(1.0 + 0.18 * jax.random.normal(keys[8], (HEAD_DIM,), jnp.float32), 0.1, 1.9),
        "cache_keys": draw_cache_keys(jax.random.fold_in(keys[13], 71), 0),
        "cache_values": scatter_about(keys[10], (GROUPS, CACHE, KV_HEADS * HEAD_DIM), 1.0, 6.0, ((1, 64), (2, 8))),
        "cached_len": draw_cached_len(jax.random.fold_in(keys[13], 71), 0),
        "group_of": draw_group_of(jax.random.fold_in(keys[13], 71), 0),
    }


norm_eps = 1e-06
rope_base = 1000000.0
masked_score = -1e+30

def head_norm(vec, gain):
    return vec * lax.rsqrt(lax.optimization_barrier(jnp.mean(vec * vec, -1, keepdims=True)) + norm_eps) * gain

def rotate(vec, positions):
    half = vec.shape[-1] // 2
    freq = jnp.exp(jnp.arange(half, dtype=jnp.float32) * (-2.0 * math.log(rope_base) / vec.shape[-1]))
    angle = positions.astype(jnp.float32)[:, None] * freq[None, :]
    shape_out = (vec.shape[0],) + (1,) * (vec.ndim - 2) + (half,)
    cosine = jnp.cos(angle).reshape(shape_out)
    sine = jnp.sin(angle).reshape(shape_out)
    first = vec[..., :half]
    second = vec[..., half:]
    return jnp.concatenate([first * cosine - second * sine, second * cosine + first * sine], -1)

def to_requests(array):
    blocks = SPAN // TOK_DEV
    rest = array.shape[1:]
    shaped = array.reshape((blocks, REQ, TOK_DEV) + rest)
    return jnp.swapaxes(shaped, 0, 1).reshape((REQ, SPAN) + rest)

def from_requests(array):
    blocks = SPAN // TOK_DEV
    rest = array.shape[2:]
    shaped = array.reshape((REQ, blocks, TOK_DEV) + rest)
    return jnp.swapaxes(shaped, 0, 1).reshape((TOKENS,) + rest)

def reference(hidden_in, norm_gain, w_query, w_key, w_value, w_headgate, w_out, q_gain, k_gain, cache_keys, cache_values, cached_len, group_of):
    group_size = HEADS // KV_HEADS
    widened = hidden_in.astype(jnp.float32)
    normed = (widened * lax.rsqrt(lax.optimization_barrier(jnp.mean(widened * widened, -1, keepdims=True)) + norm_eps) * norm_gain).astype(jnp.bfloat16)
    query_all = to_requests(jnp.dot(normed, w_query, preferred_element_type=jnp.float32)).reshape(REQ, SPAN, KV_HEADS, group_size, HEAD_DIM)
    key_all = to_requests(jnp.dot(normed, w_key, preferred_element_type=jnp.float32)).reshape(REQ, SPAN, KV_HEADS, HEAD_DIM)
    value_all = to_requests(jnp.dot(normed, w_value, preferred_element_type=jnp.float32).astype(jnp.bfloat16)).reshape(REQ, SPAN, KV_HEADS, HEAD_DIM)
    gate_all = to_requests(jax.nn.sigmoid(jnp.dot(normed, w_headgate, preferred_element_type=jnp.float32))).reshape(REQ, SPAN, KV_HEADS, group_size)
    cache_k = cache_keys.reshape(GROUPS, CACHE, KV_HEADS, HEAD_DIM)
    cache_v = cache_values.reshape(GROUPS, CACHE, KV_HEADS, HEAD_DIM)
    scale = HEAD_DIM ** (-0.5)

    def one_request(inputs):
        query_raw, key_raw, values_new, gates, length, group_id = inputs
        positions = length + jnp.arange(SPAN, dtype=jnp.int32)
        queries = rotate(head_norm(query_raw, q_gain), positions).astype(jnp.bfloat16)
        keys_new = rotate(head_norm(key_raw, k_gain), positions).astype(jnp.bfloat16)
        old_keys = lax.dynamic_index_in_dim(cache_k, group_id, 0, keepdims=False)
        old_values = lax.dynamic_index_in_dim(cache_v, group_id, 0, keepdims=False)
        keys_cat = jnp.concatenate([old_keys, keys_new], 0)
        values_cat = jnp.concatenate([old_values, values_new], 0)
        scores = jnp.einsum('tcgd,kcd->tcgk', queries.astype(jnp.float32), keys_cat.astype(jnp.float32)) * scale
        cache_seen = jnp.broadcast_to((jnp.arange(CACHE, dtype=jnp.int32) < length)[None, :], (SPAN, CACHE))
        row_ids = jnp.arange(SPAN, dtype=jnp.int32)
        span_seen = row_ids[None, :] <= row_ids[:, None]
        visible = jnp.concatenate([cache_seen, span_seen], 1)
        scores = jnp.where(visible[:, None, None, :], scores, masked_score)
        top = lax.optimization_barrier(jnp.max(scores, -1))
        expo = jnp.exp(scores - top[..., None])
        total = lax.optimization_barrier(jnp.sum(expo, -1))
        weights = expo.astype(jnp.bfloat16)
        summed = jnp.einsum('tcgk,kcd->tcgd', weights.astype(jnp.float32), values_cat.astype(jnp.float32))
        mixed = summed / total[..., None] * gates[..., None]
        return mixed.astype(jnp.bfloat16).reshape(SPAN, HEADS * HEAD_DIM)
    mixed_all = lax.map(one_request, (query_all, key_all, value_all, gate_all, cached_len, group_of))
    mixed_all = from_requests(mixed_all)
    projected = jnp.dot(mixed_all, w_out, preferred_element_type=jnp.float32)
    return (widened + projected).astype(jnp.bfloat16)
```

```python
import math

import jax
import jax.numpy as jnp
from jax import lax
from jax.sharding import PartitionSpec as P

SPAN = 1024


norm_eps = 1e-06
rope_base = 1000000.0
masked_score = -1e30


def shifted(value, axis, by):
    peers = lax.axis_size(axis)
    pairs = [(i, i + by) for i in range(peers) if 0 <= i + by < peers]
    return lax.ppermute(value, axis, pairs)


def head_norm(vec, gain):
    return vec * lax.rsqrt(jnp.mean(vec * vec, -1, keepdims=True) + norm_eps) * gain


def rotate(vec, positions):
    half = vec.shape[-1] // 2
    freq = jnp.exp(
        jnp.arange(half, dtype=jnp.float32) * (-2.0 * math.log(rope_base) / vec.shape[-1])
    )
    angle = positions.astype(jnp.float32)[:, None] * freq[None, :]
    shape_out = (vec.shape[0],) + (1,) * (vec.ndim - 2) + (half,)
    cosine = jnp.cos(angle).reshape(shape_out)
    sine = jnp.sin(angle).reshape(shape_out)
    first = vec[..., :half]
    second = vec[..., half:]
    return jnp.concatenate([first * cosine - second * sine, second * cosine + first * sine], -1)


def attend(state_now, queries, keys_block, values_block, visible):
    running_max, running_sum, running_acc = state_now
    scores = jnp.einsum(
        "tcgd,kcd->tcgk", queries, keys_block, preferred_element_type=jnp.float32
    ) * queries.shape[-1] ** (-0.5)
    scores = jnp.where(visible[:, None, None, :], scores, masked_score)
    new_max = jnp.maximum(running_max, jnp.max(scores, -1))
    rescale = jnp.exp(running_max - new_max)
    expo = jnp.exp(scores - new_max[..., None])
    new_sum = running_sum * rescale + jnp.sum(expo, -1)
    update = jnp.einsum(
        "tcgk,kcd->tcgd",
        expo.astype(jnp.bfloat16),
        values_block,
        preferred_element_type=jnp.float32,
    )
    return (new_max, new_sum, running_acc * rescale[..., None] + update)


def per_device(
    hidden_in,
    norm_gain,
    w_query,
    w_key,
    w_value,
    w_headgate,
    w_out,
    q_gain,
    k_gain,
    cache_keys,
    cache_values,
    cached_len,
    group_of,
):
    tok_rows = hidden_in.shape[0]
    head_dim = q_gain.shape[0]
    kv_local = w_key.shape[1] // head_dim
    heads_local = w_query.shape[1] // head_dim
    group_size = heads_local // kv_local
    per_request = SPAN // tok_rows
    seq_size = lax.axis_size("seq")
    req_count = seq_size // per_request
    gathered = lax.all_gather(hidden_in, "tp", axis=1, tiled=True)
    widened = gathered.astype(jnp.float32)
    normed = (
        widened * lax.rsqrt(jnp.mean(widened * widened, -1, keepdims=True) + norm_eps) * norm_gain
    ).astype(jnp.bfloat16)
    seq_index = lax.axis_index("seq")
    local_part = seq_index // req_count
    request = seq_index % req_count
    length = cached_len[request]
    group_id = group_of[request]
    positions = length + local_part * tok_rows + jnp.arange(tok_rows, dtype=jnp.int32)
    query_raw = jnp.dot(normed, w_query, preferred_element_type=jnp.float32).reshape(
        tok_rows, kv_local, group_size, head_dim
    )
    queries = rotate(head_norm(query_raw, q_gain), positions).astype(jnp.bfloat16)
    key_raw = jnp.dot(normed, w_key, preferred_element_type=jnp.float32).reshape(
        tok_rows, kv_local, head_dim
    )
    keys_new = rotate(head_norm(key_raw, k_gain), positions).astype(jnp.bfloat16)
    values_new = (
        jnp.dot(normed, w_value, preferred_element_type=jnp.float32)
        .astype(jnp.bfloat16)
        .reshape(tok_rows, kv_local, head_dim)
    )
    gates = jax.nn.sigmoid(jnp.dot(normed, w_headgate, preferred_element_type=jnp.float32)).reshape(
        tok_rows, kv_local, group_size
    )
    state_now = (
        jnp.full((tok_rows, kv_local, group_size), masked_score, jnp.float32),
        jnp.zeros((tok_rows, kv_local, group_size), jnp.float32),
        jnp.zeros((tok_rows, kv_local, group_size, head_dim), jnp.float32),
    )
    row_ids = jnp.arange(tok_rows, dtype=jnp.int32)
    state_now = attend(
        state_now, queries, keys_new, values_new, row_ids[None, :] <= row_ids[:, None]
    )
    all_seen = jnp.ones((1, tok_rows), bool)
    for distance in range(1, per_request):
        earlier_keys, earlier_values = shifted((keys_new, values_new), "seq", distance * req_count)
        state_now = lax.cond(
            local_part >= distance,
            lambda state_in: attend(state_in, queries, earlier_keys, earlier_values, all_seen),
            lambda state_in: state_in,
            state_now,
        )
    peer_groups = group_of[jnp.arange(seq_size, dtype=jnp.int32) % req_count]
    cache_both = jnp.stack([cache_keys, cache_values], 1)
    outgoing = cache_both[peer_groups]
    incoming = lax.all_to_all(outgoing, "seq", 0, 0, tiled=True)
    row_count = seq_size * cache_keys.shape[1]
    keys_block = incoming[:, 0].reshape(row_count, kv_local, head_dim)
    values_block = incoming[:, 1].reshape(row_count, kv_local, head_dim)
    visible = (jnp.arange(row_count, dtype=jnp.int32) < length)[None, :]
    state_now = lax.cond(
        jnp.int32(0) < length,
        lambda state_old: attend(state_old, queries, keys_block, values_block, visible),
        lambda state_old: state_old,
        state_now,
    )
    running_max, running_sum, running_acc = state_now
    mixed = (
        (running_acc / running_sum[..., None] * gates[..., None])
        .astype(jnp.bfloat16)
        .reshape(tok_rows, heads_local * head_dim)
    )
    partial_out = jnp.dot(mixed, w_out, preferred_element_type=jnp.float32)
    tp_size = lax.axis_size("tp")
    pieces = partial_out.astype(jnp.bfloat16).reshape(tok_rows, tp_size, -1)
    arrived = lax.all_to_all(pieces, "tp", 1, 1, tiled=True)
    summed = jnp.sum(arrived.astype(jnp.float32), 1)
    return (hidden_in.astype(jnp.float32) + summed).astype(jnp.bfloat16)


def solution(mesh):
    in_specs = (
        P("seq", "tp"),
        P(),
        P(None, "tp"),
        P(None, "tp"),
        P(None, "tp"),
        P(None, "tp"),
        P("tp", None),
        P(),
        P(),
        P(None, "seq", "tp"),
        P(None, "seq", "tp"),
        P(),
        P(),
    )
    out_specs = P("seq", "tp")
    return jax.shard_map(
        per_device, mesh=mesh, in_specs=in_specs, out_specs=out_specs, check_vma=False
    )
```

```python
import math

import jax
import jax.numpy as jnp
from jax import lax
from jax.sharding import Mesh, PartitionSpec as P

SPAN = 1024


norm_eps = 1e-06
rope_base = 1000000.0
masked_score = -1e30


def shifted(value, axis, by):
    peers = lax.axis_size(axis)
    pairs = [(i, i + by) for i in range(peers) if 0 <= i + by < peers]
    return lax.ppermute(value, axis, pairs)


def head_norm(vec, gain):
    return vec * lax.rsqrt(jnp.mean(vec * vec, -1, keepdims=True) + norm_eps) * gain


def rotate(vec, positions):
    half = vec.shape[-1] // 2
    freq = jnp.exp(
        jnp.arange(half, dtype=jnp.float32) * (-2.0 * math.log(rope_base) / vec.shape[-1])
    )
    angle = positions.astype(jnp.float32)[:, None] * freq[None, :]
    shape_out = (vec.shape[0],) + (1,) * (vec.ndim - 2) + (half,)
    cosine = jnp.cos(angle).reshape(shape_out)
    sine = jnp.sin(angle).reshape(shape_out)
    first = vec[..., :half]
    second = vec[..., half:]
    return jnp.concatenate([first * cosine - second * sine, second * cosine + first * sine], -1)


def attend(state_now, queries, keys_block, values_block, visible):
    running_max, running_sum, running_acc = state_now
    scores = jnp.einsum(
        "tcgd,kcd->tcgk", queries, keys_block, preferred_element_type=jnp.float32
    ) * queries.shape[-1] ** (-0.5)
    scores = jnp.where(visible[:, None, None, :], scores, masked_score)
    new_max = jnp.maximum(running_max, jnp.max(scores, -1))
    rescale = jnp.exp(running_max - new_max)
    expo = jnp.exp(scores - new_max[..., None])
    new_sum = running_sum * rescale + jnp.sum(expo, -1)
    update = jnp.einsum(
        "tcgk,kcd->tcgd",
        expo.astype(jnp.bfloat16),
        values_block,
        preferred_element_type=jnp.float32,
    )
    return (new_max, new_sum, running_acc * rescale[..., None] + update)


def per_device(
    hidden_in,
    norm_gain,
    w_query,
    w_key,
    w_value,
    w_headgate,
    w_out,
    q_gain,
    k_gain,
    cache_keys,
    cache_values,
    cached_len,
    group_of,
):
    tok_rows = hidden_in.shape[0]
    head_dim = q_gain.shape[0]
    kv_local = w_key.shape[1] // head_dim
    heads_local = w_query.shape[1] // head_dim
    group_size = heads_local // kv_local
    per_request = SPAN // tok_rows
    ring_x = lax.axis_size("sx")
    ring_z = lax.axis_size("sz")
    req_count = ring_x * ring_z // per_request
    pair = ring_z // req_count
    x_index = lax.axis_index("sx")
    z_index = lax.axis_index("sz")
    seq_index = x_index * ring_z + z_index
    request = seq_index % req_count
    local_part = seq_index // req_count
    parity = z_index // req_count
    length = cached_len[request]

    peer_groups = group_of[jnp.arange(ring_z, dtype=jnp.int32) % req_count]
    cache_both = jnp.stack([cache_keys, cache_values], 1)
    incoming = lax.all_to_all(cache_both[peer_groups], "sz", 0, 0, tiled=True)
    cache_rows = ring_z * cache_keys.shape[1]
    keys_cache = incoming[:, 0].reshape(cache_rows, kv_local, head_dim)
    values_cache = incoming[:, 1].reshape(cache_rows, kv_local, head_dim)
    cache_pos = x_index * cache_rows + jnp.arange(cache_rows, dtype=jnp.int32)

    gathered = lax.all_gather(hidden_in, "tp", axis=1, tiled=True)
    widened = gathered.astype(jnp.float32)
    normed = (
        widened * lax.rsqrt(jnp.mean(widened * widened, -1, keepdims=True) + norm_eps) * norm_gain
    ).astype(jnp.bfloat16)
    positions = length + local_part * tok_rows + jnp.arange(tok_rows, dtype=jnp.int32)
    query_raw = jnp.dot(normed, w_query, preferred_element_type=jnp.float32).reshape(
        tok_rows, kv_local, group_size, head_dim
    )
    queries = rotate(head_norm(query_raw, q_gain), positions).astype(jnp.bfloat16)
    key_raw = jnp.dot(normed, w_key, preferred_element_type=jnp.float32).reshape(
        tok_rows, kv_local, head_dim
    )
    keys_new = rotate(head_norm(key_raw, k_gain), positions).astype(jnp.bfloat16)
    values_new = (
        jnp.dot(normed, w_value, preferred_element_type=jnp.float32)
        .astype(jnp.bfloat16)
        .reshape(tok_rows, kv_local, head_dim)
    )
    gates = jax.nn.sigmoid(jnp.dot(normed, w_headgate, preferred_element_type=jnp.float32)).reshape(
        tok_rows, kv_local, group_size
    )

    partner_pairs = [(z, (z + req_count) % ring_z) for z in range(ring_z)]
    partner_keys, partner_values = lax.ppermute((keys_new, values_new), "sz", partner_pairs)
    partner_part = x_index * pair + (pair - 1 - parity)
    all_queries = lax.all_gather(queries, "sx", axis=0, tiled=True)
    query_tok = (
        (jnp.arange(ring_x, dtype=jnp.int32) * pair + parity)[:, None] * tok_rows
        + jnp.arange(tok_rows, dtype=jnp.int32)[None, :]
    ).reshape(-1)
    row_ids = jnp.arange(tok_rows, dtype=jnp.int32)
    key_tok = jnp.concatenate([local_part * tok_rows + row_ids, partner_part * tok_rows + row_ids])
    keys_all = jnp.concatenate([keys_cache, keys_new, partner_keys], 0)
    values_all = jnp.concatenate([values_cache, values_new, partner_values], 0)
    query_count = query_tok.shape[0]
    visible = jnp.concatenate(
        [
            jnp.broadcast_to((cache_pos < length)[None, :], (query_count, cache_rows)),
            key_tok[None, :] <= query_tok[:, None],
        ],
        1,
    )
    scores = jnp.einsum(
        "tcgd,kcd->tcgk", all_queries, keys_all, preferred_element_type=jnp.float32
    ) * head_dim ** (-0.5)
    seen = visible[:, None, None, :]
    scores = jnp.where(seen, scores, masked_score)
    top = jnp.max(scores, -1)
    expo = jnp.where(seen, jnp.exp(scores - top[..., None]), 0.0)
    total = jnp.sum(expo, -1)
    acc = jnp.einsum(
        "tcgk,kcd->tcgd", expo.astype(jnp.bfloat16), values_all, preferred_element_type=jnp.float32
    )
    stats = jnp.stack([top, total], -1).reshape(ring_x, tok_rows, kv_local, group_size, 2)
    acc = acc.reshape(ring_x, tok_rows, kv_local, group_size, head_dim)
    stats_in = lax.all_to_all(stats, "sx", 0, 0, tiled=True)
    acc_in = lax.all_to_all(acc, "sx", 0, 0, tiled=True)
    best = jnp.max(stats_in[..., 0], 0)
    factor = jnp.exp(stats_in[..., 0] - best[None])
    total = jnp.sum(stats_in[..., 1] * factor, 0)
    summed_acc = jnp.sum(acc_in * factor[..., None], 0)
    mixed = (
        (summed_acc / total[..., None] * gates[..., None])
        .astype(jnp.bfloat16)
        .reshape(tok_rows, heads_local * head_dim)
    )
    partial_out = jnp.dot(mixed, w_out, preferred_element_type=jnp.float32)
    tp_size = lax.axis_size("tp")
    pieces = partial_out.astype(jnp.bfloat16).reshape(tok_rows, tp_size, -1)
    arrived = lax.all_to_all(pieces, "tp", 1, 1, tiled=True)
    summed = jnp.sum(arrived.astype(jnp.float32), 1)
    return (hidden_in.astype(jnp.float32) + summed).astype(jnp.bfloat16)


def solution(mesh):
    seq_size = mesh.shape["seq"]
    tp_size = mesh.shape["tp"]
    req_count = seq_size // (SPAN // 128)
    ring_z = 2 * req_count
    ring_x = seq_size // ring_z
    split_mesh = Mesh(mesh.devices.reshape(ring_x, ring_z, tp_size), ("sx", "sz", "tp"))
    seq = ("sx", "sz")
    in_specs = (
        P(seq, "tp"),
        P(),
        P(None, "tp"),
        P(None, "tp"),
        P(None, "tp"),
        P(None, "tp"),
        P("tp", None),
        P(),
        P(),
        P(None, seq, "tp"),
        P(None, seq, "tp"),
        P(),
        P(),
    )
    out_specs = P(seq, "tp")
    return jax.shard_map(
        per_device, mesh=split_mesh, in_specs=in_specs, out_specs=out_specs, check_vma=False
    )
```

```python
import math

import jax
import jax.numpy as jnp
from jax import lax
from jax.experimental import pallas as pl
from jax.experimental.pallas import tpu as pltpu
from jax.sharding import Mesh, PartitionSpec as P

SPAN = 1024


norm_eps = 1e-06
rope_base = 1000000.0
masked_score = -1e30


def shifted(value, axis, by):
    peers = lax.axis_size(axis)
    pairs = [(i, i + by) for i in range(peers) if 0 <= i + by < peers]
    return lax.ppermute(value, axis, pairs)


def head_norm(vec, gain):
    return vec * lax.rsqrt(jnp.mean(vec * vec, -1, keepdims=True) + norm_eps) * gain


def rotate(vec, positions):
    half = vec.shape[-1] // 2
    freq = jnp.exp(
        jnp.arange(half, dtype=jnp.float32) * (-2.0 * math.log(rope_base) / vec.shape[-1])
    )
    angle = positions.astype(jnp.float32)[:, None] * freq[None, :]
    shape_out = (vec.shape[0],) + (1,) * (vec.ndim - 2) + (half,)
    cosine = jnp.cos(angle).reshape(shape_out)
    sine = jnp.sin(angle).reshape(shape_out)
    first = vec[..., :half]
    second = vec[..., half:]
    return jnp.concatenate([first * cosine - second * sine, second * cosine + first * sine], -1)


def attend(state_now, queries, keys_block, values_block, visible):
    running_max, running_sum, running_acc = state_now
    scores = jnp.einsum(
        "tcgd,kcd->tcgk", queries, keys_block, preferred_element_type=jnp.float32
    ) * queries.shape[-1] ** (-0.5)
    scores = jnp.where(visible[:, None, None, :], scores, masked_score)
    new_max = jnp.maximum(running_max, jnp.max(scores, -1))
    rescale = jnp.exp(running_max - new_max)
    expo = jnp.exp(scores - new_max[..., None])
    new_sum = running_sum * rescale + jnp.sum(expo, -1)
    update = jnp.einsum(
        "tcgk,kcd->tcgd",
        expo.astype(jnp.bfloat16),
        values_block,
        preferred_element_type=jnp.float32,
    )
    return (new_max, new_sum, running_acc * rescale[..., None] + update)


def attention_kernel(
    scalars, q_ref, qtok_ref, kc_ref, vc_ref, kn_ref, vn_ref, ktok_ref, acc_ref, top_ref, total_ref
):
    scale = q_ref.shape[-1] ** (-0.5)
    dims = (((1,), (1,)), ((), ()))
    q = q_ref[...]
    cache_scores = lax.dot_general(q, kc_ref[...], dims, preferred_element_type=jnp.float32) * scale
    cache_pos = scalars[1] + lax.broadcasted_iota(jnp.int32, (1, kc_ref.shape[0]), 1)
    cache_seen = cache_pos < scalars[0]
    cache_scores = jnp.where(cache_seen, cache_scores, masked_score)
    new_scores = lax.dot_general(q, kn_ref[...], dims, preferred_element_type=jnp.float32) * scale
    new_seen = ktok_ref[...] <= qtok_ref[...]
    new_scores = jnp.where(new_seen, new_scores, masked_score)
    top = jnp.maximum(
        jnp.max(cache_scores, 1, keepdims=True), jnp.max(new_scores, 1, keepdims=True)
    )
    cache_expo = jnp.where(cache_seen, jnp.exp(cache_scores - top), 0.0)
    new_expo = jnp.where(new_seen, jnp.exp(new_scores - top), 0.0)
    total_ref[...] = jnp.sum(cache_expo, 1, keepdims=True) + jnp.sum(new_expo, 1, keepdims=True)
    top_ref[...] = top
    acc_ref[...] = jnp.dot(
        cache_expo.astype(jnp.bfloat16), vc_ref[...], preferred_element_type=jnp.float32
    ) + jnp.dot(new_expo.astype(jnp.bfloat16), vn_ref[...], preferred_element_type=jnp.float32)


def attention(scalars, q_rows, q_tok, keys_cache, values_cache, keys_new, values_new, key_tok):
    rows, width = q_rows.shape
    cache_rows = keys_cache.shape[0]
    new_rows = keys_new.shape[0]
    block = 256
    full = lambda shape: pl.BlockSpec(shape, lambda i, s: (0, 0))
    row_block = lambda cols: pl.BlockSpec((block, cols), lambda i, s: (i, 0))
    flops = 4 * rows * (cache_rows + new_rows) * width
    return pl.pallas_call(
        attention_kernel,
        out_shape=(
            jax.ShapeDtypeStruct((rows, width), jnp.float32),
            jax.ShapeDtypeStruct((rows, 1), jnp.float32),
            jax.ShapeDtypeStruct((rows, 1), jnp.float32),
        ),
        grid_spec=pltpu.PrefetchScalarGridSpec(
            num_scalar_prefetch=1,
            grid=(rows // block,),
            in_specs=[
                row_block(width),
                row_block(1),
                full((cache_rows, width)),
                full((cache_rows, width)),
                full((new_rows, width)),
                full((new_rows, width)),
                full((1, new_rows)),
            ],
            out_specs=[row_block(width), row_block(1), row_block(1)],
        ),
        cost_estimate=pl.CostEstimate(
            flops=flops,
            transcendentals=rows * (cache_rows + new_rows),
            bytes_accessed=2 * (rows + 2 * cache_rows + 2 * new_rows) * width + 4 * rows * width,
        ),
    )(scalars, q_rows, q_tok, keys_cache, values_cache, keys_new, values_new, key_tok)


def per_device(
    hidden_in,
    norm_gain,
    w_query,
    w_key,
    w_value,
    w_headgate,
    w_out,
    q_gain,
    k_gain,
    cache_keys,
    cache_values,
    cached_len,
    group_of,
):
    tok_rows = hidden_in.shape[0]
    head_dim = q_gain.shape[0]
    kv_local = w_key.shape[1] // head_dim
    heads_local = w_query.shape[1] // head_dim
    group_size = heads_local // kv_local
    per_request = SPAN // tok_rows
    ring_x = lax.axis_size("sx")
    ring_z = lax.axis_size("sz")
    req_count = ring_x * ring_z // per_request
    pair = ring_z // req_count
    x_index = lax.axis_index("sx")
    z_index = lax.axis_index("sz")
    seq_index = x_index * ring_z + z_index
    request = seq_index % req_count
    local_part = seq_index // req_count
    parity = z_index // req_count
    length = cached_len[request]

    peer_groups = group_of[jnp.arange(ring_z, dtype=jnp.int32) % req_count]
    cache_both = jnp.stack([cache_keys, cache_values], 1)
    incoming = lax.all_to_all(cache_both[peer_groups], "sz", 0, 0, tiled=True)
    cache_rows = ring_z * cache_keys.shape[1]
    keys_cache = incoming[:, 0].reshape(cache_rows, kv_local, head_dim)
    values_cache = incoming[:, 1].reshape(cache_rows, kv_local, head_dim)
    cache_pos = x_index * cache_rows + jnp.arange(cache_rows, dtype=jnp.int32)

    gathered = lax.all_gather(hidden_in, "tp", axis=1, tiled=True)
    widened = gathered.astype(jnp.float32)
    normed = (
        widened * lax.rsqrt(jnp.mean(widened * widened, -1, keepdims=True) + norm_eps) * norm_gain
    ).astype(jnp.bfloat16)
    positions = length + local_part * tok_rows + jnp.arange(tok_rows, dtype=jnp.int32)
    query_raw = jnp.dot(normed, w_query, preferred_element_type=jnp.float32).reshape(
        tok_rows, kv_local, group_size, head_dim
    )
    queries = rotate(head_norm(query_raw, q_gain), positions).astype(jnp.bfloat16)
    key_raw = jnp.dot(normed, w_key, preferred_element_type=jnp.float32).reshape(
        tok_rows, kv_local, head_dim
    )
    keys_new = rotate(head_norm(key_raw, k_gain), positions).astype(jnp.bfloat16)
    values_new = (
        jnp.dot(normed, w_value, preferred_element_type=jnp.float32)
        .astype(jnp.bfloat16)
        .reshape(tok_rows, kv_local, head_dim)
    )
    gates = jax.nn.sigmoid(jnp.dot(normed, w_headgate, preferred_element_type=jnp.float32)).reshape(
        tok_rows, kv_local, group_size
    )

    partner_pairs = [(z, (z + req_count) % ring_z) for z in range(ring_z)]
    partner_kv = lax.ppermute(jnp.stack([keys_new, values_new]), "sz", partner_pairs)
    partner_part = x_index * pair + (pair - 1 - parity)
    all_queries = lax.all_gather(queries, "sx", axis=0, tiled=True)
    query_tok = (
        (jnp.arange(ring_x, dtype=jnp.int32) * pair + parity)[:, None] * tok_rows
        + jnp.arange(tok_rows, dtype=jnp.int32)[None, :]
    ).reshape(-1)
    row_ids = jnp.arange(tok_rows, dtype=jnp.int32)
    key_tok = jnp.concatenate([local_part * tok_rows + row_ids, partner_part * tok_rows + row_ids])
    keys_two = jnp.concatenate([keys_new, partner_kv[0]], 0).reshape(-1, head_dim)
    values_two = jnp.concatenate([values_new, partner_kv[1]], 0).reshape(-1, head_dim)
    query_count = query_tok.shape[0]
    scalars = jnp.stack([length, x_index * cache_rows]).astype(jnp.int32)
    acc, top, total = attention(
        scalars,
        all_queries.reshape(-1, head_dim),
        jnp.repeat(query_tok, heads_local)[:, None],
        keys_cache.reshape(cache_rows, head_dim),
        values_cache.reshape(cache_rows, head_dim),
        keys_two,
        values_two,
        key_tok[None, :],
    )
    stats = jnp.concatenate([top, total], -1).reshape(ring_x, tok_rows, kv_local, group_size, 2)
    acc = acc.reshape(ring_x, tok_rows, kv_local, group_size, head_dim)
    stats_in = lax.all_to_all(stats, "sx", 0, 0, tiled=True)
    acc_in = lax.all_to_all(acc, "sx", 0, 0, tiled=True)
    best = jnp.max(stats_in[..., 0], 0)
    factor = jnp.exp(stats_in[..., 0] - best[None])
    total = jnp.sum(stats_in[..., 1] * factor, 0)
    summed_acc = jnp.sum(acc_in * factor[..., None], 0)
    mixed = (
        (summed_acc / total[..., None] * gates[..., None])
        .astype(jnp.bfloat16)
        .reshape(tok_rows, heads_local * head_dim)
    )
    partial_out = jnp.dot(mixed, w_out, preferred_element_type=jnp.float32)
    tp_size = lax.axis_size("tp")
    pieces = partial_out.astype(jnp.bfloat16).reshape(tok_rows, tp_size, -1)
    arrived = lax.all_to_all(pieces, "tp", 1, 1, tiled=True)
    summed = jnp.sum(arrived.astype(jnp.float32), 1)
    return (hidden_in.astype(jnp.float32) + summed).astype(jnp.bfloat16)


def solution(mesh):
    seq_size = mesh.shape["seq"]
    tp_size = mesh.shape["tp"]
    req_count = seq_size // (SPAN // 128)
    ring_z = 2 * req_count
    ring_x = seq_size // ring_z
    split_mesh = Mesh(mesh.devices.reshape(ring_x, ring_z, tp_size), ("sx", "sz", "tp"))
    seq = ("sx", "sz")
    in_specs = (
        P(seq, "tp"),
        P(),
        P(None, "tp"),
        P(None, "tp"),
        P(None, "tp"),
        P(None, "tp"),
        P("tp", None),
        P(),
        P(),
        P(None, seq, "tp"),
        P(None, seq, "tp"),
        P(),
        P(),
    )
    out_specs = P(seq, "tp")
    return jax.shard_map(
        per_device, mesh=split_mesh, in_specs=in_specs, out_specs=out_specs, check_vma=False
    )
```

```python
import math

import jax
import jax.numpy as jnp
from jax import lax
from jax.experimental import pallas as pl
from jax.experimental.pallas import tpu as pltpu
from jax.sharding import Mesh, PartitionSpec as P

SPAN = 1024


norm_eps = 1e-06
rope_base = 1000000.0
masked_score = -1e30


def shifted(value, axis, by):
    peers = lax.axis_size(axis)
    pairs = [(i, i + by) for i in range(peers) if 0 <= i + by < peers]
    return lax.ppermute(value, axis, pairs)


def head_norm(vec, gain):
    return vec * lax.rsqrt(jnp.mean(vec * vec, -1, keepdims=True) + norm_eps) * gain


def rotate(vec, positions):
    half = vec.shape[-1] // 2
    freq = jnp.exp(
        jnp.arange(half, dtype=jnp.float32) * (-2.0 * math.log(rope_base) / vec.shape[-1])
    )
    angle = positions.astype(jnp.float32)[:, None] * freq[None, :]
    shape_out = (vec.shape[0],) + (1,) * (vec.ndim - 2) + (half,)
    cosine = jnp.cos(angle).reshape(shape_out)
    sine = jnp.sin(angle).reshape(shape_out)
    first = vec[..., :half]
    second = vec[..., half:]
    return jnp.concatenate([first * cosine - second * sine, second * cosine + first * sine], -1)


def attend(state_now, queries, keys_block, values_block, visible):
    running_max, running_sum, running_acc = state_now
    scores = jnp.einsum(
        "tcgd,kcd->tcgk", queries, keys_block, preferred_element_type=jnp.float32
    ) * queries.shape[-1] ** (-0.5)
    scores = jnp.where(visible[:, None, None, :], scores, masked_score)
    new_max = jnp.maximum(running_max, jnp.max(scores, -1))
    rescale = jnp.exp(running_max - new_max)
    expo = jnp.exp(scores - new_max[..., None])
    new_sum = running_sum * rescale + jnp.sum(expo, -1)
    update = jnp.einsum(
        "tcgk,kcd->tcgd",
        expo.astype(jnp.bfloat16),
        values_block,
        preferred_element_type=jnp.float32,
    )
    return (new_max, new_sum, running_acc * rescale[..., None] + update)


def attention_kernel(
    scalars, q_ref, qtok_ref, kc_ref, vc_ref, kn_ref, vn_ref, ktok_ref, acc_ref, top_ref, total_ref
):
    scale = q_ref.shape[-1] ** (-0.5)
    dims = (((1,), (1,)), ((), ()))
    q = q_ref[...]
    cache_scores = lax.dot_general(q, kc_ref[...], dims, preferred_element_type=jnp.float32) * scale
    cache_pos = scalars[1] + lax.broadcasted_iota(jnp.int32, (1, kc_ref.shape[0]), 1)
    cache_seen = cache_pos < scalars[0]
    cache_scores = jnp.where(cache_seen, cache_scores, masked_score)
    new_scores = lax.dot_general(q, kn_ref[...], dims, preferred_element_type=jnp.float32) * scale
    new_seen = ktok_ref[...] <= qtok_ref[...]
    new_scores = jnp.where(new_seen, new_scores, masked_score)
    top = jnp.maximum(
        jnp.max(cache_scores, 1, keepdims=True), jnp.max(new_scores, 1, keepdims=True)
    )
    cache_expo = jnp.where(cache_seen, jnp.exp(cache_scores - top), 0.0)
    new_expo = jnp.where(new_seen, jnp.exp(new_scores - top), 0.0)
    total_ref[...] = jnp.sum(cache_expo, 1, keepdims=True) + jnp.sum(new_expo, 1, keepdims=True)
    top_ref[...] = top
    acc_ref[...] = jnp.dot(
        cache_expo.astype(jnp.bfloat16), vc_ref[...], preferred_element_type=jnp.float32
    ) + jnp.dot(new_expo.astype(jnp.bfloat16), vn_ref[...], preferred_element_type=jnp.float32)


def attention(scalars, q_rows, q_tok, keys_cache, values_cache, keys_new, values_new, key_tok):
    rows, width = q_rows.shape
    cache_rows = keys_cache.shape[0]
    new_rows = keys_new.shape[0]
    block = 256
    full = lambda shape: pl.BlockSpec(shape, lambda i, s: (0, 0))
    row_block = lambda cols: pl.BlockSpec((block, cols), lambda i, s: (i, 0))
    flops = 4 * rows * (cache_rows + new_rows) * width
    return pl.pallas_call(
        attention_kernel,
        out_shape=(
            jax.ShapeDtypeStruct((rows, width), jnp.float32),
            jax.ShapeDtypeStruct((rows, 1), jnp.float32),
            jax.ShapeDtypeStruct((rows, 1), jnp.float32),
        ),
        grid_spec=pltpu.PrefetchScalarGridSpec(
            num_scalar_prefetch=1,
            grid=(rows // block,),
            in_specs=[
                row_block(width),
                row_block(1),
                full((cache_rows, width)),
                full((cache_rows, width)),
                full((new_rows, width)),
                full((new_rows, width)),
                full((1, new_rows)),
            ],
            out_specs=[row_block(width), row_block(1), row_block(1)],
        ),
        cost_estimate=pl.CostEstimate(
            flops=flops,
            transcendentals=rows * (cache_rows + new_rows),
            bytes_accessed=2 * (rows + 2 * cache_rows + 2 * new_rows) * width + 4 * rows * width,
        ),
    )(scalars, q_rows, q_tok, keys_cache, values_cache, keys_new, values_new, key_tok)


def per_device(
    hidden_in,
    norm_gain,
    w_query,
    w_key,
    w_value,
    w_headgate,
    w_out,
    q_gain,
    k_gain,
    cache_keys,
    cache_values,
    cached_len,
    group_of,
):
    tok_rows = hidden_in.shape[0]
    head_dim = q_gain.shape[0]
    kv_local = w_key.shape[1] // head_dim
    heads_local = w_query.shape[1] // head_dim
    group_size = heads_local // kv_local
    per_request = SPAN // tok_rows
    ring_x = lax.axis_size("sx")
    ring_z = lax.axis_size("sz")
    req_count = ring_x * ring_z // per_request
    pair = ring_z // req_count
    x_index = lax.axis_index("sx")
    z_index = lax.axis_index("sz")
    seq_index = x_index * ring_z + z_index
    request = seq_index % req_count
    local_part = seq_index // req_count
    parity = z_index // req_count
    length = cached_len[request]

    peer_groups = group_of[jnp.arange(ring_z, dtype=jnp.int32) % req_count]
    cache_both = jnp.stack([cache_keys, cache_values], 1)
    incoming = lax.all_to_all(cache_both[peer_groups], "sz", 0, 0, tiled=True)
    cache_rows = ring_z * cache_keys.shape[1]
    keys_cache = incoming[:, 0].reshape(cache_rows, kv_local, head_dim)
    values_cache = incoming[:, 1].reshape(cache_rows, kv_local, head_dim)
    cache_pos = x_index * cache_rows + jnp.arange(cache_rows, dtype=jnp.int32)

    gathered = lax.all_gather(hidden_in, "tp", axis=1, tiled=True)
    widened = gathered.astype(jnp.float32)
    normed = (
        widened * lax.rsqrt(jnp.mean(widened * widened, -1, keepdims=True) + norm_eps) * norm_gain
    ).astype(jnp.bfloat16)
    positions = length + local_part * tok_rows + jnp.arange(tok_rows, dtype=jnp.int32)
    query_raw = jnp.dot(normed, w_query, preferred_element_type=jnp.float32).reshape(
        tok_rows, kv_local, group_size, head_dim
    )
    queries = rotate(head_norm(query_raw, q_gain), positions).astype(jnp.bfloat16)
    key_raw = jnp.dot(normed, w_key, preferred_element_type=jnp.float32).reshape(
        tok_rows, kv_local, head_dim
    )
    keys_new = rotate(head_norm(key_raw, k_gain), positions).astype(jnp.bfloat16)
    values_new = (
        jnp.dot(normed, w_value, preferred_element_type=jnp.float32)
        .astype(jnp.bfloat16)
        .reshape(tok_rows, kv_local, head_dim)
    )
    gates = jax.nn.sigmoid(jnp.dot(normed, w_headgate, preferred_element_type=jnp.float32)).reshape(
        tok_rows, kv_local, group_size
    )

    partner_pairs = [(z, (z + req_count) % ring_z) for z in range(ring_z)]
    partner_kv = lax.ppermute(jnp.stack([keys_new, values_new]), "sz", partner_pairs)
    partner_part = x_index * pair + (pair - 1 - parity)
    all_queries = lax.all_gather(queries, "sx", axis=0, tiled=True)
    query_tok = (
        (jnp.arange(ring_x, dtype=jnp.int32) * pair + parity)[:, None] * tok_rows
        + jnp.arange(tok_rows, dtype=jnp.int32)[None, :]
    ).reshape(-1)
    row_ids = jnp.arange(tok_rows, dtype=jnp.int32)
    key_tok = jnp.concatenate([local_part * tok_rows + row_ids, partner_part * tok_rows + row_ids])
    keys_two = jnp.concatenate([keys_new, partner_kv[0]], 0).reshape(-1, head_dim)
    values_two = jnp.concatenate([values_new, partner_kv[1]], 0).reshape(-1, head_dim)
    query_count = query_tok.shape[0]
    scalars = jnp.stack([length, x_index * cache_rows]).astype(jnp.int32)
    acc, top, total = attention(
        scalars,
        all_queries.reshape(-1, head_dim),
        jnp.repeat(query_tok, heads_local)[:, None],
        keys_cache.reshape(cache_rows, head_dim),
        values_cache.reshape(cache_rows, head_dim),
        keys_two,
        values_two,
        key_tok[None, :],
    )
    slot_rows = tok_rows * heads_local
    stats = jnp.concatenate([top, total], -1).reshape(ring_x, -1, head_dim)
    packed = jnp.concatenate([acc.reshape(ring_x, slot_rows, head_dim), stats], 1)
    packed_in = lax.all_to_all(packed, "sx", 0, 0, tiled=True)
    acc_in = packed_in[:, :slot_rows].reshape(ring_x, tok_rows, kv_local, group_size, head_dim)
    stats_in = packed_in[:, slot_rows:].reshape(ring_x, tok_rows, kv_local, group_size, 2)
    best = jnp.max(stats_in[..., 0], 0)
    factor = jnp.exp(stats_in[..., 0] - best[None])
    total = jnp.sum(stats_in[..., 1] * factor, 0)
    summed_acc = jnp.sum(acc_in * factor[..., None], 0)
    mixed = (
        (summed_acc / total[..., None] * gates[..., None])
        .astype(jnp.bfloat16)
        .reshape(tok_rows, heads_local * head_dim)
    )
    partial_out = jnp.dot(mixed, w_out, preferred_element_type=jnp.float32)
    tp_size = lax.axis_size("tp")
    pieces = partial_out.astype(jnp.bfloat16).reshape(tok_rows, tp_size, -1)
    arrived = lax.all_to_all(pieces, "tp", 1, 1, tiled=True)
    summed = jnp.sum(arrived.astype(jnp.float32), 1)
    return (hidden_in.astype(jnp.float32) + summed).astype(jnp.bfloat16)


def solution(mesh):
    seq_size = mesh.shape["seq"]
    tp_size = mesh.shape["tp"]
    req_count = seq_size // (SPAN // 128)
    ring_z = 2 * req_count
    ring_x = seq_size // ring_z
    split_mesh = Mesh(mesh.devices.reshape(ring_x, ring_z, tp_size), ("sx", "sz", "tp"))
    seq = ("sx", "sz")
    in_specs = (
        P(seq, "tp"),
        P(),
        P(None, "tp"),
        P(None, "tp"),
        P(None, "tp"),
        P(None, "tp"),
        P("tp", None),
        P(),
        P(),
        P(None, seq, "tp"),
        P(None, seq, "tp"),
        P(),
        P(),
    )
    out_specs = P(seq, "tp")
    return jax.shard_map(
        per_device, mesh=split_mesh, in_specs=in_specs, out_specs=out_specs, check_vma=False
    )
```

```python
import math

import jax
import jax.numpy as jnp
from jax import lax
from jax.experimental import pallas as pl
from jax.experimental.pallas import tpu as pltpu
from jax.sharding import Mesh, PartitionSpec as P

SPAN = 1024


norm_eps = 1e-06
rope_base = 1000000.0
masked_score = -1e30


def shifted(value, axis, by):
    peers = lax.axis_size(axis)
    pairs = [(i, i + by) for i in range(peers) if 0 <= i + by < peers]
    return lax.ppermute(value, axis, pairs)


def head_norm(vec, gain):
    return vec * lax.rsqrt(jnp.mean(vec * vec, -1, keepdims=True) + norm_eps) * gain


def rotate(vec, positions):
    half = vec.shape[-1] // 2
    freq = jnp.exp(
        jnp.arange(half, dtype=jnp.float32) * (-2.0 * math.log(rope_base) / vec.shape[-1])
    )
    angle = positions.astype(jnp.float32)[:, None] * freq[None, :]
    shape_out = (vec.shape[0],) + (1,) * (vec.ndim - 2) + (half,)
    cosine = jnp.cos(angle).reshape(shape_out)
    sine = jnp.sin(angle).reshape(shape_out)
    first = vec[..., :half]
    second = vec[..., half:]
    return jnp.concatenate([first * cosine - second * sine, second * cosine + first * sine], -1)


def attend(state_now, queries, keys_block, values_block, visible):
    running_max, running_sum, running_acc = state_now
    scores = jnp.einsum(
        "tcgd,kcd->tcgk", queries, keys_block, preferred_element_type=jnp.float32
    ) * queries.shape[-1] ** (-0.5)
    scores = jnp.where(visible[:, None, None, :], scores, masked_score)
    new_max = jnp.maximum(running_max, jnp.max(scores, -1))
    rescale = jnp.exp(running_max - new_max)
    expo = jnp.exp(scores - new_max[..., None])
    new_sum = running_sum * rescale + jnp.sum(expo, -1)
    update = jnp.einsum(
        "tcgk,kcd->tcgd",
        expo.astype(jnp.bfloat16),
        values_block,
        preferred_element_type=jnp.float32,
    )
    return (new_max, new_sum, running_acc * rescale[..., None] + update)


def attention_kernel(
    scalars, q_ref, qtok_ref, kc_ref, vc_ref, kn_ref, vn_ref, ktok_ref, acc_ref, top_ref, total_ref
):
    scale = q_ref.shape[-1] ** (-0.5)
    dims = (((1,), (1,)), ((), ()))
    q = q_ref[...]
    cache_scores = lax.dot_general(q, kc_ref[...], dims, preferred_element_type=jnp.float32) * scale
    cache_pos = scalars[1] + lax.broadcasted_iota(jnp.int32, (1, kc_ref.shape[0]), 1)
    cache_seen = cache_pos < scalars[0]
    cache_scores = jnp.where(cache_seen, cache_scores, masked_score)
    new_scores = lax.dot_general(q, kn_ref[...], dims, preferred_element_type=jnp.float32) * scale
    new_seen = ktok_ref[...] <= qtok_ref[...]
    new_scores = jnp.where(new_seen, new_scores, masked_score)
    top = jnp.maximum(
        jnp.max(cache_scores, 1, keepdims=True), jnp.max(new_scores, 1, keepdims=True)
    )
    cache_expo = jnp.where(cache_seen, jnp.exp(cache_scores - top), 0.0)
    new_expo = jnp.where(new_seen, jnp.exp(new_scores - top), 0.0)
    total_ref[...] = jnp.sum(cache_expo, 1, keepdims=True) + jnp.sum(new_expo, 1, keepdims=True)
    top_ref[...] = top
    acc_ref[...] = jnp.dot(
        cache_expo.astype(jnp.bfloat16), vc_ref[...], preferred_element_type=jnp.float32
    ) + jnp.dot(new_expo.astype(jnp.bfloat16), vn_ref[...], preferred_element_type=jnp.float32)


def attention(scalars, q_rows, q_tok, keys_cache, values_cache, keys_new, values_new, key_tok):
    rows, width = q_rows.shape
    cache_rows = keys_cache.shape[0]
    new_rows = keys_new.shape[0]
    block = 256
    full = lambda shape: pl.BlockSpec(shape, lambda i, s: (0, 0))
    row_block = lambda cols: pl.BlockSpec((block, cols), lambda i, s: (i, 0))
    flops = 4 * rows * (cache_rows + new_rows) * width
    return pl.pallas_call(
        attention_kernel,
        out_shape=(
            jax.ShapeDtypeStruct((rows, width), jnp.float32),
            jax.ShapeDtypeStruct((rows, 1), jnp.float32),
            jax.ShapeDtypeStruct((rows, 1), jnp.float32),
        ),
        grid_spec=pltpu.PrefetchScalarGridSpec(
            num_scalar_prefetch=1,
            grid=(rows // block,),
            in_specs=[
                row_block(width),
                row_block(1),
                full((cache_rows, width)),
                full((cache_rows, width)),
                full((new_rows, width)),
                full((new_rows, width)),
                full((1, new_rows)),
            ],
            out_specs=[row_block(width), row_block(1), row_block(1)],
        ),
        cost_estimate=pl.CostEstimate(
            flops=flops,
            transcendentals=rows * (cache_rows + new_rows),
            bytes_accessed=2 * (rows + 2 * cache_rows + 2 * new_rows) * width + 4 * rows * width,
        ),
    )(scalars, q_rows, q_tok, keys_cache, values_cache, keys_new, values_new, key_tok)


def per_device(
    hidden_in,
    norm_gain,
    w_query,
    w_key,
    w_value,
    w_headgate,
    w_out,
    q_gain,
    k_gain,
    cache_keys,
    cache_values,
    cached_len,
    group_of,
):
    tok_rows = hidden_in.shape[0]
    head_dim = q_gain.shape[0]
    kv_local = w_key.shape[1] // head_dim
    heads_local = w_query.shape[1] // head_dim
    group_size = heads_local // kv_local
    per_request = SPAN // tok_rows
    ring_x = lax.axis_size("sx")
    ring_z = lax.axis_size("sz")
    req_count = ring_x * ring_z // per_request
    pair = ring_z // req_count
    x_index = lax.axis_index("sx")
    z_index = lax.axis_index("sz")
    seq_index = x_index * ring_z + z_index
    request = seq_index % req_count
    local_part = seq_index // req_count
    parity = z_index // req_count
    length = cached_len[request]

    peer_groups = group_of[jnp.arange(ring_z, dtype=jnp.int32) % req_count]
    cache_both = jnp.stack([cache_keys, cache_values], 1)
    incoming = lax.all_to_all(cache_both[peer_groups], "sz", 0, 0, tiled=True)
    cache_rows = ring_z * cache_keys.shape[1]
    keys_cache = incoming[:, 0].reshape(cache_rows, kv_local, head_dim)
    values_cache = incoming[:, 1].reshape(cache_rows, kv_local, head_dim)
    cache_pos = x_index * cache_rows + jnp.arange(cache_rows, dtype=jnp.int32)

    gathered = lax.all_gather(hidden_in, "tp", axis=1, tiled=True)
    widened = gathered.astype(jnp.float32)
    normed = (
        widened * lax.rsqrt(jnp.mean(widened * widened, -1, keepdims=True) + norm_eps) * norm_gain
    ).astype(jnp.bfloat16)
    positions = length + local_part * tok_rows + jnp.arange(tok_rows, dtype=jnp.int32)
    query_raw = jnp.dot(normed, w_query, preferred_element_type=jnp.float32).reshape(
        tok_rows, kv_local, group_size, head_dim
    )
    queries = rotate(head_norm(query_raw, q_gain), positions).astype(jnp.bfloat16)
    key_raw = jnp.dot(normed, w_key, preferred_element_type=jnp.float32).reshape(
        tok_rows, kv_local, head_dim
    )
    keys_new = rotate(head_norm(key_raw, k_gain), positions).astype(jnp.bfloat16)
    values_new = (
        jnp.dot(normed, w_value, preferred_element_type=jnp.float32)
        .astype(jnp.bfloat16)
        .reshape(tok_rows, kv_local, head_dim)
    )
    gates = jax.nn.sigmoid(jnp.dot(normed, w_headgate, preferred_element_type=jnp.float32)).reshape(
        tok_rows, kv_local, group_size
    )

    partner_pairs = [(z, (z + req_count) % ring_z) for z in range(ring_z)]
    partner_kv = lax.ppermute(jnp.stack([keys_new, values_new]), "sz", partner_pairs)
    partner_part = x_index * pair + (pair - 1 - parity)
    shifted_queries = [queries] + [
        lax.ppermute(queries, "sx", [(i, (i + step) % ring_x) for i in range(ring_x)])
        for step in range(1, ring_x)
    ]
    source_step = (x_index - jnp.arange(ring_x, dtype=jnp.int32)) % ring_x
    all_queries = jnp.take(jnp.stack(shifted_queries), source_step, axis=0)
    query_tok = (
        (jnp.arange(ring_x, dtype=jnp.int32) * pair + parity)[:, None] * tok_rows
        + jnp.arange(tok_rows, dtype=jnp.int32)[None, :]
    ).reshape(-1)
    row_ids = jnp.arange(tok_rows, dtype=jnp.int32)
    key_tok = jnp.concatenate([local_part * tok_rows + row_ids, partner_part * tok_rows + row_ids])
    keys_two = jnp.concatenate([keys_new, partner_kv[0]], 0).reshape(-1, head_dim)
    values_two = jnp.concatenate([values_new, partner_kv[1]], 0).reshape(-1, head_dim)
    query_count = query_tok.shape[0]
    scalars = jnp.stack([length, x_index * cache_rows]).astype(jnp.int32)
    acc, top, total = attention(
        scalars,
        all_queries.reshape(-1, head_dim),
        jnp.repeat(query_tok, heads_local)[:, None],
        keys_cache.reshape(cache_rows, head_dim),
        values_cache.reshape(cache_rows, head_dim),
        keys_two,
        values_two,
        key_tok[None, :],
    )
    slot_rows = tok_rows * heads_local
    stats = jnp.concatenate([top, total], -1).reshape(ring_x, -1, head_dim)
    packed = jnp.concatenate([acc.reshape(ring_x, slot_rows, head_dim), stats], 1)
    packed_in = lax.all_to_all(packed, "sx", 0, 0, tiled=True)
    acc_in = packed_in[:, :slot_rows].reshape(ring_x, tok_rows, kv_local, group_size, head_dim)
    stats_in = packed_in[:, slot_rows:].reshape(ring_x, tok_rows, kv_local, group_size, 2)
    best = jnp.max(stats_in[..., 0], 0)
    factor = jnp.exp(stats_in[..., 0] - best[None])
    total = jnp.sum(stats_in[..., 1] * factor, 0)
    summed_acc = jnp.sum(acc_in * factor[..., None], 0)
    mixed = (
        (summed_acc / total[..., None] * gates[..., None])
        .astype(jnp.bfloat16)
        .reshape(tok_rows, heads_local * head_dim)
    )
    partial_out = jnp.dot(mixed, w_out, preferred_element_type=jnp.float32)
    tp_size = lax.axis_size("tp")
    pieces = partial_out.astype(jnp.bfloat16).reshape(tok_rows, tp_size, -1)
    arrived = lax.all_to_all(pieces, "tp", 1, 1, tiled=True)
    summed = jnp.sum(arrived.astype(jnp.float32), 1)
    return (hidden_in.astype(jnp.float32) + summed).astype(jnp.bfloat16)


def solution(mesh):
    seq_size = mesh.shape["seq"]
    tp_size = mesh.shape["tp"]
    req_count = seq_size // (SPAN // 128)
    ring_z = 2 * req_count
    ring_x = seq_size // ring_z
    split_mesh = Mesh(mesh.devices.reshape(ring_x, ring_z, tp_size), ("sx", "sz", "tp"))
    seq = ("sx", "sz")
    in_specs = (
        P(seq, "tp"),
        P(),
        P(None, "tp"),
        P(None, "tp"),
        P(None, "tp"),
        P(None, "tp"),
        P("tp", None),
        P(),
        P(),
        P(None, seq, "tp"),
        P(None, seq, "tp"),
        P(),
        P(),
    )
    out_specs = P(seq, "tp")
    return jax.shard_map(
        per_device, mesh=split_mesh, in_specs=in_specs, out_specs=out_specs, check_vma=False
    )
```

```python
import math

import jax
import jax.numpy as jnp
from jax import lax
from jax.experimental import pallas as pl
from jax.experimental.pallas import tpu as pltpu
from jax.sharding import Mesh, PartitionSpec as P

SPAN = 1024


norm_eps = 1e-06
rope_base = 1000000.0
masked_score = -1e30


def shifted(value, axis, by):
    peers = lax.axis_size(axis)
    pairs = [(i, i + by) for i in range(peers) if 0 <= i + by < peers]
    return lax.ppermute(value, axis, pairs)


def head_norm(vec, gain):
    return vec * lax.rsqrt(jnp.mean(vec * vec, -1, keepdims=True) + norm_eps) * gain


def rotate(vec, positions):
    half = vec.shape[-1] // 2
    freq = jnp.exp(
        jnp.arange(half, dtype=jnp.float32) * (-2.0 * math.log(rope_base) / vec.shape[-1])
    )
    angle = positions.astype(jnp.float32)[:, None] * freq[None, :]
    shape_out = (vec.shape[0],) + (1,) * (vec.ndim - 2) + (half,)
    cosine = jnp.cos(angle).reshape(shape_out)
    sine = jnp.sin(angle).reshape(shape_out)
    first = vec[..., :half]
    second = vec[..., half:]
    return jnp.concatenate([first * cosine - second * sine, second * cosine + first * sine], -1)


def attend(state_now, queries, keys_block, values_block, visible):
    running_max, running_sum, running_acc = state_now
    scores = jnp.einsum(
        "tcgd,kcd->tcgk", queries, keys_block, preferred_element_type=jnp.float32
    ) * queries.shape[-1] ** (-0.5)
    scores = jnp.where(visible[:, None, None, :], scores, masked_score)
    new_max = jnp.maximum(running_max, jnp.max(scores, -1))
    rescale = jnp.exp(running_max - new_max)
    expo = jnp.exp(scores - new_max[..., None])
    new_sum = running_sum * rescale + jnp.sum(expo, -1)
    update = jnp.einsum(
        "tcgk,kcd->tcgd",
        expo.astype(jnp.bfloat16),
        values_block,
        preferred_element_type=jnp.float32,
    )
    return (new_max, new_sum, running_acc * rescale[..., None] + update)


def attention_kernel(
    scalars, q_ref, qtok_ref, kc_ref, vc_ref, kn_ref, vn_ref, ktok_ref, acc_ref, top_ref, total_ref
):
    scale = q_ref.shape[-1] ** (-0.5)
    dims = (((1,), (1,)), ((), ()))
    q = q_ref[...]
    cache_scores = lax.dot_general(q, kc_ref[...], dims, preferred_element_type=jnp.float32) * scale
    cache_pos = scalars[1] + lax.broadcasted_iota(jnp.int32, (1, kc_ref.shape[0]), 1)
    cache_seen = cache_pos < scalars[0]
    cache_scores = jnp.where(cache_seen, cache_scores, masked_score)
    new_scores = lax.dot_general(q, kn_ref[...], dims, preferred_element_type=jnp.float32) * scale
    new_seen = ktok_ref[...] <= qtok_ref[...]
    new_scores = jnp.where(new_seen, new_scores, masked_score)
    top = jnp.maximum(
        jnp.max(cache_scores, 1, keepdims=True), jnp.max(new_scores, 1, keepdims=True)
    )
    cache_expo = jnp.where(cache_seen, jnp.exp(cache_scores - top), 0.0)
    new_expo = jnp.where(new_seen, jnp.exp(new_scores - top), 0.0)
    total_ref[...] = jnp.sum(cache_expo, 1, keepdims=True) + jnp.sum(new_expo, 1, keepdims=True)
    top_ref[...] = top
    acc_ref[...] = jnp.dot(
        cache_expo.astype(jnp.bfloat16), vc_ref[...], preferred_element_type=jnp.float32
    ) + jnp.dot(new_expo.astype(jnp.bfloat16), vn_ref[...], preferred_element_type=jnp.float32)


def attention(scalars, q_rows, q_tok, keys_cache, values_cache, keys_new, values_new, key_tok):
    rows, width = q_rows.shape
    cache_rows = keys_cache.shape[0]
    new_rows = keys_new.shape[0]
    block = 256
    full = lambda shape: pl.BlockSpec(shape, lambda i, s: (0, 0))
    row_block = lambda cols: pl.BlockSpec((block, cols), lambda i, s: (i, 0))
    flops = 4 * rows * (cache_rows + new_rows) * width
    return pl.pallas_call(
        attention_kernel,
        out_shape=(
            jax.ShapeDtypeStruct((rows, width), jnp.float32),
            jax.ShapeDtypeStruct((rows, 1), jnp.float32),
            jax.ShapeDtypeStruct((rows, 1), jnp.float32),
        ),
        grid_spec=pltpu.PrefetchScalarGridSpec(
            num_scalar_prefetch=1,
            grid=(rows // block,),
            in_specs=[
                row_block(width),
                row_block(1),
                full((cache_rows, width)),
                full((cache_rows, width)),
                full((new_rows, width)),
                full((new_rows, width)),
                full((1, new_rows)),
            ],
            out_specs=[row_block(width), row_block(1), row_block(1)],
        ),
        cost_estimate=pl.CostEstimate(
            flops=flops,
            transcendentals=rows * (cache_rows + new_rows),
            bytes_accessed=2 * (rows + 2 * cache_rows + 2 * new_rows) * width + 4 * rows * width,
        ),
    )(scalars, q_rows, q_tok, keys_cache, values_cache, keys_new, values_new, key_tok)


def per_device(
    hidden_in,
    norm_gain,
    w_query,
    w_key,
    w_value,
    w_headgate,
    w_out,
    q_gain,
    k_gain,
    cache_keys,
    cache_values,
    cached_len,
    group_of,
):
    tok_rows = hidden_in.shape[0]
    head_dim = q_gain.shape[0]
    kv_local = w_key.shape[1] // head_dim
    heads_local = w_query.shape[1] // head_dim
    group_size = heads_local // kv_local
    per_request = SPAN // tok_rows
    ring_x = lax.axis_size("sx")
    ring_z = lax.axis_size("sz")
    req_count = ring_x * ring_z // per_request
    pair = ring_z // req_count
    x_index = lax.axis_index("sx")
    z_index = lax.axis_index("sz")
    seq_index = x_index * ring_z + z_index
    request = seq_index % req_count
    local_part = seq_index // req_count
    parity = z_index // req_count
    length = cached_len[request]

    peer_groups = group_of[jnp.arange(ring_z, dtype=jnp.int32) % req_count]
    cache_both = jnp.stack([cache_keys, cache_values], 1)
    incoming = lax.all_to_all(cache_both[peer_groups], "sz", 0, 0, tiled=True)
    cache_rows = ring_z * cache_keys.shape[1]
    keys_cache = incoming[:, 0].reshape(cache_rows, kv_local, head_dim)
    values_cache = incoming[:, 1].reshape(cache_rows, kv_local, head_dim)
    cache_pos = x_index * cache_rows + jnp.arange(cache_rows, dtype=jnp.int32)

    partner_pairs = [(z, (z + req_count) % ring_z) for z in range(ring_z)]
    partner_hidden = lax.ppermute(hidden_in, "sz", partner_pairs)
    partner_part = x_index * pair + (pair - 1 - parity)
    both_hidden = jnp.concatenate([hidden_in, partner_hidden], 0)
    gathered = lax.all_gather(both_hidden, "tp", axis=1, tiled=True)
    widened = gathered.astype(jnp.float32)
    normed = (
        widened * lax.rsqrt(jnp.mean(widened * widened, -1, keepdims=True) + norm_eps) * norm_gain
    ).astype(jnp.bfloat16)
    row_ids = jnp.arange(tok_rows, dtype=jnp.int32)
    key_tok = jnp.concatenate([local_part * tok_rows + row_ids, partner_part * tok_rows + row_ids])
    positions = length + key_tok
    own_normed = normed[:tok_rows]
    query_raw = jnp.dot(own_normed, w_query, preferred_element_type=jnp.float32).reshape(
        tok_rows, kv_local, group_size, head_dim
    )
    queries = rotate(head_norm(query_raw, q_gain), positions[:tok_rows]).astype(jnp.bfloat16)
    key_raw = jnp.dot(normed, w_key, preferred_element_type=jnp.float32).reshape(
        2 * tok_rows, kv_local, head_dim
    )
    keys_two = rotate(head_norm(key_raw, k_gain), positions).astype(jnp.bfloat16).reshape(-1, head_dim)
    values_two = (
        jnp.dot(normed, w_value, preferred_element_type=jnp.float32)
        .astype(jnp.bfloat16)
        .reshape(-1, head_dim)
    )
    gates = jax.nn.sigmoid(
        jnp.dot(own_normed, w_headgate, preferred_element_type=jnp.float32)
    ).reshape(tok_rows, kv_local, group_size)

    shifted_queries = [queries] + [
        lax.ppermute(queries, "sx", [(i, (i + step) % ring_x) for i in range(ring_x)])
        for step in range(1, ring_x)
    ]
    source_step = (x_index - jnp.arange(ring_x, dtype=jnp.int32)) % ring_x
    all_queries = jnp.take(jnp.stack(shifted_queries), source_step, axis=0)
    query_tok = (
        (jnp.arange(ring_x, dtype=jnp.int32) * pair + parity)[:, None] * tok_rows
        + jnp.arange(tok_rows, dtype=jnp.int32)[None, :]
    ).reshape(-1)
    query_count = query_tok.shape[0]
    scalars = jnp.stack([length, x_index * cache_rows]).astype(jnp.int32)
    acc, top, total = attention(
        scalars,
        all_queries.reshape(-1, head_dim),
        jnp.repeat(query_tok, heads_local)[:, None],
        keys_cache.reshape(cache_rows, head_dim),
        values_cache.reshape(cache_rows, head_dim),
        keys_two,
        values_two,
        key_tok[None, :],
    )
    slot_rows = tok_rows * heads_local
    stats = jnp.concatenate([top, total], -1).reshape(ring_x, -1, head_dim)
    packed = jnp.concatenate([acc.reshape(ring_x, slot_rows, head_dim), stats], 1)
    packed_in = lax.all_to_all(packed, "sx", 0, 0, tiled=True)
    acc_in = packed_in[:, :slot_rows].reshape(ring_x, tok_rows, kv_local, group_size, head_dim)
    stats_in = packed_in[:, slot_rows:].reshape(ring_x, tok_rows, kv_local, group_size, 2)
    best = jnp.max(stats_in[..., 0], 0)
    factor = jnp.exp(stats_in[..., 0] - best[None])
    total = jnp.sum(stats_in[..., 1] * factor, 0)
    summed_acc = jnp.sum(acc_in * factor[..., None], 0)
    mixed = (
        (summed_acc / total[..., None] * gates[..., None])
        .astype(jnp.bfloat16)
        .reshape(tok_rows, heads_local * head_dim)
    )
    partial_out = jnp.dot(mixed, w_out, preferred_element_type=jnp.float32)
    tp_size = lax.axis_size("tp")
    pieces = partial_out.astype(jnp.bfloat16).reshape(tok_rows, tp_size, -1)
    arrived = lax.all_to_all(pieces, "tp", 1, 1, tiled=True)
    summed = jnp.sum(arrived.astype(jnp.float32), 1)
    return (hidden_in.astype(jnp.float32) + summed).astype(jnp.bfloat16)


def solution(mesh):
    seq_size = mesh.shape["seq"]
    tp_size = mesh.shape["tp"]
    req_count = seq_size // (SPAN // 128)
    ring_z = 2 * req_count
    ring_x = seq_size // ring_z
    split_mesh = Mesh(mesh.devices.reshape(ring_x, ring_z, tp_size), ("sx", "sz", "tp"))
    seq = ("sx", "sz")
    in_specs = (
        P(seq, "tp"),
        P(),
        P(None, "tp"),
        P(None, "tp"),
        P(None, "tp"),
        P(None, "tp"),
        P("tp", None),
        P(),
        P(),
        P(None, seq, "tp"),
        P(None, seq, "tp"),
        P(),
        P(),
    )
    out_specs = P(seq, "tp")
    return jax.shard_map(
        per_device, mesh=split_mesh, in_specs=in_specs, out_specs=out_specs, check_vma=False
    )
```

```python
import math

import jax
import jax.numpy as jnp
from jax import lax
from jax.experimental import pallas as pl
from jax.experimental.pallas import tpu as pltpu
from jax.sharding import Mesh, PartitionSpec as P

SPAN = 1024


norm_eps = 1e-06
rope_base = 1000000.0
masked_score = -1e30


def shifted(value, axis, by):
    peers = lax.axis_size(axis)
    pairs = [(i, i + by) for i in range(peers) if 0 <= i + by < peers]
    return lax.ppermute(value, axis, pairs)


def head_norm(vec, gain):
    return vec * lax.rsqrt(jnp.mean(vec * vec, -1, keepdims=True) + norm_eps) * gain


def rotate(vec, positions):
    half = vec.shape[-1] // 2
    freq = jnp.exp(
        jnp.arange(half, dtype=jnp.float32) * (-2.0 * math.log(rope_base) / vec.shape[-1])
    )
    angle = positions.astype(jnp.float32)[:, None] * freq[None, :]
    shape_out = (vec.shape[0],) + (1,) * (vec.ndim - 2) + (half,)
    cosine = jnp.cos(angle).reshape(shape_out)
    sine = jnp.sin(angle).reshape(shape_out)
    first = vec[..., :half]
    second = vec[..., half:]
    return jnp.concatenate([first * cosine - second * sine, second * cosine + first * sine], -1)


def attend(state_now, queries, keys_block, values_block, visible):
    running_max, running_sum, running_acc = state_now
    scores = jnp.einsum(
        "tcgd,kcd->tcgk", queries, keys_block, preferred_element_type=jnp.float32
    ) * queries.shape[-1] ** (-0.5)
    scores = jnp.where(visible[:, None, None, :], scores, masked_score)
    new_max = jnp.maximum(running_max, jnp.max(scores, -1))
    rescale = jnp.exp(running_max - new_max)
    expo = jnp.exp(scores - new_max[..., None])
    new_sum = running_sum * rescale + jnp.sum(expo, -1)
    update = jnp.einsum(
        "tcgk,kcd->tcgd",
        expo.astype(jnp.bfloat16),
        values_block,
        preferred_element_type=jnp.float32,
    )
    return (new_max, new_sum, running_acc * rescale[..., None] + update)


def attention_kernel(
    scalars, q_ref, qtok_ref, kc_ref, vc_ref, kn_ref, vn_ref, ktok_ref, acc_ref, top_ref, total_ref
):
    scale = q_ref.shape[-1] ** (-0.5)
    dims = (((1,), (1,)), ((), ()))
    q = q_ref[...]
    new_scores = lax.dot_general(q, kn_ref[...], dims, preferred_element_type=jnp.float32) * scale
    new_seen = ktok_ref[...] <= qtok_ref[...]
    new_scores = jnp.where(new_seen, new_scores, masked_score)
    new_top = jnp.max(new_scores, 1, keepdims=True)
    cache_rows = kc_ref.shape[0]
    length, start = scalars[0], scalars[1]

    def finish(top, cache_total, cache_acc):
        new_expo = jnp.where(new_seen, jnp.exp(new_scores - top), 0.0)
        total_ref[...] = cache_total + jnp.sum(new_expo, 1, keepdims=True)
        top_ref[...] = top
        acc_ref[...] = cache_acc + jnp.dot(
            new_expo.astype(jnp.bfloat16), vn_ref[...], preferred_element_type=jnp.float32
        )

    def cache_part(masked):
        cache_scores = (
            lax.dot_general(q, kc_ref[...], dims, preferred_element_type=jnp.float32) * scale
        )
        if masked:
            cache_seen = start + lax.broadcasted_iota(jnp.int32, (1, cache_rows), 1) < length
            cache_scores = jnp.where(cache_seen, cache_scores, masked_score)
        top = jnp.maximum(jnp.max(cache_scores, 1, keepdims=True), new_top)
        cache_expo = jnp.exp(cache_scores - top)
        if masked:
            cache_expo = jnp.where(cache_seen, cache_expo, 0.0)
        cache_acc = jnp.dot(
            cache_expo.astype(jnp.bfloat16), vc_ref[...], preferred_element_type=jnp.float32
        )
        finish(top, jnp.sum(cache_expo, 1, keepdims=True), cache_acc)

    @pl.when(length >= start + cache_rows)
    def _():
        cache_part(False)

    @pl.when(jnp.logical_and(length > start, length < start + cache_rows))
    def _():
        cache_part(True)

    @pl.when(length <= start)
    def _():
        finish(new_top, jnp.zeros_like(new_top), jnp.zeros(acc_ref.shape, jnp.float32))


def attention(scalars, q_rows, q_tok, keys_cache, values_cache, keys_new, values_new, key_tok):
    rows, width = q_rows.shape
    cache_rows = keys_cache.shape[0]
    new_rows = keys_new.shape[0]
    block = 256
    full = lambda shape: pl.BlockSpec(shape, lambda i, s: (0, 0))
    row_block = lambda cols: pl.BlockSpec((block, cols), lambda i, s: (i, 0))
    flops = 4 * rows * (cache_rows + new_rows) * width
    return pl.pallas_call(
        attention_kernel,
        out_shape=(
            jax.ShapeDtypeStruct((rows, width), jnp.float32),
            jax.ShapeDtypeStruct((rows, 1), jnp.float32),
            jax.ShapeDtypeStruct((rows, 1), jnp.float32),
        ),
        grid_spec=pltpu.PrefetchScalarGridSpec(
            num_scalar_prefetch=1,
            grid=(rows // block,),
            in_specs=[
                row_block(width),
                row_block(1),
                full((cache_rows, width)),
                full((cache_rows, width)),
                full((new_rows, width)),
                full((new_rows, width)),
                full((1, new_rows)),
            ],
            out_specs=[row_block(width), row_block(1), row_block(1)],
        ),
        cost_estimate=pl.CostEstimate(
            flops=flops,
            transcendentals=rows * (cache_rows + new_rows),
            bytes_accessed=2 * (rows + 2 * cache_rows + 2 * new_rows) * width + 4 * rows * width,
        ),
    )(scalars, q_rows, q_tok, keys_cache, values_cache, keys_new, values_new, key_tok)


def per_device(
    hidden_in,
    norm_gain,
    w_query,
    w_key,
    w_value,
    w_headgate,
    w_out,
    q_gain,
    k_gain,
    cache_keys,
    cache_values,
    cached_len,
    group_of,
):
    tok_rows = hidden_in.shape[0]
    head_dim = q_gain.shape[0]
    kv_local = w_key.shape[1] // head_dim
    heads_local = w_query.shape[1] // head_dim
    group_size = heads_local // kv_local
    per_request = SPAN // tok_rows
    ring_x = lax.axis_size("sx")
    ring_z = lax.axis_size("sz")
    req_count = ring_x * ring_z // per_request
    pair = ring_z // req_count
    x_index = lax.axis_index("sx")
    z_index = lax.axis_index("sz")
    seq_index = x_index * ring_z + z_index
    request = seq_index % req_count
    local_part = seq_index // req_count
    parity = z_index // req_count
    length = cached_len[request]

    peer_groups = group_of[jnp.arange(ring_z, dtype=jnp.int32) % req_count]
    cache_both = jnp.stack([cache_keys, cache_values], 1)
    incoming = lax.all_to_all(cache_both[peer_groups], "sz", 0, 0, tiled=True)
    cache_rows = ring_z * cache_keys.shape[1]
    keys_cache = incoming[:, 0].reshape(cache_rows, kv_local, head_dim)
    values_cache = incoming[:, 1].reshape(cache_rows, kv_local, head_dim)
    cache_pos = x_index * cache_rows + jnp.arange(cache_rows, dtype=jnp.int32)

    gathered = lax.all_gather(hidden_in, "tp", axis=1, tiled=True)
    widened = gathered.astype(jnp.float32)
    normed = (
        widened * lax.rsqrt(jnp.mean(widened * widened, -1, keepdims=True) + norm_eps) * norm_gain
    ).astype(jnp.bfloat16)
    positions = length + local_part * tok_rows + jnp.arange(tok_rows, dtype=jnp.int32)
    query_raw = jnp.dot(normed, w_query, preferred_element_type=jnp.float32).reshape(
        tok_rows, kv_local, group_size, head_dim
    )
    queries = rotate(head_norm(query_raw, q_gain), positions).astype(jnp.bfloat16)
    key_raw = jnp.dot(normed, w_key, preferred_element_type=jnp.float32).reshape(
        tok_rows, kv_local, head_dim
    )
    keys_new = rotate(head_norm(key_raw, k_gain), positions).astype(jnp.bfloat16)
    values_new = (
        jnp.dot(normed, w_value, preferred_element_type=jnp.float32)
        .astype(jnp.bfloat16)
        .reshape(tok_rows, kv_local, head_dim)
    )
    gates = jax.nn.sigmoid(jnp.dot(normed, w_headgate, preferred_element_type=jnp.float32)).reshape(
        tok_rows, kv_local, group_size
    )

    partner_pairs = [(z, (z + req_count) % ring_z) for z in range(ring_z)]
    partner_kv = lax.ppermute(jnp.stack([keys_new, values_new]), "sz", partner_pairs)
    partner_part = x_index * pair + (pair - 1 - parity)
    all_queries = lax.all_gather(queries, "sx", axis=0, tiled=True)
    query_tok = (
        (jnp.arange(ring_x, dtype=jnp.int32) * pair + parity)[:, None] * tok_rows
        + jnp.arange(tok_rows, dtype=jnp.int32)[None, :]
    ).reshape(-1)
    row_ids = jnp.arange(tok_rows, dtype=jnp.int32)
    key_tok = jnp.concatenate([local_part * tok_rows + row_ids, partner_part * tok_rows + row_ids])
    keys_two = jnp.concatenate([keys_new, partner_kv[0]], 0).reshape(-1, head_dim)
    values_two = jnp.concatenate([values_new, partner_kv[1]], 0).reshape(-1, head_dim)
    query_count = query_tok.shape[0]
    scalars = jnp.stack([length, x_index * cache_rows]).astype(jnp.int32)
    acc, top, total = attention(
        scalars,
        all_queries.reshape(-1, head_dim),
        jnp.repeat(query_tok, heads_local)[:, None],
        keys_cache.reshape(cache_rows, head_dim),
        values_cache.reshape(cache_rows, head_dim),
        keys_two,
        values_two,
        key_tok[None, :],
    )
    slot_rows = tok_rows * heads_local
    stats = jnp.concatenate([top, total], -1).reshape(ring_x, -1, head_dim)
    packed = jnp.concatenate([acc.reshape(ring_x, slot_rows, head_dim), stats], 1)
    packed_in = lax.all_to_all(packed, "sx", 0, 0, tiled=True)
    acc_in = packed_in[:, :slot_rows].reshape(ring_x, tok_rows, kv_local, group_size, head_dim)
    stats_in = packed_in[:, slot_rows:].reshape(ring_x, tok_rows, kv_local, group_size, 2)
    best = jnp.max(stats_in[..., 0], 0)
    factor = jnp.exp(stats_in[..., 0] - best[None])
    total = jnp.sum(stats_in[..., 1] * factor, 0)
    summed_acc = jnp.sum(acc_in * factor[..., None], 0)
    mixed = (
        (summed_acc / total[..., None] * gates[..., None])
        .astype(jnp.bfloat16)
        .reshape(tok_rows, heads_local * head_dim)
    )
    partial_out = jnp.dot(mixed, w_out, preferred_element_type=jnp.float32)
    tp_size = lax.axis_size("tp")
    pieces = partial_out.astype(jnp.bfloat16).reshape(tok_rows, tp_size, -1)
    arrived = lax.all_to_all(pieces, "tp", 1, 1, tiled=True)
    summed = jnp.sum(arrived.astype(jnp.float32), 1)
    return (hidden_in.astype(jnp.float32) + summed).astype(jnp.bfloat16)


def solution(mesh):
    seq_size = mesh.shape["seq"]
    tp_size = mesh.shape["tp"]
    req_count = seq_size // (SPAN // 128)
    ring_z = 2 * req_count
    ring_x = seq_size // ring_z
    split_mesh = Mesh(mesh.devices.reshape(ring_x, ring_z, tp_size), ("sx", "sz", "tp"))
    seq = ("sx", "sz")
    in_specs = (
        P(seq, "tp"),
        P(),
        P(None, "tp"),
        P(None, "tp"),
        P(None, "tp"),
        P(None, "tp"),
        P("tp", None),
        P(),
        P(),
        P(None, seq, "tp"),
        P(None, seq, "tp"),
        P(),
        P(),
    )
    out_specs = P(seq, "tp")
    return jax.shard_map(
        per_device, mesh=split_mesh, in_specs=in_specs, out_specs=out_specs, check_vma=False
    )
```

```python
import math

import jax
import jax.numpy as jnp
from jax import lax
from jax.experimental import pallas as pl
from jax.experimental.pallas import tpu as pltpu
from jax.sharding import Mesh, PartitionSpec as P

SPAN = 1024


norm_eps = 1e-06
rope_base = 1000000.0
masked_score = -1e30


def shifted(value, axis, by):
    peers = lax.axis_size(axis)
    pairs = [(i, i + by) for i in range(peers) if 0 <= i + by < peers]
    return lax.ppermute(value, axis, pairs)


def head_norm(vec, gain):
    return vec * lax.rsqrt(jnp.mean(vec * vec, -1, keepdims=True) + norm_eps) * gain


def rotate(vec, positions):
    half = vec.shape[-1] // 2
    freq = jnp.exp(
        jnp.arange(half, dtype=jnp.float32) * (-2.0 * math.log(rope_base) / vec.shape[-1])
    )
    angle = positions.astype(jnp.float32)[:, None] * freq[None, :]
    shape_out = (vec.shape[0],) + (1,) * (vec.ndim - 2) + (half,)
    cosine = jnp.cos(angle).reshape(shape_out)
    sine = jnp.sin(angle).reshape(shape_out)
    first = vec[..., :half]
    second = vec[..., half:]
    return jnp.concatenate([first * cosine - second * sine, second * cosine + first * sine], -1)


def attend(state_now, queries, keys_block, values_block, visible):
    running_max, running_sum, running_acc = state_now
    scores = jnp.einsum(
        "tcgd,kcd->tcgk", queries, keys_block, preferred_element_type=jnp.float32
    ) * queries.shape[-1] ** (-0.5)
    scores = jnp.where(visible[:, None, None, :], scores, masked_score)
    new_max = jnp.maximum(running_max, jnp.max(scores, -1))
    rescale = jnp.exp(running_max - new_max)
    expo = jnp.exp(scores - new_max[..., None])
    new_sum = running_sum * rescale + jnp.sum(expo, -1)
    update = jnp.einsum(
        "tcgk,kcd->tcgd",
        expo.astype(jnp.bfloat16),
        values_block,
        preferred_element_type=jnp.float32,
    )
    return (new_max, new_sum, running_acc * rescale[..., None] + update)


def split_three(value):
    high = lax.reduce_precision(value, exponent_bits=8, mantissa_bits=7)
    rest = value - high
    middle = lax.reduce_precision(rest, exponent_bits=8, mantissa_bits=7)
    low = rest - middle
    return [part.astype(jnp.bfloat16) for part in (high, middle, low)]

def attention_kernel(
    scalars, q_ref, qtok_ref, kc_ref, vc_ref, kn_ref, vn_ref, ktok_ref, acc_ref, top_ref, total_ref
):
    scale = q_ref.shape[-1] ** (-0.5)
    dims = (((1,), (1,)), ((), ()))
    q = q_ref[...]
    new_scores = lax.dot_general(q, kn_ref[...], dims, preferred_element_type=jnp.float32) * scale
    new_seen = ktok_ref[...] <= qtok_ref[...]
    new_scores = jnp.where(new_seen, new_scores, masked_score)
    new_top = jnp.max(new_scores, 1, keepdims=True)
    cache_rows = kc_ref.shape[0]
    length, start = scalars[0], scalars[1]

    def finish(top, cache_total, cache_acc):
        new_expo = jnp.where(new_seen, jnp.exp(new_scores - top), 0.0)
        total_ref[...] = cache_total + jnp.sum(new_expo, 1, keepdims=True)
        top_ref[...] = top
        acc_ref[...] = cache_acc + jnp.dot(
            new_expo.astype(jnp.bfloat16), vn_ref[...], preferred_element_type=jnp.float32
        )

    def cache_part(masked):
        cache_scores = (
            lax.dot_general(q, kc_ref[...], dims, preferred_element_type=jnp.float32) * scale
        )
        if masked:
            cache_seen = start + lax.broadcasted_iota(jnp.int32, (1, cache_rows), 1) < length
            cache_scores = jnp.where(cache_seen, cache_scores, masked_score)
        top = jnp.maximum(jnp.max(cache_scores, 1, keepdims=True), new_top)
        cache_expo = jnp.exp(cache_scores - top)
        if masked:
            cache_expo = jnp.where(cache_seen, cache_expo, 0.0)
        cache_acc = jnp.dot(
            cache_expo.astype(jnp.bfloat16), vc_ref[...], preferred_element_type=jnp.float32
        )
        finish(top, jnp.sum(cache_expo, 1, keepdims=True), cache_acc)

    @pl.when(length >= start + cache_rows)
    def _():
        cache_part(False)

    @pl.when(jnp.logical_and(length > start, length < start + cache_rows))
    def _():
        cache_part(True)

    @pl.when(length <= start)
    def _():
        finish(new_top, jnp.zeros_like(new_top), jnp.zeros(acc_ref.shape, jnp.float32))


def attention(scalars, q_rows, q_tok, keys_cache, values_cache, keys_new, values_new, key_tok):
    rows, width = q_rows.shape
    cache_rows = keys_cache.shape[0]
    new_rows = keys_new.shape[0]
    block = 256
    full = lambda shape: pl.BlockSpec(shape, lambda i, s: (0, 0))
    row_block = lambda cols: pl.BlockSpec((block, cols), lambda i, s: (i, 0))
    flops = 4 * rows * (cache_rows + new_rows) * width
    return pl.pallas_call(
        attention_kernel,
        out_shape=(
            jax.ShapeDtypeStruct((rows, width), jnp.float32),
            jax.ShapeDtypeStruct((rows, 1), jnp.float32),
            jax.ShapeDtypeStruct((rows, 1), jnp.float32),
        ),
        grid_spec=pltpu.PrefetchScalarGridSpec(
            num_scalar_prefetch=1,
            grid=(rows // block,),
            in_specs=[
                row_block(width),
                row_block(1),
                full((cache_rows, width)),
                full((cache_rows, width)),
                full((new_rows, width)),
                full((new_rows, width)),
                full((1, new_rows)),
            ],
            out_specs=[row_block(width), row_block(1), row_block(1)],
        ),
        cost_estimate=pl.CostEstimate(
            flops=flops,
            transcendentals=rows * (cache_rows + new_rows),
            bytes_accessed=2 * (rows + 2 * cache_rows + 2 * new_rows) * width + 4 * rows * width,
        ),
    )(scalars, q_rows, q_tok, keys_cache, values_cache, keys_new, values_new, key_tok)


def per_device(
    hidden_in,
    norm_gain,
    w_query,
    w_key,
    w_value,
    w_headgate,
    w_out,
    q_gain,
    k_gain,
    cache_keys,
    cache_values,
    cached_len,
    group_of,
):
    tok_rows = hidden_in.shape[0]
    head_dim = q_gain.shape[0]
    kv_local = w_key.shape[1] // head_dim
    heads_local = w_query.shape[1] // head_dim
    group_size = heads_local // kv_local
    per_request = SPAN // tok_rows
    ring_x = lax.axis_size("sx")
    ring_z = lax.axis_size("sz")
    req_count = ring_x * ring_z // per_request
    pair = ring_z // req_count
    x_index = lax.axis_index("sx")
    z_index = lax.axis_index("sz")
    seq_index = x_index * ring_z + z_index
    request = seq_index % req_count
    local_part = seq_index // req_count
    parity = z_index // req_count
    length = cached_len[request]

    peer_groups = group_of[jnp.arange(ring_z, dtype=jnp.int32) % req_count]
    cache_both = jnp.stack([cache_keys, cache_values], 1)
    incoming = lax.all_to_all(cache_both[peer_groups], "sz", 0, 0, tiled=True)
    cache_rows = ring_z * cache_keys.shape[1]
    keys_cache = incoming[:, 0].reshape(cache_rows, kv_local, head_dim)
    values_cache = incoming[:, 1].reshape(cache_rows, kv_local, head_dim)
    cache_pos = x_index * cache_rows + jnp.arange(cache_rows, dtype=jnp.int32)

    gathered = lax.all_gather(hidden_in, "tp", axis=1, tiled=True)
    widened = gathered.astype(jnp.float32)
    normed = (
        widened * lax.rsqrt(jnp.mean(widened * widened, -1, keepdims=True) + norm_eps) * norm_gain
    ).astype(jnp.bfloat16)
    positions = length + local_part * tok_rows + jnp.arange(tok_rows, dtype=jnp.int32)
    query_raw = jnp.dot(normed, w_query, preferred_element_type=jnp.float32).reshape(
        tok_rows, kv_local, group_size, head_dim
    )
    queries = rotate(head_norm(query_raw, q_gain), positions).astype(jnp.bfloat16)
    key_raw = jnp.dot(normed, w_key, preferred_element_type=jnp.float32).reshape(
        tok_rows, kv_local, head_dim
    )
    keys_new = rotate(head_norm(key_raw, k_gain), positions).astype(jnp.bfloat16)
    values_new = (
        jnp.dot(normed, w_value, preferred_element_type=jnp.float32)
        .astype(jnp.bfloat16)
        .reshape(tok_rows, kv_local, head_dim)
    )
    gates = jax.nn.sigmoid(jnp.dot(normed, w_headgate, preferred_element_type=jnp.float32)).reshape(
        tok_rows, kv_local, group_size
    )

    partner_pairs = [(z, (z + req_count) % ring_z) for z in range(ring_z)]
    partner_kv = lax.ppermute(jnp.stack([keys_new, values_new]), "sz", partner_pairs)
    partner_part = x_index * pair + (pair - 1 - parity)
    all_queries = lax.all_gather(queries, "sx", axis=0, tiled=True)
    query_tok = (
        (jnp.arange(ring_x, dtype=jnp.int32) * pair + parity)[:, None] * tok_rows
        + jnp.arange(tok_rows, dtype=jnp.int32)[None, :]
    ).reshape(-1)
    row_ids = jnp.arange(tok_rows, dtype=jnp.int32)
    key_tok = jnp.concatenate([local_part * tok_rows + row_ids, partner_part * tok_rows + row_ids])
    keys_two = jnp.concatenate([keys_new, partner_kv[0]], 0).reshape(-1, head_dim)
    values_two = jnp.concatenate([values_new, partner_kv[1]], 0).reshape(-1, head_dim)
    query_count = query_tok.shape[0]
    scalars = jnp.stack([length, x_index * cache_rows]).astype(jnp.int32)
    acc, top, total = attention(
        scalars,
        all_queries.reshape(-1, head_dim),
        jnp.repeat(query_tok, heads_local)[:, None],
        keys_cache.reshape(cache_rows, head_dim),
        values_cache.reshape(cache_rows, head_dim),
        keys_two,
        values_two,
        key_tok[None, :],
    )
    slot_rows = tok_rows * heads_local
    pieces = [split_three(top), split_three(total)]
    stats = jnp.concatenate(pieces[0] + pieces[1], -1).reshape(ring_x, -1, head_dim)
    acc_half = acc.astype(jnp.bfloat16).reshape(ring_x, slot_rows, head_dim)
    packed_in = lax.all_to_all(jnp.concatenate([acc_half, stats], 1), "sx", 0, 0, tiled=True)
    packed_in = packed_in.astype(jnp.float32)
    acc_in = packed_in[:, :slot_rows].reshape(ring_x, tok_rows, kv_local, group_size, head_dim)
    stats_in = packed_in[:, slot_rows:].reshape(ring_x, tok_rows, kv_local, group_size, 6)
    stats_in = jnp.stack(
        [
            stats_in[..., 0] + stats_in[..., 1] + stats_in[..., 2],
            stats_in[..., 3] + stats_in[..., 4] + stats_in[..., 5],
        ],
        -1,
    )
    best = jnp.max(stats_in[..., 0], 0)
    factor = jnp.exp(stats_in[..., 0] - best[None])
    total = jnp.sum(stats_in[..., 1] * factor, 0)
    summed_acc = jnp.sum(acc_in * factor[..., None], 0)
    mixed = (
        (summed_acc / total[..., None] * gates[..., None])
        .astype(jnp.bfloat16)
        .reshape(tok_rows, heads_local * head_dim)
    )
    partial_out = jnp.dot(mixed, w_out, preferred_element_type=jnp.float32)
    tp_size = lax.axis_size("tp")
    pieces = partial_out.astype(jnp.bfloat16).reshape(tok_rows, tp_size, -1)
    arrived = lax.all_to_all(pieces, "tp", 1, 1, tiled=True)
    summed = jnp.sum(arrived.astype(jnp.float32), 1)
    return (hidden_in.astype(jnp.float32) + summed).astype(jnp.bfloat16)


def solution(mesh):
    seq_size = mesh.shape["seq"]
    tp_size = mesh.shape["tp"]
    req_count = seq_size // (SPAN // 128)
    ring_z = 2 * req_count
    ring_x = seq_size // ring_z
    split_mesh = Mesh(mesh.devices.reshape(ring_x, ring_z, tp_size), ("sx", "sz", "tp"))
    seq = ("sx", "sz")
    in_specs = (
        P(seq, "tp"),
        P(),
        P(None, "tp"),
        P(None, "tp"),
        P(None, "tp"),
        P(None, "tp"),
        P("tp", None),
        P(),
        P(),
        P(None, seq, "tp"),
        P(None, seq, "tp"),
        P(),
        P(),
    )
    out_specs = P(seq, "tp")
    return jax.shard_map(
        per_device, mesh=split_mesh, in_specs=in_specs, out_specs=out_specs, check_vma=False
    )
```

```python
import math

import jax
import jax.numpy as jnp
from jax import lax
from jax.experimental import pallas as pl
from jax.experimental.pallas import tpu as pltpu
from jax.sharding import Mesh, PartitionSpec as P

SPAN = 1024


norm_eps = 1e-06
rope_base = 1000000.0
masked_score = -1e30


def shifted(value, axis, by):
    peers = lax.axis_size(axis)
    pairs = [(i, i + by) for i in range(peers) if 0 <= i + by < peers]
    return lax.ppermute(value, axis, pairs)


def head_norm(vec, gain):
    return vec * lax.rsqrt(jnp.mean(vec * vec, -1, keepdims=True) + norm_eps) * gain


def rotate(vec, positions):
    half = vec.shape[-1] // 2
    freq = jnp.exp(
        jnp.arange(half, dtype=jnp.float32) * (-2.0 * math.log(rope_base) / vec.shape[-1])
    )
    angle = positions.astype(jnp.float32)[:, None] * freq[None, :]
    shape_out = (vec.shape[0],) + (1,) * (vec.ndim - 2) + (half,)
    cosine = jnp.cos(angle).reshape(shape_out)
    sine = jnp.sin(angle).reshape(shape_out)
    first = vec[..., :half]
    second = vec[..., half:]
    return jnp.concatenate([first * cosine - second * sine, second * cosine + first * sine], -1)


def attend(state_now, queries, keys_block, values_block, visible):
    running_max, running_sum, running_acc = state_now
    scores = jnp.einsum(
        "tcgd,kcd->tcgk", queries, keys_block, preferred_element_type=jnp.float32
    ) * queries.shape[-1] ** (-0.5)
    scores = jnp.where(visible[:, None, None, :], scores, masked_score)
    new_max = jnp.maximum(running_max, jnp.max(scores, -1))
    rescale = jnp.exp(running_max - new_max)
    expo = jnp.exp(scores - new_max[..., None])
    new_sum = running_sum * rescale + jnp.sum(expo, -1)
    update = jnp.einsum(
        "tcgk,kcd->tcgd",
        expo.astype(jnp.bfloat16),
        values_block,
        preferred_element_type=jnp.float32,
    )
    return (new_max, new_sum, running_acc * rescale[..., None] + update)


def attention_kernel(
    scalars, q_ref, qtok_ref, kc_ref, vc_ref, kn_ref, vn_ref, ktok_ref, acc_ref, top_ref, total_ref
):
    scale = q_ref.shape[-1] ** (-0.5)
    dims = (((1,), (1,)), ((), ()))
    q = q_ref[...]
    cache_scores = lax.dot_general(q, kc_ref[...], dims, preferred_element_type=jnp.float32) * scale
    cache_pos = scalars[1] + lax.broadcasted_iota(jnp.int32, (1, kc_ref.shape[0]), 1)
    cache_seen = cache_pos < scalars[0]
    cache_scores = jnp.where(cache_seen, cache_scores, masked_score)
    new_scores = lax.dot_general(q, kn_ref[...], dims, preferred_element_type=jnp.float32) * scale
    new_seen = ktok_ref[...] <= qtok_ref[...]
    new_scores = jnp.where(new_seen, new_scores, masked_score)
    top = jnp.maximum(
        jnp.max(cache_scores, 1, keepdims=True), jnp.max(new_scores, 1, keepdims=True)
    )
    cache_expo = jnp.where(cache_seen, jnp.exp(cache_scores - top), 0.0)
    new_expo = jnp.where(new_seen, jnp.exp(new_scores - top), 0.0)
    total_ref[...] = jnp.sum(cache_expo, 1, keepdims=True) + jnp.sum(new_expo, 1, keepdims=True)
    top_ref[...] = top
    acc_ref[...] = jnp.dot(
        cache_expo.astype(jnp.bfloat16), vc_ref[...], preferred_element_type=jnp.float32
    ) + jnp.dot(new_expo.astype(jnp.bfloat16), vn_ref[...], preferred_element_type=jnp.float32)


def attention(scalars, q_rows, q_tok, keys_cache, values_cache, keys_new, values_new, key_tok):
    rows, width = q_rows.shape
    cache_rows = keys_cache.shape[0]
    new_rows = keys_new.shape[0]
    block = 256
    full = lambda shape: pl.BlockSpec(shape, lambda i, s: (0, 0))
    row_block = lambda cols: pl.BlockSpec((block, cols), lambda i, s: (i, 0))
    flops = 4 * rows * (cache_rows + new_rows) * width
    return pl.pallas_call(
        attention_kernel,
        out_shape=(
            jax.ShapeDtypeStruct((rows, width), jnp.float32),
            jax.ShapeDtypeStruct((rows, 1), jnp.float32),
            jax.ShapeDtypeStruct((rows, 1), jnp.float32),
        ),
        grid_spec=pltpu.PrefetchScalarGridSpec(
            num_scalar_prefetch=1,
            grid=(rows // block,),
            in_specs=[
                row_block(width),
                row_block(1),
                full((cache_rows, width)),
                full((cache_rows, width)),
                full((new_rows, width)),
                full((new_rows, width)),
                full((1, new_rows)),
            ],
            out_specs=[row_block(width), row_block(1), row_block(1)],
        ),
        cost_estimate=pl.CostEstimate(
            flops=flops,
            transcendentals=rows * (cache_rows + new_rows),
            bytes_accessed=2 * (rows + 2 * cache_rows + 2 * new_rows) * width + 4 * rows * width,
        ),
    )(scalars, q_rows, q_tok, keys_cache, values_cache, keys_new, values_new, key_tok)


def per_device(
    hidden_in,
    norm_gain,
    w_query,
    w_key,
    w_value,
    w_headgate,
    w_out,
    q_gain,
    k_gain,
    cache_keys,
    cache_values,
    cached_len,
    group_of,
):
    tok_rows = hidden_in.shape[0]
    head_dim = q_gain.shape[0]
    kv_local = w_key.shape[1] // head_dim
    heads_local = w_query.shape[1] // head_dim
    group_size = heads_local // kv_local
    per_request = SPAN // tok_rows
    ring_x = lax.axis_size("sx")
    ring_z = lax.axis_size("sz")
    req_count = ring_x * ring_z // per_request
    pair = ring_z // req_count
    x_index = lax.axis_index("sx")
    z_index = lax.axis_index("sz")
    seq_index = x_index * ring_z + z_index
    request = seq_index % req_count
    local_part = seq_index // req_count
    parity = z_index // req_count
    length = cached_len[request]

    peer_groups = group_of[jnp.arange(ring_z, dtype=jnp.int32) % req_count]
    cache_both = jnp.stack([cache_keys, cache_values], 1)
    incoming = lax.all_to_all(cache_both[peer_groups], "sz", 0, 0, tiled=True)
    cache_rows = ring_z * cache_keys.shape[1]
    keys_cache = incoming[:, 0].reshape(cache_rows, kv_local, head_dim)
    values_cache = incoming[:, 1].reshape(cache_rows, kv_local, head_dim)
    cache_pos = x_index * cache_rows + jnp.arange(cache_rows, dtype=jnp.int32)

    gathered = lax.all_gather(hidden_in, "tp", axis=1, tiled=True)
    widened = gathered.astype(jnp.float32)
    normed = (
        widened * lax.rsqrt(jnp.mean(widened * widened, -1, keepdims=True) + norm_eps) * norm_gain
    ).astype(jnp.bfloat16)
    positions = length + local_part * tok_rows + jnp.arange(tok_rows, dtype=jnp.int32)
    query_raw = jnp.dot(normed, w_query, preferred_element_type=jnp.float32).reshape(
        tok_rows, kv_local, group_size, head_dim
    )
    queries = rotate(head_norm(query_raw, q_gain), positions).astype(jnp.bfloat16)
    key_raw = jnp.dot(normed, w_key, preferred_element_type=jnp.float32).reshape(
        tok_rows, kv_local, head_dim
    )
    keys_new = rotate(head_norm(key_raw, k_gain), positions).astype(jnp.bfloat16)
    values_new = (
        jnp.dot(normed, w_value, preferred_element_type=jnp.float32)
        .astype(jnp.bfloat16)
        .reshape(tok_rows, kv_local, head_dim)
    )
    gates = jax.nn.sigmoid(jnp.dot(normed, w_headgate, preferred_element_type=jnp.float32)).reshape(
        tok_rows, kv_local, group_size
    )

    hop = req_count // 2
    ahead = [(z, (z + hop) % ring_z) for z in range(ring_z)]
    behind = [(z, (z - hop) % ring_z) for z in range(ring_z)]
    partner_keys = lax.ppermute(lax.ppermute(keys_new, "sz", ahead), "sz", ahead)
    partner_values = lax.ppermute(lax.ppermute(values_new, "sz", behind), "sz", behind)
    partner_kv = (partner_keys, partner_values)
    partner_part = x_index * pair + (pair - 1 - parity)
    all_queries = lax.all_gather(queries, "sx", axis=0, tiled=True)
    query_tok = (
        (jnp.arange(ring_x, dtype=jnp.int32) * pair + parity)[:, None] * tok_rows
        + jnp.arange(tok_rows, dtype=jnp.int32)[None, :]
    ).reshape(-1)
    row_ids = jnp.arange(tok_rows, dtype=jnp.int32)
    key_tok = jnp.concatenate([local_part * tok_rows + row_ids, partner_part * tok_rows + row_ids])
    keys_two = jnp.concatenate([keys_new, partner_kv[0]], 0).reshape(-1, head_dim)
    values_two = jnp.concatenate([values_new, partner_kv[1]], 0).reshape(-1, head_dim)
    query_count = query_tok.shape[0]
    scalars = jnp.stack([length, x_index * cache_rows]).astype(jnp.int32)
    acc, top, total = attention(
        scalars,
        all_queries.reshape(-1, head_dim),
        jnp.repeat(query_tok, heads_local)[:, None],
        keys_cache.reshape(cache_rows, head_dim),
        values_cache.reshape(cache_rows, head_dim),
        keys_two,
        values_two,
        key_tok[None, :],
    )
    slot_rows = tok_rows * heads_local
    stats = jnp.concatenate([top, total], -1).reshape(ring_x, -1, head_dim)
    packed = jnp.concatenate([acc.reshape(ring_x, slot_rows, head_dim), stats], 1)
    packed_in = lax.all_to_all(packed, "sx", 0, 0, tiled=True)
    acc_in = packed_in[:, :slot_rows].reshape(ring_x, tok_rows, kv_local, group_size, head_dim)
    stats_in = packed_in[:, slot_rows:].reshape(ring_x, tok_rows, kv_local, group_size, 2)
    best = jnp.max(stats_in[..., 0], 0)
    factor = jnp.exp(stats_in[..., 0] - best[None])
    total = jnp.sum(stats_in[..., 1] * factor, 0)
    summed_acc = jnp.sum(acc_in * factor[..., None], 0)
    mixed = (
        (summed_acc / total[..., None] * gates[..., None])
        .astype(jnp.bfloat16)
        .reshape(tok_rows, heads_local * head_dim)
    )
    partial_out = jnp.dot(mixed, w_out, preferred_element_type=jnp.float32)
    tp_size = lax.axis_size("tp")
    pieces = partial_out.astype(jnp.bfloat16).reshape(tok_rows, tp_size, -1)
    arrived = lax.all_to_all(pieces, "tp", 1, 1, tiled=True)
    summed = jnp.sum(arrived.astype(jnp.float32), 1)
    return (hidden_in.astype(jnp.float32) + summed).astype(jnp.bfloat16)


def solution(mesh):
    seq_size = mesh.shape["seq"]
    tp_size = mesh.shape["tp"]
    req_count = seq_size // (SPAN // 128)
    ring_z = 2 * req_count
    ring_x = seq_size // ring_z
    split_mesh = Mesh(mesh.devices.reshape(ring_x, ring_z, tp_size), ("sx", "sz", "tp"))
    seq = ("sx", "sz")
    in_specs = (
        P(seq, "tp"),
        P(),
        P(None, "tp"),
        P(None, "tp"),
        P(None, "tp"),
        P(None, "tp"),
        P("tp", None),
        P(),
        P(),
        P(None, seq, "tp"),
        P(None, seq, "tp"),
        P(),
        P(),
    )
    out_specs = P(seq, "tp")
    return jax.shard_map(
        per_device, mesh=split_mesh, in_specs=in_specs, out_specs=out_specs, check_vma=False
    )
```

```python
import math

import jax
import jax.numpy as jnp
from jax import lax
from jax.experimental import pallas as pl
from jax.experimental.pallas import tpu as pltpu
from jax.sharding import Mesh, PartitionSpec as P

SPAN = 1024


norm_eps = 1e-06
rope_base = 1000000.0
masked_score = -1e30


def shifted(value, axis, by):
    peers = lax.axis_size(axis)
    pairs = [(i, i + by) for i in range(peers) if 0 <= i + by < peers]
    return lax.ppermute(value, axis, pairs)


def head_norm(vec, gain):
    return vec * lax.rsqrt(jnp.mean(vec * vec, -1, keepdims=True) + norm_eps) * gain


def rotate(vec, positions):
    half = vec.shape[-1] // 2
    freq = jnp.exp(
        jnp.arange(half, dtype=jnp.float32) * (-2.0 * math.log(rope_base) / vec.shape[-1])
    )
    angle = positions.astype(jnp.float32)[:, None] * freq[None, :]
    shape_out = (vec.shape[0],) + (1,) * (vec.ndim - 2) + (half,)
    cosine = jnp.cos(angle).reshape(shape_out)
    sine = jnp.sin(angle).reshape(shape_out)
    first = vec[..., :half]
    second = vec[..., half:]
    return jnp.concatenate([first * cosine - second * sine, second * cosine + first * sine], -1)


def attend(state_now, queries, keys_block, values_block, visible):
    running_max, running_sum, running_acc = state_now
    scores = jnp.einsum(
        "tcgd,kcd->tcgk", queries, keys_block, preferred_element_type=jnp.float32
    ) * queries.shape[-1] ** (-0.5)
    scores = jnp.where(visible[:, None, None, :], scores, masked_score)
    new_max = jnp.maximum(running_max, jnp.max(scores, -1))
    rescale = jnp.exp(running_max - new_max)
    expo = jnp.exp(scores - new_max[..., None])
    new_sum = running_sum * rescale + jnp.sum(expo, -1)
    update = jnp.einsum(
        "tcgk,kcd->tcgd",
        expo.astype(jnp.bfloat16),
        values_block,
        preferred_element_type=jnp.float32,
    )
    return (new_max, new_sum, running_acc * rescale[..., None] + update)


def attention_kernel(
    scalars, q_ref, qtok_ref, kc_ref, vc_ref, kn_ref, vn_ref, ktok_ref, acc_ref, top_ref, total_ref
):
    scale = q_ref.shape[-1] ** (-0.5)
    dims = (((1,), (1,)), ((), ()))
    q = q_ref[...]
    cache_scores = lax.dot_general(q, kc_ref[...], dims, preferred_element_type=jnp.float32) * scale
    cache_pos = scalars[1] + lax.broadcasted_iota(jnp.int32, (1, kc_ref.shape[0]), 1)
    cache_seen = cache_pos < scalars[0]
    cache_scores = jnp.where(cache_seen, cache_scores, masked_score)
    new_scores = lax.dot_general(q, kn_ref[...], dims, preferred_element_type=jnp.float32) * scale
    new_seen = ktok_ref[...] <= qtok_ref[...]
    new_scores = jnp.where(new_seen, new_scores, masked_score)
    top = jnp.maximum(
        jnp.max(cache_scores, 1, keepdims=True), jnp.max(new_scores, 1, keepdims=True)
    )
    zero = jnp.zeros((), jnp.bfloat16)
    cache_expo = jnp.where(cache_seen, jnp.exp((cache_scores - top).astype(jnp.bfloat16)), zero)
    new_expo = jnp.where(new_seen, jnp.exp((new_scores - top).astype(jnp.bfloat16)), zero)
    total_ref[...] = jnp.sum(cache_expo.astype(jnp.float32), 1, keepdims=True) + jnp.sum(
        new_expo.astype(jnp.float32), 1, keepdims=True
    )
    top_ref[...] = top
    acc_ref[...] = jnp.dot(cache_expo, vc_ref[...], preferred_element_type=jnp.float32) + jnp.dot(
        new_expo, vn_ref[...], preferred_element_type=jnp.float32
    )


def attention(scalars, q_rows, q_tok, keys_cache, values_cache, keys_new, values_new, key_tok):
    rows, width = q_rows.shape
    cache_rows = keys_cache.shape[0]
    new_rows = keys_new.shape[0]
    block = 256
    full = lambda shape: pl.BlockSpec(shape, lambda i, s: (0, 0))
    row_block = lambda cols: pl.BlockSpec((block, cols), lambda i, s: (i, 0))
    flops = 4 * rows * (cache_rows + new_rows) * width
    return pl.pallas_call(
        attention_kernel,
        out_shape=(
            jax.ShapeDtypeStruct((rows, width), jnp.float32),
            jax.ShapeDtypeStruct((rows, 1), jnp.float32),
            jax.ShapeDtypeStruct((rows, 1), jnp.float32),
        ),
        grid_spec=pltpu.PrefetchScalarGridSpec(
            num_scalar_prefetch=1,
            grid=(rows // block,),
            in_specs=[
                row_block(width),
                row_block(1),
                full((cache_rows, width)),
                full((cache_rows, width)),
                full((new_rows, width)),
                full((new_rows, width)),
                full((1, new_rows)),
            ],
            out_specs=[row_block(width), row_block(1), row_block(1)],
        ),
        cost_estimate=pl.CostEstimate(
            flops=flops,
            transcendentals=rows * (cache_rows + new_rows),
            bytes_accessed=2 * (rows + 2 * cache_rows + 2 * new_rows) * width + 4 * rows * width,
        ),
    )(scalars, q_rows, q_tok, keys_cache, values_cache, keys_new, values_new, key_tok)


def per_device(
    hidden_in,
    norm_gain,
    w_query,
    w_key,
    w_value,
    w_headgate,
    w_out,
    q_gain,
    k_gain,
    cache_keys,
    cache_values,
    cached_len,
    group_of,
):
    tok_rows = hidden_in.shape[0]
    head_dim = q_gain.shape[0]
    kv_local = w_key.shape[1] // head_dim
    heads_local = w_query.shape[1] // head_dim
    group_size = heads_local // kv_local
    per_request = SPAN // tok_rows
    ring_x = lax.axis_size("sx")
    ring_z = lax.axis_size("sz")
    req_count = ring_x * ring_z // per_request
    pair = ring_z // req_count
    x_index = lax.axis_index("sx")
    z_index = lax.axis_index("sz")
    seq_index = x_index * ring_z + z_index
    request = seq_index % req_count
    local_part = seq_index // req_count
    parity = z_index // req_count
    length = cached_len[request]

    peer_groups = group_of[jnp.arange(ring_z, dtype=jnp.int32) % req_count]
    cache_both = jnp.stack([cache_keys, cache_values], 1)
    incoming = lax.all_to_all(cache_both[peer_groups], "sz", 0, 0, tiled=True)
    cache_rows = ring_z * cache_keys.shape[1]
    keys_cache = incoming[:, 0].reshape(cache_rows, kv_local, head_dim)
    values_cache = incoming[:, 1].reshape(cache_rows, kv_local, head_dim)
    cache_pos = x_index * cache_rows + jnp.arange(cache_rows, dtype=jnp.int32)

    gathered = lax.all_gather(hidden_in, "tp", axis=1, tiled=True)
    widened = gathered.astype(jnp.float32)
    normed = (
        widened * lax.rsqrt(jnp.mean(widened * widened, -1, keepdims=True) + norm_eps) * norm_gain
    ).astype(jnp.bfloat16)
    positions = length + local_part * tok_rows + jnp.arange(tok_rows, dtype=jnp.int32)
    query_raw = jnp.dot(normed, w_query, preferred_element_type=jnp.float32).reshape(
        tok_rows, kv_local, group_size, head_dim
    )
    queries = rotate(head_norm(query_raw, q_gain), positions).astype(jnp.bfloat16)
    key_raw = jnp.dot(normed, w_key, preferred_element_type=jnp.float32).reshape(
        tok_rows, kv_local, head_dim
    )
    keys_new = rotate(head_norm(key_raw, k_gain), positions).astype(jnp.bfloat16)
    values_new = (
        jnp.dot(normed, w_value, preferred_element_type=jnp.float32)
        .astype(jnp.bfloat16)
        .reshape(tok_rows, kv_local, head_dim)
    )
    gates = jax.nn.sigmoid(jnp.dot(normed, w_headgate, preferred_element_type=jnp.float32)).reshape(
        tok_rows, kv_local, group_size
    )

    partner_pairs = [(z, (z + req_count) % ring_z) for z in range(ring_z)]
    partner_kv = lax.ppermute(jnp.stack([keys_new, values_new]), "sz", partner_pairs)
    partner_part = x_index * pair + (pair - 1 - parity)
    all_queries = lax.all_gather(queries, "sx", axis=0, tiled=True)
    query_tok = (
        (jnp.arange(ring_x, dtype=jnp.int32) * pair + parity)[:, None] * tok_rows
        + jnp.arange(tok_rows, dtype=jnp.int32)[None, :]
    ).reshape(-1)
    row_ids = jnp.arange(tok_rows, dtype=jnp.int32)
    key_tok = jnp.concatenate([local_part * tok_rows + row_ids, partner_part * tok_rows + row_ids])
    keys_two = jnp.concatenate([keys_new, partner_kv[0]], 0).reshape(-1, head_dim)
    values_two = jnp.concatenate([values_new, partner_kv[1]], 0).reshape(-1, head_dim)
    query_count = query_tok.shape[0]
    scalars = jnp.stack([length, x_index * cache_rows]).astype(jnp.int32)
    acc, top, total = attention(
        scalars,
        all_queries.reshape(-1, head_dim),
        jnp.repeat(query_tok, heads_local)[:, None],
        keys_cache.reshape(cache_rows, head_dim),
        values_cache.reshape(cache_rows, head_dim),
        keys_two,
        values_two,
        key_tok[None, :],
    )
    slot_rows = tok_rows * heads_local
    stats = jnp.concatenate([top, total], -1).reshape(ring_x, -1, head_dim)
    packed = jnp.concatenate([acc.reshape(ring_x, slot_rows, head_dim), stats], 1)
    packed_in = lax.all_to_all(packed, "sx", 0, 0, tiled=True)
    acc_in = packed_in[:, :slot_rows].reshape(ring_x, tok_rows, kv_local, group_size, head_dim)
    stats_in = packed_in[:, slot_rows:].reshape(ring_x, tok_rows, kv_local, group_size, 2)
    best = jnp.max(stats_in[..., 0], 0)
    factor = jnp.exp(stats_in[..., 0] - best[None])
    total = jnp.sum(stats_in[..., 1] * factor, 0)
    summed_acc = jnp.sum(acc_in * factor[..., None], 0)
    mixed = (
        (summed_acc / total[..., None] * gates[..., None])
        .astype(jnp.bfloat16)
        .reshape(tok_rows, heads_local * head_dim)
    )
    partial_out = jnp.dot(mixed, w_out, preferred_element_type=jnp.float32)
    tp_size = lax.axis_size("tp")
    pieces = partial_out.astype(jnp.bfloat16).reshape(tok_rows, tp_size, -1)
    arrived = lax.all_to_all(pieces, "tp", 1, 1, tiled=True)
    summed = jnp.sum(arrived.astype(jnp.float32), 1)
    return (hidden_in.astype(jnp.float32) + summed).astype(jnp.bfloat16)


def solution(mesh):
    seq_size = mesh.shape["seq"]
    tp_size = mesh.shape["tp"]
    req_count = seq_size // (SPAN // 128)
    ring_z = 2 * req_count
    ring_x = seq_size // ring_z
    split_mesh = Mesh(mesh.devices.reshape(ring_x, ring_z, tp_size), ("sx", "sz", "tp"))
    seq = ("sx", "sz")
    in_specs = (
        P(seq, "tp"),
        P(),
        P(None, "tp"),
        P(None, "tp"),
        P(None, "tp"),
        P(None, "tp"),
        P("tp", None),
        P(),
        P(),
        P(None, seq, "tp"),
        P(None, seq, "tp"),
        P(),
        P(),
    )
    out_specs = P(seq, "tp")
    return jax.shard_map(
        per_device, mesh=split_mesh, in_specs=in_specs, out_specs=out_specs, check_vma=False
    )
```

```python
import math

import jax
import jax.numpy as jnp
from jax import lax
from jax.experimental import pallas as pl
from jax.experimental.pallas import tpu as pltpu
from jax.sharding import Mesh, PartitionSpec as P

SPAN = 1024


norm_eps = 1e-06
rope_base = 1000000.0
masked_score = -1e30


def shifted(value, axis, by):
    peers = lax.axis_size(axis)
    pairs = [(i, i + by) for i in range(peers) if 0 <= i + by < peers]
    return lax.ppermute(value, axis, pairs)


def head_norm(vec, gain):
    return vec * lax.rsqrt(jnp.mean(vec * vec, -1, keepdims=True) + norm_eps) * gain


def rotate(vec, positions):
    half = vec.shape[-1] // 2
    freq = jnp.exp(
        jnp.arange(half, dtype=jnp.float32) * (-2.0 * math.log(rope_base) / vec.shape[-1])
    )
    angle = positions.astype(jnp.float32)[:, None] * freq[None, :]
    shape_out = (vec.shape[0],) + (1,) * (vec.ndim - 2) + (half,)
    cosine = jnp.cos(angle).reshape(shape_out)
    sine = jnp.sin(angle).reshape(shape_out)
    first = vec[..., :half]
    second = vec[..., half:]
    return jnp.concatenate([first * cosine - second * sine, second * cosine + first * sine], -1)


def attend(state_now, queries, keys_block, values_block, visible):
    running_max, running_sum, running_acc = state_now
    scores = jnp.einsum(
        "tcgd,kcd->tcgk", queries, keys_block, preferred_element_type=jnp.float32
    ) * queries.shape[-1] ** (-0.5)
    scores = jnp.where(visible[:, None, None, :], scores, masked_score)
    new_max = jnp.maximum(running_max, jnp.max(scores, -1))
    rescale = jnp.exp(running_max - new_max)
    expo = jnp.exp(scores - new_max[..., None])
    new_sum = running_sum * rescale + jnp.sum(expo, -1)
    update = jnp.einsum(
        "tcgk,kcd->tcgd",
        expo.astype(jnp.bfloat16),
        values_block,
        preferred_element_type=jnp.float32,
    )
    return (new_max, new_sum, running_acc * rescale[..., None] + update)


def attention_kernel(
    scalars, q_ref, qtok_ref, kc_ref, vc_ref, kn_ref, vn_ref, ktok_ref, acc_ref, top_ref, total_ref
):
    scale = q_ref.shape[-1] ** (-0.5)
    dims = (((1,), (1,)), ((), ()))
    q = q_ref[...]
    cache_scores = jnp.dot(q, kc_ref[...], preferred_element_type=jnp.float32) * scale
    cache_pos = scalars[1] + lax.broadcasted_iota(jnp.int32, (1, kc_ref.shape[1]), 1)
    cache_seen = cache_pos < scalars[0]
    cache_scores = jnp.where(cache_seen, cache_scores, masked_score)
    new_scores = jnp.dot(q, kn_ref[...], preferred_element_type=jnp.float32) * scale
    new_seen = ktok_ref[...] <= qtok_ref[...]
    new_scores = jnp.where(new_seen, new_scores, masked_score)
    top = jnp.maximum(
        jnp.max(cache_scores, 1, keepdims=True), jnp.max(new_scores, 1, keepdims=True)
    )
    cache_expo = jnp.where(cache_seen, jnp.exp(cache_scores - top), 0.0)
    new_expo = jnp.where(new_seen, jnp.exp(new_scores - top), 0.0)
    total_ref[...] = jnp.sum(cache_expo, 1, keepdims=True) + jnp.sum(new_expo, 1, keepdims=True)
    top_ref[...] = top
    acc_ref[...] = jnp.dot(
        cache_expo.astype(jnp.bfloat16), vc_ref[...], preferred_element_type=jnp.float32
    ) + jnp.dot(new_expo.astype(jnp.bfloat16), vn_ref[...], preferred_element_type=jnp.float32)


def attention(scalars, q_rows, q_tok, keys_cache, values_cache, keys_new, values_new, key_tok):
    rows, width = q_rows.shape
    cache_rows = keys_cache.shape[1]
    new_rows = keys_new.shape[1]
    block = 256
    full = lambda shape: pl.BlockSpec(shape, lambda i, s: (0, 0))
    row_block = lambda cols: pl.BlockSpec((block, cols), lambda i, s: (i, 0))
    flops = 4 * rows * (cache_rows + new_rows) * width
    return pl.pallas_call(
        attention_kernel,
        out_shape=(
            jax.ShapeDtypeStruct((rows, width), jnp.float32),
            jax.ShapeDtypeStruct((rows, 1), jnp.float32),
            jax.ShapeDtypeStruct((rows, 1), jnp.float32),
        ),
        grid_spec=pltpu.PrefetchScalarGridSpec(
            num_scalar_prefetch=1,
            grid=(rows // block,),
            in_specs=[
                row_block(width),
                row_block(1),
                full((width, cache_rows)),
                full((cache_rows, width)),
                full((width, new_rows)),
                full((new_rows, width)),
                full((1, new_rows)),
            ],
            out_specs=[row_block(width), row_block(1), row_block(1)],
        ),
        cost_estimate=pl.CostEstimate(
            flops=flops,
            transcendentals=rows * (cache_rows + new_rows),
            bytes_accessed=2 * (rows + 2 * cache_rows + 2 * new_rows) * width + 4 * rows * width,
        ),
    )(scalars, q_rows, q_tok, keys_cache, values_cache, keys_new, values_new, key_tok)


def per_device(
    hidden_in,
    norm_gain,
    w_query,
    w_key,
    w_value,
    w_headgate,
    w_out,
    q_gain,
    k_gain,
    cache_keys,
    cache_values,
    cached_len,
    group_of,
):
    tok_rows = hidden_in.shape[0]
    head_dim = q_gain.shape[0]
    kv_local = w_key.shape[1] // head_dim
    heads_local = w_query.shape[1] // head_dim
    group_size = heads_local // kv_local
    per_request = SPAN // tok_rows
    ring_x = lax.axis_size("sx")
    ring_z = lax.axis_size("sz")
    req_count = ring_x * ring_z // per_request
    pair = ring_z // req_count
    x_index = lax.axis_index("sx")
    z_index = lax.axis_index("sz")
    seq_index = x_index * ring_z + z_index
    request = seq_index % req_count
    local_part = seq_index // req_count
    parity = z_index // req_count
    length = cached_len[request]

    peer_groups = group_of[jnp.arange(ring_z, dtype=jnp.int32) % req_count]
    cache_both = jnp.stack([cache_keys, cache_values], 1)
    incoming = lax.all_to_all(cache_both[peer_groups], "sz", 0, 0, tiled=True)
    cache_rows = ring_z * cache_keys.shape[1]
    keys_cache = incoming[:, 0].reshape(cache_rows, kv_local, head_dim)
    values_cache = incoming[:, 1].reshape(cache_rows, kv_local, head_dim)
    cache_pos = x_index * cache_rows + jnp.arange(cache_rows, dtype=jnp.int32)

    gathered = lax.all_gather(hidden_in, "tp", axis=1, tiled=True)
    widened = gathered.astype(jnp.float32)
    normed = (
        widened * lax.rsqrt(jnp.mean(widened * widened, -1, keepdims=True) + norm_eps) * norm_gain
    ).astype(jnp.bfloat16)
    positions = length + local_part * tok_rows + jnp.arange(tok_rows, dtype=jnp.int32)
    query_raw = jnp.dot(normed, w_query, preferred_element_type=jnp.float32).reshape(
        tok_rows, kv_local, group_size, head_dim
    )
    queries = rotate(head_norm(query_raw, q_gain), positions).astype(jnp.bfloat16)
    key_raw = jnp.dot(normed, w_key, preferred_element_type=jnp.float32).reshape(
        tok_rows, kv_local, head_dim
    )
    keys_new = rotate(head_norm(key_raw, k_gain), positions).astype(jnp.bfloat16)
    values_new = (
        jnp.dot(normed, w_value, preferred_element_type=jnp.float32)
        .astype(jnp.bfloat16)
        .reshape(tok_rows, kv_local, head_dim)
    )
    gates = jax.nn.sigmoid(jnp.dot(normed, w_headgate, preferred_element_type=jnp.float32)).reshape(
        tok_rows, kv_local, group_size
    )

    partner_pairs = [(z, (z + req_count) % ring_z) for z in range(ring_z)]
    partner_kv = lax.ppermute(jnp.stack([keys_new, values_new]), "sz", partner_pairs)
    partner_part = x_index * pair + (pair - 1 - parity)
    all_queries = lax.all_gather(queries, "sx", axis=0, tiled=True)
    query_tok = (
        (jnp.arange(ring_x, dtype=jnp.int32) * pair + parity)[:, None] * tok_rows
        + jnp.arange(tok_rows, dtype=jnp.int32)[None, :]
    ).reshape(-1)
    row_ids = jnp.arange(tok_rows, dtype=jnp.int32)
    key_tok = jnp.concatenate([local_part * tok_rows + row_ids, partner_part * tok_rows + row_ids])
    keys_two = jnp.concatenate([keys_new, partner_kv[0]], 0).reshape(-1, head_dim)
    values_two = jnp.concatenate([values_new, partner_kv[1]], 0).reshape(-1, head_dim)
    query_count = query_tok.shape[0]
    scalars = jnp.stack([length, x_index * cache_rows]).astype(jnp.int32)
    acc, top, total = attention(
        scalars,
        all_queries.reshape(-1, head_dim),
        jnp.repeat(query_tok, heads_local)[:, None],
        keys_cache.reshape(cache_rows, head_dim).T,
        values_cache.reshape(cache_rows, head_dim),
        keys_two.T,
        values_two,
        key_tok[None, :],
    )
    slot_rows = tok_rows * heads_local
    stats = jnp.concatenate([top, total], -1).reshape(ring_x, -1, head_dim)
    packed = jnp.concatenate([acc.reshape(ring_x, slot_rows, head_dim), stats], 1)
    packed_in = lax.all_to_all(packed, "sx", 0, 0, tiled=True)
    acc_in = packed_in[:, :slot_rows].reshape(ring_x, tok_rows, kv_local, group_size, head_dim)
    stats_in = packed_in[:, slot_rows:].reshape(ring_x, tok_rows, kv_local, group_size, 2)
    best = jnp.max(stats_in[..., 0], 0)
    factor = jnp.exp(stats_in[..., 0] - best[None])
    total = jnp.sum(stats_in[..., 1] * factor, 0)
    summed_acc = jnp.sum(acc_in * factor[..., None], 0)
    mixed = (
        (summed_acc / total[..., None] * gates[..., None])
        .astype(jnp.bfloat16)
        .reshape(tok_rows, heads_local * head_dim)
    )
    partial_out = jnp.dot(mixed, w_out, preferred_element_type=jnp.float32)
    tp_size = lax.axis_size("tp")
    pieces = partial_out.astype(jnp.bfloat16).reshape(tok_rows, tp_size, -1)
    arrived = lax.all_to_all(pieces, "tp", 1, 1, tiled=True)
    summed = jnp.sum(arrived.astype(jnp.float32), 1)
    return (hidden_in.astype(jnp.float32) + summed).astype(jnp.bfloat16)


def solution(mesh):
    seq_size = mesh.shape["seq"]
    tp_size = mesh.shape["tp"]
    req_count = seq_size // (SPAN // 128)
    ring_z = 2 * req_count
    ring_x = seq_size // ring_z
    split_mesh = Mesh(mesh.devices.reshape(ring_x, ring_z, tp_size), ("sx", "sz", "tp"))
    seq = ("sx", "sz")
    in_specs = (
        P(seq, "tp"),
        P(),
        P(None, "tp"),
        P(None, "tp"),
        P(None, "tp"),
        P(None, "tp"),
        P("tp", None),
        P(),
        P(),
        P(None, seq, "tp"),
        P(None, seq, "tp"),
        P(),
        P(),
    )
    out_specs = P(seq, "tp")
    return jax.shard_map(
        per_device, mesh=split_mesh, in_specs=in_specs, out_specs=out_specs, check_vma=False
    )
```

```python
import math

import jax
import jax.numpy as jnp
from jax import lax
from jax.experimental import pallas as pl
from jax.experimental.pallas import tpu as pltpu
from jax.sharding import Mesh, PartitionSpec as P

SPAN = 1024


norm_eps = 1e-06
rope_base = 1000000.0
masked_score = -1e30


def shifted(value, axis, by):
    peers = lax.axis_size(axis)
    pairs = [(i, i + by) for i in range(peers) if 0 <= i + by < peers]
    return lax.ppermute(value, axis, pairs)


def head_norm(vec, gain):
    return vec * lax.rsqrt(jnp.mean(vec * vec, -1, keepdims=True) + norm_eps) * gain


def rotate(vec, positions):
    half = vec.shape[-1] // 2
    freq = jnp.exp(
        jnp.arange(half, dtype=jnp.float32) * (-2.0 * math.log(rope_base) / vec.shape[-1])
    )
    angle = positions.astype(jnp.float32)[:, None] * freq[None, :]
    shape_out = (vec.shape[0],) + (1,) * (vec.ndim - 2) + (half,)
    cosine = jnp.cos(angle).reshape(shape_out)
    sine = jnp.sin(angle).reshape(shape_out)
    first = vec[..., :half]
    second = vec[..., half:]
    return jnp.concatenate([first * cosine - second * sine, second * cosine + first * sine], -1)


def attend(state_now, queries, keys_block, values_block, visible):
    running_max, running_sum, running_acc = state_now
    scores = jnp.einsum(
        "tcgd,kcd->tcgk", queries, keys_block, preferred_element_type=jnp.float32
    ) * queries.shape[-1] ** (-0.5)
    scores = jnp.where(visible[:, None, None, :], scores, masked_score)
    new_max = jnp.maximum(running_max, jnp.max(scores, -1))
    rescale = jnp.exp(running_max - new_max)
    expo = jnp.exp(scores - new_max[..., None])
    new_sum = running_sum * rescale + jnp.sum(expo, -1)
    update = jnp.einsum(
        "tcgk,kcd->tcgd",
        expo.astype(jnp.bfloat16),
        values_block,
        preferred_element_type=jnp.float32,
    )
    return (new_max, new_sum, running_acc * rescale[..., None] + update)


def attention_kernel(
    scalars, q_ref, qtok_ref, kc_ref, vc_ref, kn_ref, vn_ref, ktok_ref, acc_ref, top_ref, total_ref
):
    scale = q_ref.shape[-1] ** (-0.5)
    dims = (((1,), (1,)), ((), ()))
    q = q_ref[...]
    cache_scores = lax.dot_general(q, kc_ref[...], dims, preferred_element_type=jnp.float32) * scale
    cache_pos = scalars[1] + lax.broadcasted_iota(jnp.int32, (1, kc_ref.shape[0]), 1)
    cache_seen = cache_pos < scalars[0]
    cache_scores = jnp.where(cache_seen, cache_scores, masked_score)
    new_scores = lax.dot_general(q, kn_ref[...], dims, preferred_element_type=jnp.float32) * scale
    new_seen = ktok_ref[...] <= qtok_ref[...]
    new_scores = jnp.where(new_seen, new_scores, masked_score)
    top = jnp.maximum(
        jnp.max(cache_scores, 1, keepdims=True), jnp.max(new_scores, 1, keepdims=True)
    )
    cache_expo = jnp.where(cache_seen, jnp.exp(cache_scores - top), 0.0)
    new_expo = jnp.where(new_seen, jnp.exp(new_scores - top), 0.0)
    total_ref[...] = jnp.sum(cache_expo, 1, keepdims=True) + jnp.sum(new_expo, 1, keepdims=True)
    top_ref[...] = top
    acc_ref[...] = jnp.dot(
        cache_expo.astype(jnp.bfloat16), vc_ref[...], preferred_element_type=jnp.float32
    ) + jnp.dot(new_expo.astype(jnp.bfloat16), vn_ref[...], preferred_element_type=jnp.float32)


def attention(scalars, q_rows, q_tok, keys_cache, values_cache, keys_new, values_new, key_tok):
    rows, width = q_rows.shape
    cache_rows = keys_cache.shape[0]
    new_rows = keys_new.shape[0]
    block = 512
    full = lambda shape: pl.BlockSpec(shape, lambda i, s: (0, 0))
    row_block = lambda cols: pl.BlockSpec((block, cols), lambda i, s: (i, 0))
    flops = 4 * rows * (cache_rows + new_rows) * width
    return pl.pallas_call(
        attention_kernel,
        out_shape=(
            jax.ShapeDtypeStruct((rows, width), jnp.float32),
            jax.ShapeDtypeStruct((rows, 1), jnp.float32),
            jax.ShapeDtypeStruct((rows, 1), jnp.float32),
        ),
        grid_spec=pltpu.PrefetchScalarGridSpec(
            num_scalar_prefetch=1,
            grid=(rows // block,),
            in_specs=[
                row_block(width),
                row_block(1),
                full((cache_rows, width)),
                full((cache_rows, width)),
                full((new_rows, width)),
                full((new_rows, width)),
                full((1, new_rows)),
            ],
            out_specs=[row_block(width), row_block(1), row_block(1)],
        ),
        cost_estimate=pl.CostEstimate(
            flops=flops,
            transcendentals=rows * (cache_rows + new_rows),
            bytes_accessed=2 * (rows + 2 * cache_rows + 2 * new_rows) * width + 4 * rows * width,
        ),
    )(scalars, q_rows, q_tok, keys_cache, values_cache, keys_new, values_new, key_tok)


def per_device(
    hidden_in,
    norm_gain,
    w_query,
    w_key,
    w_value,
    w_headgate,
    w_out,
    q_gain,
    k_gain,
    cache_keys,
    cache_values,
    cached_len,
    group_of,
):
    tok_rows = hidden_in.shape[0]
    head_dim = q_gain.shape[0]
    kv_local = w_key.shape[1] // head_dim
    heads_local = w_query.shape[1] // head_dim
    group_size = heads_local // kv_local
    per_request = SPAN // tok_rows
    ring_x = lax.axis_size("sx")
    ring_z = lax.axis_size("sz")
    req_count = ring_x * ring_z // per_request
    pair = ring_z // req_count
    x_index = lax.axis_index("sx")
    z_index = lax.axis_index("sz")
    seq_index = x_index * ring_z + z_index
    request = seq_index % req_count
    local_part = seq_index // req_count
    parity = z_index // req_count
    length = cached_len[request]

    peer_groups = group_of[jnp.arange(ring_z, dtype=jnp.int32) % req_count]
    cache_both = jnp.stack([cache_keys, cache_values], 1)
    incoming = lax.all_to_all(cache_both[peer_groups], "sz", 0, 0, tiled=True)
    cache_rows = ring_z * cache_keys.shape[1]
    keys_cache = incoming[:, 0].reshape(cache_rows, kv_local, head_dim)
    values_cache = incoming[:, 1].reshape(cache_rows, kv_local, head_dim)
    cache_pos = x_index * cache_rows + jnp.arange(cache_rows, dtype=jnp.int32)

    gathered = lax.all_gather(hidden_in, "tp", axis=1, tiled=True)
    widened = gathered.astype(jnp.float32)
    normed = (
        widened * lax.rsqrt(jnp.mean(widened * widened, -1, keepdims=True) + norm_eps) * norm_gain
    ).astype(jnp.bfloat16)
    positions = length + local_part * tok_rows + jnp.arange(tok_rows, dtype=jnp.int32)
    query_raw = jnp.dot(normed, w_query, preferred_element_type=jnp.float32).reshape(
        tok_rows, kv_local, group_size, head_dim
    )
    queries = rotate(head_norm(query_raw, q_gain), positions).astype(jnp.bfloat16)
    key_raw = jnp.dot(normed, w_key, preferred_element_type=jnp.float32).reshape(
        tok_rows, kv_local, head_dim
    )
    keys_new = rotate(head_norm(key_raw, k_gain), positions).astype(jnp.bfloat16)
    values_new = (
        jnp.dot(normed, w_value, preferred_element_type=jnp.float32)
        .astype(jnp.bfloat16)
        .reshape(tok_rows, kv_local, head_dim)
    )
    gates = jax.nn.sigmoid(jnp.dot(normed, w_headgate, preferred_element_type=jnp.float32)).reshape(
        tok_rows, kv_local, group_size
    )

    partner_pairs = [(z, (z + req_count) % ring_z) for z in range(ring_z)]
    partner_kv = lax.ppermute(jnp.stack([keys_new, values_new]), "sz", partner_pairs)
    partner_part = x_index * pair + (pair - 1 - parity)
    all_queries = lax.all_gather(queries, "sx", axis=0, tiled=True)
    query_tok = (
        (jnp.arange(ring_x, dtype=jnp.int32) * pair + parity)[:, None] * tok_rows
        + jnp.arange(tok_rows, dtype=jnp.int32)[None, :]
    ).reshape(-1)
    row_ids = jnp.arange(tok_rows, dtype=jnp.int32)
    key_tok = jnp.concatenate([local_part * tok_rows + row_ids, partner_part * tok_rows + row_ids])
    keys_two = jnp.concatenate([keys_new, partner_kv[0]], 0).reshape(-1, head_dim)
    values_two = jnp.concatenate([values_new, partner_kv[1]], 0).reshape(-1, head_dim)
    query_count = query_tok.shape[0]
    scalars = jnp.stack([length, x_index * cache_rows]).astype(jnp.int32)
    acc, top, total = attention(
        scalars,
        all_queries.reshape(-1, head_dim),
        jnp.repeat(query_tok, heads_local)[:, None],
        keys_cache.reshape(cache_rows, head_dim),
        values_cache.reshape(cache_rows, head_dim),
        keys_two,
        values_two,
        key_tok[None, :],
    )
    slot_rows = tok_rows * heads_local
    stats = jnp.concatenate([top, total], -1).reshape(ring_x, -1, head_dim)
    packed = jnp.concatenate([acc.reshape(ring_x, slot_rows, head_dim), stats], 1)
    packed_in = lax.all_to_all(packed, "sx", 0, 0, tiled=True)
    acc_in = packed_in[:, :slot_rows].reshape(ring_x, tok_rows, kv_local, group_size, head_dim)
    stats_in = packed_in[:, slot_rows:].reshape(ring_x, tok_rows, kv_local, group_size, 2)
    best = jnp.max(stats_in[..., 0], 0)
    factor = jnp.exp(stats_in[..., 0] - best[None])
    total = jnp.sum(stats_in[..., 1] * factor, 0)
    summed_acc = jnp.sum(acc_in * factor[..., None], 0)
    mixed = (
        (summed_acc / total[..., None] * gates[..., None])
        .astype(jnp.bfloat16)
        .reshape(tok_rows, heads_local * head_dim)
    )
    partial_out = jnp.dot(mixed, w_out, preferred_element_type=jnp.float32)
    tp_size = lax.axis_size("tp")
    pieces = partial_out.astype(jnp.bfloat16).reshape(tok_rows, tp_size, -1)
    arrived = lax.all_to_all(pieces, "tp", 1, 1, tiled=True)
    summed = jnp.sum(arrived.astype(jnp.float32), 1)
    return (hidden_in.astype(jnp.float32) + summed).astype(jnp.bfloat16)


def solution(mesh):
    seq_size = mesh.shape["seq"]
    tp_size = mesh.shape["tp"]
    req_count = seq_size // (SPAN // 128)
    ring_z = 2 * req_count
    ring_x = seq_size // ring_z
    split_mesh = Mesh(mesh.devices.reshape(ring_x, ring_z, tp_size), ("sx", "sz", "tp"))
    seq = ("sx", "sz")
    in_specs = (
        P(seq, "tp"),
        P(),
        P(None, "tp"),
        P(None, "tp"),
        P(None, "tp"),
        P(None, "tp"),
        P("tp", None),
        P(),
        P(),
        P(None, seq, "tp"),
        P(None, seq, "tp"),
        P(),
        P(),
    )
    out_specs = P(seq, "tp")
    return jax.shard_map(
        per_device, mesh=split_mesh, in_specs=in_specs, out_specs=out_specs, check_vma=False
    )
```

```python
import math

import jax
import jax.numpy as jnp
from jax import lax
from jax.experimental import pallas as pl
from jax.experimental.pallas import tpu as pltpu
from jax.sharding import Mesh, PartitionSpec as P

SPAN = 1024


norm_eps = 1e-06
rope_base = 1000000.0
masked_score = -1e30


def shifted(value, axis, by):
    peers = lax.axis_size(axis)
    pairs = [(i, i + by) for i in range(peers) if 0 <= i + by < peers]
    return lax.ppermute(value, axis, pairs)


def head_norm(vec, gain):
    return vec * lax.rsqrt(jnp.mean(vec * vec, -1, keepdims=True) + norm_eps) * gain


def rotate(vec, positions):
    half = vec.shape[-1] // 2
    freq = jnp.exp(
        jnp.arange(half, dtype=jnp.float32) * (-2.0 * math.log(rope_base) / vec.shape[-1])
    )
    angle = positions.astype(jnp.float32)[:, None] * freq[None, :]
    shape_out = (vec.shape[0],) + (1,) * (vec.ndim - 2) + (half,)
    cosine = jnp.cos(angle).reshape(shape_out)
    sine = jnp.sin(angle).reshape(shape_out)
    first = vec[..., :half]
    second = vec[..., half:]
    return jnp.concatenate([first * cosine - second * sine, second * cosine + first * sine], -1)


def attend(state_now, queries, keys_block, values_block, visible):
    running_max, running_sum, running_acc = state_now
    scores = jnp.einsum(
        "tcgd,kcd->tcgk", queries, keys_block, preferred_element_type=jnp.float32
    ) * queries.shape[-1] ** (-0.5)
    scores = jnp.where(visible[:, None, None, :], scores, masked_score)
    new_max = jnp.maximum(running_max, jnp.max(scores, -1))
    rescale = jnp.exp(running_max - new_max)
    expo = jnp.exp(scores - new_max[..., None])
    new_sum = running_sum * rescale + jnp.sum(expo, -1)
    update = jnp.einsum(
        "tcgk,kcd->tcgd",
        expo.astype(jnp.bfloat16),
        values_block,
        preferred_element_type=jnp.float32,
    )
    return (new_max, new_sum, running_acc * rescale[..., None] + update)


def attention_kernel(
    scalars, q_ref, qtok_ref, kc_ref, vc_ref, kn_ref, vn_ref, ktok_ref, acc_ref, top_ref, total_ref
):
    scale = q_ref.shape[-1] ** (-0.5)
    dims = (((1,), (1,)), ((), ()))
    q = q_ref[...]
    cache_scores = lax.dot_general(q, kc_ref[...], dims, preferred_element_type=jnp.float32) * scale
    cache_pos = scalars[1] + lax.broadcasted_iota(jnp.int32, (1, kc_ref.shape[0]), 1)
    cache_seen = cache_pos < scalars[0]
    cache_scores = jnp.where(cache_seen, cache_scores, masked_score)
    new_scores = lax.dot_general(q, kn_ref[...], dims, preferred_element_type=jnp.float32) * scale
    new_seen = ktok_ref[...] <= qtok_ref[...]
    new_scores = jnp.where(new_seen, new_scores, masked_score)
    top = jnp.maximum(
        jnp.max(cache_scores, 1, keepdims=True), jnp.max(new_scores, 1, keepdims=True)
    )
    cache_expo = jnp.where(cache_seen, jnp.exp(cache_scores - top), 0.0)
    new_expo = jnp.where(new_seen, jnp.exp(new_scores - top), 0.0)
    total_ref[...] = jnp.sum(cache_expo, 1, keepdims=True) + jnp.sum(new_expo, 1, keepdims=True)
    top_ref[...] = top
    acc_ref[...] = jnp.dot(
        cache_expo.astype(jnp.bfloat16), vc_ref[...], preferred_element_type=jnp.float32
    ) + jnp.dot(new_expo.astype(jnp.bfloat16), vn_ref[...], preferred_element_type=jnp.float32)


def attention(scalars, q_rows, q_tok, keys_cache, values_cache, keys_new, values_new, key_tok):
    rows, width = q_rows.shape
    cache_rows = keys_cache.shape[0]
    new_rows = keys_new.shape[0]
    block = 128
    full = lambda shape: pl.BlockSpec(shape, lambda i, s: (0, 0))
    row_block = lambda cols: pl.BlockSpec((block, cols), lambda i, s: (i, 0))
    flops = 4 * rows * (cache_rows + new_rows) * width
    return pl.pallas_call(
        attention_kernel,
        out_shape=(
            jax.ShapeDtypeStruct((rows, width), jnp.float32),
            jax.ShapeDtypeStruct((rows, 1), jnp.float32),
            jax.ShapeDtypeStruct((rows, 1), jnp.float32),
        ),
        grid_spec=pltpu.PrefetchScalarGridSpec(
            num_scalar_prefetch=1,
            grid=(rows // block,),
            in_specs=[
                row_block(width),
                row_block(1),
                full((cache_rows, width)),
                full((cache_rows, width)),
                full((new_rows, width)),
                full((new_rows, width)),
                full((1, new_rows)),
            ],
            out_specs=[row_block(width), row_block(1), row_block(1)],
        ),
        cost_estimate=pl.CostEstimate(
            flops=flops,
            transcendentals=rows * (cache_rows + new_rows),
            bytes_accessed=2 * (rows + 2 * cache_rows + 2 * new_rows) * width + 4 * rows * width,
        ),
    )(scalars, q_rows, q_tok, keys_cache, values_cache, keys_new, values_new, key_tok)


def per_device(
    hidden_in,
    norm_gain,
    w_query,
    w_key,
    w_value,
    w_headgate,
    w_out,
    q_gain,
    k_gain,
    cache_keys,
    cache_values,
    cached_len,
    group_of,
):
    tok_rows = hidden_in.shape[0]
    head_dim = q_gain.shape[0]
    kv_local = w_key.shape[1] // head_dim
    heads_local = w_query.shape[1] // head_dim
    group_size = heads_local // kv_local
    per_request = SPAN // tok_rows
    ring_x = lax.axis_size("sx")
    ring_z = lax.axis_size("sz")
    req_count = ring_x * ring_z // per_request
    pair = ring_z // req_count
    x_index = lax.axis_index("sx")
    z_index = lax.axis_index("sz")
    seq_index = x_index * ring_z + z_index
    request = seq_index % req_count
    local_part = seq_index // req_count
    parity = z_index // req_count
    length = cached_len[request]

    peer_groups = group_of[jnp.arange(ring_z, dtype=jnp.int32) % req_count]
    cache_both = jnp.stack([cache_keys, cache_values], 1)
    incoming = lax.all_to_all(cache_both[peer_groups], "sz", 0, 0, tiled=True)
    cache_rows = ring_z * cache_keys.shape[1]
    keys_cache = incoming[:, 0].reshape(cache_rows, kv_local, head_dim)
    values_cache = incoming[:, 1].reshape(cache_rows, kv_local, head_dim)
    cache_pos = x_index * cache_rows + jnp.arange(cache_rows, dtype=jnp.int32)

    gathered = lax.all_gather(hidden_in, "tp", axis=1, tiled=True)
    widened = gathered.astype(jnp.float32)
    normed = (
        widened * lax.rsqrt(jnp.mean(widened * widened, -1, keepdims=True) + norm_eps) * norm_gain
    ).astype(jnp.bfloat16)
    positions = length + local_part * tok_rows + jnp.arange(tok_rows, dtype=jnp.int32)
    query_raw = jnp.dot(normed, w_query, preferred_element_type=jnp.float32).reshape(
        tok_rows, kv_local, group_size, head_dim
    )
    queries = rotate(head_norm(query_raw, q_gain), positions).astype(jnp.bfloat16)
    key_raw = jnp.dot(normed, w_key, preferred_element_type=jnp.float32).reshape(
        tok_rows, kv_local, head_dim
    )
    keys_new = rotate(head_norm(key_raw, k_gain), positions).astype(jnp.bfloat16)
    values_new = (
        jnp.dot(normed, w_value, preferred_element_type=jnp.float32)
        .astype(jnp.bfloat16)
        .reshape(tok_rows, kv_local, head_dim)
    )
    gates = jax.nn.sigmoid(jnp.dot(normed, w_headgate, preferred_element_type=jnp.float32)).reshape(
        tok_rows, kv_local, group_size
    )

    partner_pairs = [(z, (z + req_count) % ring_z) for z in range(ring_z)]
    partner_kv = lax.ppermute(jnp.stack([keys_new, values_new]), "sz", partner_pairs)
    partner_part = x_index * pair + (pair - 1 - parity)
    all_queries = lax.all_gather(queries, "sx", axis=0, tiled=True)
    query_tok = (
        (jnp.arange(ring_x, dtype=jnp.int32) * pair + parity)[:, None] * tok_rows
        + jnp.arange(tok_rows, dtype=jnp.int32)[None, :]
    ).reshape(-1)
    row_ids = jnp.arange(tok_rows, dtype=jnp.int32)
    key_tok = jnp.concatenate([local_part * tok_rows + row_ids, partner_part * tok_rows + row_ids])
    keys_two = jnp.concatenate([keys_new, partner_kv[0]], 0).reshape(-1, head_dim)
    values_two = jnp.concatenate([values_new, partner_kv[1]], 0).reshape(-1, head_dim)
    query_count = query_tok.shape[0]
    scalars = jnp.stack([length, x_index * cache_rows]).astype(jnp.int32)
    acc, top, total = attention(
        scalars,
        all_queries.reshape(-1, head_dim),
        jnp.repeat(query_tok, heads_local)[:, None],
        keys_cache.reshape(cache_rows, head_dim),
        values_cache.reshape(cache_rows, head_dim),
        keys_two,
        values_two,
        key_tok[None, :],
    )
    slot_rows = tok_rows * heads_local
    stats = jnp.concatenate([top, total], -1).reshape(ring_x, -1, head_dim)
    packed = jnp.concatenate([acc.reshape(ring_x, slot_rows, head_dim), stats], 1)
    packed_in = lax.all_to_all(packed, "sx", 0, 0, tiled=True)
    acc_in = packed_in[:, :slot_rows].reshape(ring_x, tok_rows, kv_local, group_size, head_dim)
    stats_in = packed_in[:, slot_rows:].reshape(ring_x, tok_rows, kv_local, group_size, 2)
    best = jnp.max(stats_in[..., 0], 0)
    factor = jnp.exp(stats_in[..., 0] - best[None])
    total = jnp.sum(stats_in[..., 1] * factor, 0)
    summed_acc = jnp.sum(acc_in * factor[..., None], 0)
    mixed = (
        (summed_acc / total[..., None] * gates[..., None])
        .astype(jnp.bfloat16)
        .reshape(tok_rows, heads_local * head_dim)
    )
    partial_out = jnp.dot(mixed, w_out, preferred_element_type=jnp.float32)
    tp_size = lax.axis_size("tp")
    pieces = partial_out.astype(jnp.bfloat16).reshape(tok_rows, tp_size, -1)
    arrived = lax.all_to_all(pieces, "tp", 1, 1, tiled=True)
    summed = jnp.sum(arrived.astype(jnp.float32), 1)
    return (hidden_in.astype(jnp.float32) + summed).astype(jnp.bfloat16)


def solution(mesh):
    seq_size = mesh.shape["seq"]
    tp_size = mesh.shape["tp"]
    req_count = seq_size // (SPAN // 128)
    ring_z = 2 * req_count
    ring_x = seq_size // ring_z
    split_mesh = Mesh(mesh.devices.reshape(ring_x, ring_z, tp_size), ("sx", "sz", "tp"))
    seq = ("sx", "sz")
    in_specs = (
        P(seq, "tp"),
        P(),
        P(None, "tp"),
        P(None, "tp"),
        P(None, "tp"),
        P(None, "tp"),
        P("tp", None),
        P(),
        P(),
        P(None, seq, "tp"),
        P(None, seq, "tp"),
        P(),
        P(),
    )
    out_specs = P(seq, "tp")
    return jax.shard_map(
        per_device, mesh=split_mesh, in_specs=in_specs, out_specs=out_specs, check_vma=False
    )
```

```python
import math

import jax
import jax.numpy as jnp
from jax import lax
from jax.experimental import pallas as pl
from jax.experimental.pallas import tpu as pltpu
from jax.sharding import Mesh, PartitionSpec as P

SPAN = 1024


norm_eps = 1e-06
rope_base = 1000000.0
masked_score = -1e30


def shifted(value, axis, by):
    peers = lax.axis_size(axis)
    pairs = [(i, i + by) for i in range(peers) if 0 <= i + by < peers]
    return lax.ppermute(value, axis, pairs)


def head_norm(vec, gain):
    return vec * lax.rsqrt(jnp.mean(vec * vec, -1, keepdims=True) + norm_eps) * gain


def rotate(vec, positions):
    half = vec.shape[-1] // 2
    freq = jnp.exp(
        jnp.arange(half, dtype=jnp.float32) * (-2.0 * math.log(rope_base) / vec.shape[-1])
    )
    angle = positions.astype(jnp.float32)[:, None] * freq[None, :]
    shape_out = (vec.shape[0],) + (1,) * (vec.ndim - 2) + (half,)
    cosine = jnp.cos(angle).reshape(shape_out)
    sine = jnp.sin(angle).reshape(shape_out)
    first = vec[..., :half]
    second = vec[..., half:]
    return jnp.concatenate([first * cosine - second * sine, second * cosine + first * sine], -1)


def attend(state_now, queries, keys_block, values_block, visible):
    running_max, running_sum, running_acc = state_now
    scores = jnp.einsum(
        "tcgd,kcd->tcgk", queries, keys_block, preferred_element_type=jnp.float32
    ) * queries.shape[-1] ** (-0.5)
    scores = jnp.where(visible[:, None, None, :], scores, masked_score)
    new_max = jnp.maximum(running_max, jnp.max(scores, -1))
    rescale = jnp.exp(running_max - new_max)
    expo = jnp.exp(scores - new_max[..., None])
    new_sum = running_sum * rescale + jnp.sum(expo, -1)
    update = jnp.einsum(
        "tcgk,kcd->tcgd",
        expo.astype(jnp.bfloat16),
        values_block,
        preferred_element_type=jnp.float32,
    )
    return (new_max, new_sum, running_acc * rescale[..., None] + update)


def attention_kernel(scalars, q_ref, qtok_ref, kc_ref, vc_ref, kn_ref, vn_ref, ktok_ref, out_ref):
    scale = q_ref.shape[-1] ** (-0.5)
    dims = (((1,), (1,)), ((), ()))
    q = q_ref[...]
    cache_scores = lax.dot_general(q, kc_ref[...], dims, preferred_element_type=jnp.float32) * scale
    cache_pos = scalars[1] + lax.broadcasted_iota(jnp.int32, (1, kc_ref.shape[0]), 1)
    cache_seen = cache_pos < scalars[0]
    cache_scores = jnp.where(cache_seen, cache_scores, masked_score)
    new_scores = lax.dot_general(q, kn_ref[...], dims, preferred_element_type=jnp.float32) * scale
    new_seen = ktok_ref[...] <= qtok_ref[...]
    new_scores = jnp.where(new_seen, new_scores, masked_score)
    top = jnp.maximum(
        jnp.max(cache_scores, 1, keepdims=True), jnp.max(new_scores, 1, keepdims=True)
    )
    cache_expo = jnp.where(cache_seen, jnp.exp(cache_scores - top), 0.0)
    new_expo = jnp.where(new_seen, jnp.exp(new_scores - top), 0.0)
    total = jnp.sum(cache_expo, 1, keepdims=True) + jnp.sum(new_expo, 1, keepdims=True)
    acc = jnp.dot(
        cache_expo.astype(jnp.bfloat16), vc_ref[...], preferred_element_type=jnp.float32
    ) + jnp.dot(new_expo.astype(jnp.bfloat16), vn_ref[...], preferred_element_type=jnp.float32)
    rows, width = acc.shape
    top_t = jnp.transpose(jnp.broadcast_to(top, (rows, width)))[0:1]
    total_t = jnp.transpose(jnp.broadcast_to(total, (rows, width)))[0:1]
    out_ref[0, :rows, :] = acc
    for half in range(rows // width):
        cols = slice(half * width, (half + 1) * width)
        out_ref[0, rows + half : rows + half + 1, :] = top_t[:, cols]
        out_ref[0, rows + rows // width + half : rows + rows // width + half + 1, :] = total_t[:, cols]


def attention(scalars, q_rows, q_tok, keys_cache, values_cache, keys_new, values_new, key_tok):
    rows, width = q_rows.shape
    cache_rows = keys_cache.shape[0]
    new_rows = keys_new.shape[0]
    block = 256
    packed_rows = block + 2 * (block // width)
    full = lambda shape: pl.BlockSpec(shape, lambda i, s: (0, 0))
    row_block = lambda cols: pl.BlockSpec((block, cols), lambda i, s: (i, 0))
    flops = 4 * rows * (cache_rows + new_rows) * width
    return pl.pallas_call(
        attention_kernel,
        out_shape=jax.ShapeDtypeStruct((rows // block, packed_rows, width), jnp.float32),
        grid_spec=pltpu.PrefetchScalarGridSpec(
            num_scalar_prefetch=1,
            grid=(rows // block,),
            in_specs=[
                row_block(width),
                row_block(1),
                full((cache_rows, width)),
                full((cache_rows, width)),
                full((new_rows, width)),
                full((new_rows, width)),
                full((1, new_rows)),
            ],
            out_specs=pl.BlockSpec((1, packed_rows, width), lambda i, s: (i, 0, 0)),
        ),
        cost_estimate=pl.CostEstimate(
            flops=flops,
            transcendentals=rows * (cache_rows + new_rows),
            bytes_accessed=2 * (rows + 2 * cache_rows + 2 * new_rows) * width + 4 * rows * width,
        ),
    )(scalars, q_rows, q_tok, keys_cache, values_cache, keys_new, values_new, key_tok)


def per_device(
    hidden_in,
    norm_gain,
    w_query,
    w_key,
    w_value,
    w_headgate,
    w_out,
    q_gain,
    k_gain,
    cache_keys,
    cache_values,
    cached_len,
    group_of,
):
    tok_rows = hidden_in.shape[0]
    head_dim = q_gain.shape[0]
    kv_local = w_key.shape[1] // head_dim
    heads_local = w_query.shape[1] // head_dim
    group_size = heads_local // kv_local
    per_request = SPAN // tok_rows
    ring_x = lax.axis_size("sx")
    ring_z = lax.axis_size("sz")
    req_count = ring_x * ring_z // per_request
    pair = ring_z // req_count
    x_index = lax.axis_index("sx")
    z_index = lax.axis_index("sz")
    seq_index = x_index * ring_z + z_index
    request = seq_index % req_count
    local_part = seq_index // req_count
    parity = z_index // req_count
    length = cached_len[request]

    peer_groups = group_of[jnp.arange(ring_z, dtype=jnp.int32) % req_count]
    cache_both = jnp.stack([cache_keys, cache_values], 1)
    incoming = lax.all_to_all(cache_both[peer_groups], "sz", 0, 0, tiled=True)
    cache_rows = ring_z * cache_keys.shape[1]
    keys_cache = incoming[:, 0].reshape(cache_rows, kv_local, head_dim)
    values_cache = incoming[:, 1].reshape(cache_rows, kv_local, head_dim)
    cache_pos = x_index * cache_rows + jnp.arange(cache_rows, dtype=jnp.int32)

    gathered = lax.all_gather(hidden_in, "tp", axis=1, tiled=True)
    widened = gathered.astype(jnp.float32)
    normed = (
        widened * lax.rsqrt(jnp.mean(widened * widened, -1, keepdims=True) + norm_eps) * norm_gain
    ).astype(jnp.bfloat16)
    positions = length + local_part * tok_rows + jnp.arange(tok_rows, dtype=jnp.int32)
    query_raw = jnp.dot(normed, w_query, preferred_element_type=jnp.float32).reshape(
        tok_rows, kv_local, group_size, head_dim
    )
    queries = rotate(head_norm(query_raw, q_gain), positions).astype(jnp.bfloat16)
    key_raw = jnp.dot(normed, w_key, preferred_element_type=jnp.float32).reshape(
        tok_rows, kv_local, head_dim
    )
    keys_new = rotate(head_norm(key_raw, k_gain), positions).astype(jnp.bfloat16)
    values_new = (
        jnp.dot(normed, w_value, preferred_element_type=jnp.float32)
        .astype(jnp.bfloat16)
        .reshape(tok_rows, kv_local, head_dim)
    )
    gates = jax.nn.sigmoid(jnp.dot(normed, w_headgate, preferred_element_type=jnp.float32)).reshape(
        tok_rows, kv_local, group_size
    )

    partner_pairs = [(z, (z + req_count) % ring_z) for z in range(ring_z)]
    partner_kv = lax.ppermute(jnp.stack([keys_new, values_new]), "sz", partner_pairs)
    partner_part = x_index * pair + (pair - 1 - parity)
    all_queries = lax.all_gather(queries, "sx", axis=0, tiled=True)
    query_tok = (
        (jnp.arange(ring_x, dtype=jnp.int32) * pair + parity)[:, None] * tok_rows
        + jnp.arange(tok_rows, dtype=jnp.int32)[None, :]
    ).reshape(-1)
    row_ids = jnp.arange(tok_rows, dtype=jnp.int32)
    key_tok = jnp.concatenate([local_part * tok_rows + row_ids, partner_part * tok_rows + row_ids])
    keys_two = jnp.concatenate([keys_new, partner_kv[0]], 0).reshape(-1, head_dim)
    values_two = jnp.concatenate([values_new, partner_kv[1]], 0).reshape(-1, head_dim)
    query_count = query_tok.shape[0]
    scalars = jnp.stack([length, x_index * cache_rows]).astype(jnp.int32)
    packed = attention(
        scalars,
        all_queries.reshape(-1, head_dim),
        jnp.repeat(query_tok, heads_local)[:, None],
        keys_cache.reshape(cache_rows, head_dim),
        values_cache.reshape(cache_rows, head_dim),
        keys_two,
        values_two,
        key_tok[None, :],
    )
    slot_rows = tok_rows * heads_local
    packed_in = lax.all_to_all(packed, "sx", 0, 0, tiled=True)
    acc_in = packed_in[:, :slot_rows].reshape(ring_x, tok_rows, kv_local, group_size, head_dim)
    stats_in = packed_in[:, slot_rows:].reshape(ring_x, 2, tok_rows, kv_local, group_size)
    stats_in = jnp.moveaxis(stats_in, 1, -1)
    best = jnp.max(stats_in[..., 0], 0)
    factor = jnp.exp(stats_in[..., 0] - best[None])
    total = jnp.sum(stats_in[..., 1] * factor, 0)
    summed_acc = jnp.sum(acc_in * factor[..., None], 0)
    mixed = (
        (summed_acc / total[..., None] * gates[..., None])
        .astype(jnp.bfloat16)
        .reshape(tok_rows, heads_local * head_dim)
    )
    partial_out = jnp.dot(mixed, w_out, preferred_element_type=jnp.float32)
    tp_size = lax.axis_size("tp")
    pieces = partial_out.astype(jnp.bfloat16).reshape(tok_rows, tp_size, -1)
    arrived = lax.all_to_all(pieces, "tp", 1, 1, tiled=True)
    summed = jnp.sum(arrived.astype(jnp.float32), 1)
    return (hidden_in.astype(jnp.float32) + summed).astype(jnp.bfloat16)


def solution(mesh):
    seq_size = mesh.shape["seq"]
    tp_size = mesh.shape["tp"]
    req_count = seq_size // (SPAN // 128)
    ring_z = 2 * req_count
    ring_x = seq_size // ring_z
    split_mesh = Mesh(mesh.devices.reshape(ring_x, ring_z, tp_size), ("sx", "sz", "tp"))
    seq = ("sx", "sz")
    in_specs = (
        P(seq, "tp"),
        P(),
        P(None, "tp"),
        P(None, "tp"),
        P(None, "tp"),
        P(None, "tp"),
        P("tp", None),
        P(),
        P(),
        P(None, seq, "tp"),
        P(None, seq, "tp"),
        P(),
        P(),
    )
    out_specs = P(seq, "tp")
    return jax.shard_map(
        per_device, mesh=split_mesh, in_specs=in_specs, out_specs=out_specs, check_vma=False
    )
```

```python
import math

import jax
import jax.numpy as jnp
from jax import lax
from jax.experimental import pallas as pl
from jax.experimental.pallas import tpu as pltpu
from jax.sharding import Mesh, PartitionSpec as P

SPAN = 1024


norm_eps = 1e-06
rope_base = 1000000.0
masked_score = -1e30


def shifted(value, axis, by):
    peers = lax.axis_size(axis)
    pairs = [(i, i + by) for i in range(peers) if 0 <= i + by < peers]
    return lax.ppermute(value, axis, pairs)


def head_norm(vec, gain):
    return vec * lax.rsqrt(jnp.mean(vec * vec, -1, keepdims=True) + norm_eps) * gain


def rotate(vec, positions):
    half = vec.shape[-1] // 2
    freq = jnp.exp(
        jnp.arange(half, dtype=jnp.float32) * (-2.0 * math.log(rope_base) / vec.shape[-1])
    )
    angle = positions.astype(jnp.float32)[:, None] * freq[None, :]
    shape_out = (vec.shape[0],) + (1,) * (vec.ndim - 2) + (half,)
    cosine = jnp.cos(angle).reshape(shape_out)
    sine = jnp.sin(angle).reshape(shape_out)
    first = vec[..., :half]
    second = vec[..., half:]
    return jnp.concatenate([first * cosine - second * sine, second * cosine + first * sine], -1)


def attend(state_now, queries, keys_block, values_block, visible):
    running_max, running_sum, running_acc = state_now
    scores = jnp.einsum(
        "tcgd,kcd->tcgk", queries, keys_block, preferred_element_type=jnp.float32
    ) * queries.shape[-1] ** (-0.5)
    scores = jnp.where(visible[:, None, None, :], scores, masked_score)
    new_max = jnp.maximum(running_max, jnp.max(scores, -1))
    rescale = jnp.exp(running_max - new_max)
    expo = jnp.exp(scores - new_max[..., None])
    new_sum = running_sum * rescale + jnp.sum(expo, -1)
    update = jnp.einsum(
        "tcgk,kcd->tcgd",
        expo.astype(jnp.bfloat16),
        values_block,
        preferred_element_type=jnp.float32,
    )
    return (new_max, new_sum, running_acc * rescale[..., None] + update)


def attention_kernel(scalars, q_ref, qtok_ref, cache_ref, kn_ref, vn_ref, ktok_ref, out_ref):
    scale = q_ref.shape[-1] ** (-0.5)
    dims = (((1,), (1,)), ((), ()))
    q = q_ref[...]
    sources, _, depth, width = cache_ref.shape
    keys_cache = cache_ref[:, 0].reshape(sources * depth, width)
    values_cache = cache_ref[:, 1].reshape(sources * depth, width)
    cache_scores = lax.dot_general(q, keys_cache, dims, preferred_element_type=jnp.float32) * scale
    cache_pos = scalars[1] + lax.broadcasted_iota(jnp.int32, (1, sources * depth), 1)
    cache_seen = cache_pos < scalars[0]
    cache_scores = jnp.where(cache_seen, cache_scores, masked_score)
    new_scores = lax.dot_general(q, kn_ref[...], dims, preferred_element_type=jnp.float32) * scale
    new_seen = ktok_ref[...] <= qtok_ref[...]
    new_scores = jnp.where(new_seen, new_scores, masked_score)
    top = jnp.maximum(
        jnp.max(cache_scores, 1, keepdims=True), jnp.max(new_scores, 1, keepdims=True)
    )
    cache_expo = jnp.where(cache_seen, jnp.exp(cache_scores - top), 0.0)
    new_expo = jnp.where(new_seen, jnp.exp(new_scores - top), 0.0)
    total = jnp.sum(cache_expo, 1, keepdims=True) + jnp.sum(new_expo, 1, keepdims=True)
    acc = jnp.dot(
        cache_expo.astype(jnp.bfloat16), values_cache, preferred_element_type=jnp.float32
    ) + jnp.dot(new_expo.astype(jnp.bfloat16), vn_ref[...], preferred_element_type=jnp.float32)
    rows, width = acc.shape
    top_t = jnp.transpose(jnp.broadcast_to(top, (rows, width)))[0:1]
    total_t = jnp.transpose(jnp.broadcast_to(total, (rows, width)))[0:1]
    out_ref[0, :rows, :] = acc
    for half in range(rows // width):
        cols = slice(half * width, (half + 1) * width)
        out_ref[0, rows + half : rows + half + 1, :] = top_t[:, cols]
        out_ref[0, rows + rows // width + half : rows + rows // width + half + 1, :] = total_t[:, cols]


def attention(scalars, q_rows, q_tok, cache_both, keys_new, values_new, key_tok):
    rows, width = q_rows.shape
    cache_rows = cache_both.shape[0] * cache_both.shape[2]
    new_rows = keys_new.shape[0]
    block = 256
    packed_rows = block + 2 * (block // width)
    full = lambda shape: pl.BlockSpec(shape, lambda i, s: (0, 0))
    row_block = lambda cols: pl.BlockSpec((block, cols), lambda i, s: (i, 0))
    flops = 4 * rows * (cache_rows + new_rows) * width
    return pl.pallas_call(
        attention_kernel,
        out_shape=jax.ShapeDtypeStruct((rows // block, packed_rows, width), jnp.float32),
        grid_spec=pltpu.PrefetchScalarGridSpec(
            num_scalar_prefetch=1,
            grid=(rows // block,),
            in_specs=[
                row_block(width),
                row_block(1),
                pl.BlockSpec(cache_both.shape, lambda i, s: (0, 0, 0, 0)),
                full((new_rows, width)),
                full((new_rows, width)),
                full((1, new_rows)),
            ],
            out_specs=pl.BlockSpec((1, packed_rows, width), lambda i, s: (i, 0, 0)),
        ),
        cost_estimate=pl.CostEstimate(
            flops=flops,
            transcendentals=rows * (cache_rows + new_rows),
            bytes_accessed=2 * (rows + 2 * cache_rows + 2 * new_rows) * width + 4 * rows * width,
        ),
    )(scalars, q_rows, q_tok, cache_both, keys_new, values_new, key_tok)


def per_device(
    hidden_in,
    norm_gain,
    w_query,
    w_key,
    w_value,
    w_headgate,
    w_out,
    q_gain,
    k_gain,
    cache_keys,
    cache_values,
    cached_len,
    group_of,
):
    tok_rows = hidden_in.shape[0]
    head_dim = q_gain.shape[0]
    kv_local = w_key.shape[1] // head_dim
    heads_local = w_query.shape[1] // head_dim
    group_size = heads_local // kv_local
    per_request = SPAN // tok_rows
    ring_x = lax.axis_size("sx")
    ring_z = lax.axis_size("sz")
    req_count = ring_x * ring_z // per_request
    pair = ring_z // req_count
    x_index = lax.axis_index("sx")
    z_index = lax.axis_index("sz")
    seq_index = x_index * ring_z + z_index
    request = seq_index % req_count
    local_part = seq_index // req_count
    parity = z_index // req_count
    length = cached_len[request]

    peer_groups = group_of[jnp.arange(ring_z, dtype=jnp.int32) % req_count]
    cache_both = jnp.stack([cache_keys, cache_values], 1)
    incoming = lax.all_to_all(cache_both[peer_groups], "sz", 0, 0, tiled=True)
    cache_rows = ring_z * cache_keys.shape[1]
    keys_cache = incoming[:, 0].reshape(cache_rows, kv_local, head_dim)
    values_cache = incoming[:, 1].reshape(cache_rows, kv_local, head_dim)
    cache_pos = x_index * cache_rows + jnp.arange(cache_rows, dtype=jnp.int32)

    gathered = lax.all_gather(hidden_in, "tp", axis=1, tiled=True)
    widened = gathered.astype(jnp.float32)
    normed = (
        widened * lax.rsqrt(jnp.mean(widened * widened, -1, keepdims=True) + norm_eps) * norm_gain
    ).astype(jnp.bfloat16)
    positions = length + local_part * tok_rows + jnp.arange(tok_rows, dtype=jnp.int32)
    query_raw = jnp.dot(normed, w_query, preferred_element_type=jnp.float32).reshape(
        tok_rows, kv_local, group_size, head_dim
    )
    queries = rotate(head_norm(query_raw, q_gain), positions).astype(jnp.bfloat16)
    key_raw = jnp.dot(normed, w_key, preferred_element_type=jnp.float32).reshape(
        tok_rows, kv_local, head_dim
    )
    keys_new = rotate(head_norm(key_raw, k_gain), positions).astype(jnp.bfloat16)
    values_new = (
        jnp.dot(normed, w_value, preferred_element_type=jnp.float32)
        .astype(jnp.bfloat16)
        .reshape(tok_rows, kv_local, head_dim)
    )
    gates = jax.nn.sigmoid(jnp.dot(normed, w_headgate, preferred_element_type=jnp.float32)).reshape(
        tok_rows, kv_local, group_size
    )

    partner_pairs = [(z, (z + req_count) % ring_z) for z in range(ring_z)]
    partner_kv = lax.ppermute(jnp.stack([keys_new, values_new]), "sz", partner_pairs)
    partner_part = x_index * pair + (pair - 1 - parity)
    all_queries = lax.all_gather(queries, "sx", axis=0, tiled=True)
    query_tok = (
        (jnp.arange(ring_x, dtype=jnp.int32) * pair + parity)[:, None] * tok_rows
        + jnp.arange(tok_rows, dtype=jnp.int32)[None, :]
    ).reshape(-1)
    row_ids = jnp.arange(tok_rows, dtype=jnp.int32)
    key_tok = jnp.concatenate([local_part * tok_rows + row_ids, partner_part * tok_rows + row_ids])
    keys_two = jnp.concatenate([keys_new, partner_kv[0]], 0).reshape(-1, head_dim)
    values_two = jnp.concatenate([values_new, partner_kv[1]], 0).reshape(-1, head_dim)
    query_count = query_tok.shape[0]
    scalars = jnp.stack([length, x_index * cache_rows]).astype(jnp.int32)
    packed = attention(
        scalars,
        all_queries.reshape(-1, head_dim),
        jnp.repeat(query_tok, heads_local)[:, None],
        incoming,
        keys_two,
        values_two,
        key_tok[None, :],
    )
    slot_rows = tok_rows * heads_local
    packed_in = lax.all_to_all(packed, "sx", 0, 0, tiled=True)
    acc_in = packed_in[:, :slot_rows].reshape(ring_x, tok_rows, kv_local, group_size, head_dim)
    stats_in = packed_in[:, slot_rows:].reshape(ring_x, 2, tok_rows, kv_local, group_size)
    stats_in = jnp.moveaxis(stats_in, 1, -1)
    best = jnp.max(stats_in[..., 0], 0)
    factor = jnp.exp(stats_in[..., 0] - best[None])
    total = jnp.sum(stats_in[..., 1] * factor, 0)
    summed_acc = jnp.sum(acc_in * factor[..., None], 0)
    mixed = (
        (summed_acc / total[..., None] * gates[..., None])
        .astype(jnp.bfloat16)
        .reshape(tok_rows, heads_local * head_dim)
    )
    partial_out = jnp.dot(mixed, w_out, preferred_element_type=jnp.float32)
    tp_size = lax.axis_size("tp")
    pieces = partial_out.astype(jnp.bfloat16).reshape(tok_rows, tp_size, -1)
    arrived = lax.all_to_all(pieces, "tp", 1, 1, tiled=True)
    summed = jnp.sum(arrived.astype(jnp.float32), 1)
    return (hidden_in.astype(jnp.float32) + summed).astype(jnp.bfloat16)


def solution(mesh):
    seq_size = mesh.shape["seq"]
    tp_size = mesh.shape["tp"]
    req_count = seq_size // (SPAN // 128)
    ring_z = 2 * req_count
    ring_x = seq_size // ring_z
    split_mesh = Mesh(mesh.devices.reshape(ring_x, ring_z, tp_size), ("sx", "sz", "tp"))
    seq = ("sx", "sz")
    in_specs = (
        P(seq, "tp"),
        P(),
        P(None, "tp"),
        P(None, "tp"),
        P(None, "tp"),
        P(None, "tp"),
        P("tp", None),
        P(),
        P(),
        P(None, seq, "tp"),
        P(None, seq, "tp"),
        P(),
        P(),
    )
    out_specs = P(seq, "tp")
    return jax.shard_map(
        per_device, mesh=split_mesh, in_specs=in_specs, out_specs=out_specs, check_vma=False
    )
```

```python
import math

import jax
import jax.numpy as jnp
from jax import lax
from jax.experimental import pallas as pl
from jax.experimental.pallas import tpu as pltpu
from jax.sharding import Mesh, PartitionSpec as P

SPAN = 1024


norm_eps = 1e-06
rope_base = 1000000.0
masked_score = -1e30


def shifted(value, axis, by):
    peers = lax.axis_size(axis)
    pairs = [(i, i + by) for i in range(peers) if 0 <= i + by < peers]
    return lax.ppermute(value, axis, pairs)


def head_norm(vec, gain):
    return vec * lax.rsqrt(jnp.mean(vec * vec, -1, keepdims=True) + norm_eps) * gain


def rotate(vec, positions):
    half = vec.shape[-1] // 2
    freq = jnp.exp(
        jnp.arange(half, dtype=jnp.float32) * (-2.0 * math.log(rope_base) / vec.shape[-1])
    )
    angle = positions.astype(jnp.float32)[:, None] * freq[None, :]
    shape_out = (vec.shape[0],) + (1,) * (vec.ndim - 2) + (half,)
    cosine = jnp.cos(angle).reshape(shape_out)
    sine = jnp.sin(angle).reshape(shape_out)
    first = vec[..., :half]
    second = vec[..., half:]
    return jnp.concatenate([first * cosine - second * sine, second * cosine + first * sine], -1)


def attend(state_now, queries, keys_block, values_block, visible):
    running_max, running_sum, running_acc = state_now
    scores = jnp.einsum(
        "tcgd,kcd->tcgk", queries, keys_block, preferred_element_type=jnp.float32
    ) * queries.shape[-1] ** (-0.5)
    scores = jnp.where(visible[:, None, None, :], scores, masked_score)
    new_max = jnp.maximum(running_max, jnp.max(scores, -1))
    rescale = jnp.exp(running_max - new_max)
    expo = jnp.exp(scores - new_max[..., None])
    new_sum = running_sum * rescale + jnp.sum(expo, -1)
    update = jnp.einsum(
        "tcgk,kcd->tcgd",
        expo.astype(jnp.bfloat16),
        values_block,
        preferred_element_type=jnp.float32,
    )
    return (new_max, new_sum, running_acc * rescale[..., None] + update)


def attention_kernel(scalars, q_ref, qtok_ref, cache_ref, kn_ref, kp_ref, vn_ref, vp_ref, ktok_ref, out_ref):
    scale = q_ref.shape[-1] ** (-0.5)
    dims = (((1,), (1,)), ((), ()))
    q = q_ref[...]
    sources, _, depth, width = cache_ref.shape
    keys_cache = cache_ref[:, 0].reshape(sources * depth, width)
    values_cache = cache_ref[:, 1].reshape(sources * depth, width)
    cache_scores = lax.dot_general(q, keys_cache, dims, preferred_element_type=jnp.float32) * scale
    cache_pos = scalars[1] + lax.broadcasted_iota(jnp.int32, (1, sources * depth), 1)
    cache_seen = cache_pos < scalars[0]
    cache_scores = jnp.where(cache_seen, cache_scores, masked_score)
    keys_new = jnp.concatenate([kn_ref[...], kp_ref[...]], 0)
    values_new = jnp.concatenate([vn_ref[...], vp_ref[...]], 0)
    new_scores = lax.dot_general(q, keys_new, dims, preferred_element_type=jnp.float32) * scale
    new_seen = ktok_ref[...] <= qtok_ref[...]
    new_scores = jnp.where(new_seen, new_scores, masked_score)
    top = jnp.maximum(
        jnp.max(cache_scores, 1, keepdims=True), jnp.max(new_scores, 1, keepdims=True)
    )
    cache_expo = jnp.where(cache_seen, jnp.exp(cache_scores - top), 0.0)
    new_expo = jnp.where(new_seen, jnp.exp(new_scores - top), 0.0)
    total = jnp.sum(cache_expo, 1, keepdims=True) + jnp.sum(new_expo, 1, keepdims=True)
    acc = jnp.dot(
        cache_expo.astype(jnp.bfloat16), values_cache, preferred_element_type=jnp.float32
    ) + jnp.dot(new_expo.astype(jnp.bfloat16), values_new, preferred_element_type=jnp.float32)
    rows, width = acc.shape
    top_t = jnp.transpose(jnp.broadcast_to(top, (rows, width)))[0:1]
    total_t = jnp.transpose(jnp.broadcast_to(total, (rows, width)))[0:1]
    out_ref[0, :rows, :] = acc
    for half in range(rows // width):
        cols = slice(half * width, (half + 1) * width)
        out_ref[0, rows + half : rows + half + 1, :] = top_t[:, cols]
        out_ref[0, rows + rows // width + half : rows + rows // width + half + 1, :] = total_t[:, cols]


def attention(scalars, q_rows, q_tok, cache_both, keys_new, keys_partner, values_new, values_partner, key_tok):
    rows, width = q_rows.shape
    cache_rows = cache_both.shape[0] * cache_both.shape[2]
    new_rows = 2 * keys_new.shape[0]
    block = 256
    packed_rows = block + 2 * (block // width)
    full = lambda shape: pl.BlockSpec(shape, lambda i, s: (0, 0))
    row_block = lambda cols: pl.BlockSpec((block, cols), lambda i, s: (i, 0))
    flops = 4 * rows * (cache_rows + new_rows) * width
    return pl.pallas_call(
        attention_kernel,
        out_shape=jax.ShapeDtypeStruct((rows // block, packed_rows, width), jnp.float32),
        grid_spec=pltpu.PrefetchScalarGridSpec(
            num_scalar_prefetch=1,
            grid=(rows // block,),
            in_specs=[
                row_block(width),
                row_block(1),
                pl.BlockSpec(cache_both.shape, lambda i, s: (0, 0, 0, 0)),
                full((new_rows // 2, width)),
                full((new_rows // 2, width)),
                full((new_rows // 2, width)),
                full((new_rows // 2, width)),
                full((1, new_rows)),
            ],
            out_specs=pl.BlockSpec((1, packed_rows, width), lambda i, s: (i, 0, 0)),
        ),
        cost_estimate=pl.CostEstimate(
            flops=flops,
            transcendentals=rows * (cache_rows + new_rows),
            bytes_accessed=2 * (rows + 2 * cache_rows + 2 * new_rows) * width + 4 * rows * width,
        ),
    )(scalars, q_rows, q_tok, cache_both, keys_new, keys_partner, values_new, values_partner, key_tok)


def per_device(
    hidden_in,
    norm_gain,
    w_query,
    w_key,
    w_value,
    w_headgate,
    w_out,
    q_gain,
    k_gain,
    cache_keys,
    cache_values,
    cached_len,
    group_of,
):
    tok_rows = hidden_in.shape[0]
    head_dim = q_gain.shape[0]
    kv_local = w_key.shape[1] // head_dim
    heads_local = w_query.shape[1] // head_dim
    group_size = heads_local // kv_local
    per_request = SPAN // tok_rows
    ring_x = lax.axis_size("sx")
    ring_z = lax.axis_size("sz")
    req_count = ring_x * ring_z // per_request
    pair = ring_z // req_count
    x_index = lax.axis_index("sx")
    z_index = lax.axis_index("sz")
    seq_index = x_index * ring_z + z_index
    request = seq_index % req_count
    local_part = seq_index // req_count
    parity = z_index // req_count
    length = cached_len[request]

    peer_groups = group_of[jnp.arange(ring_z, dtype=jnp.int32) % req_count]
    cache_both = jnp.stack([cache_keys, cache_values], 1)
    incoming = lax.all_to_all(cache_both[peer_groups], "sz", 0, 0, tiled=True)
    cache_rows = ring_z * cache_keys.shape[1]
    keys_cache = incoming[:, 0].reshape(cache_rows, kv_local, head_dim)
    values_cache = incoming[:, 1].reshape(cache_rows, kv_local, head_dim)
    cache_pos = x_index * cache_rows + jnp.arange(cache_rows, dtype=jnp.int32)

    gathered = lax.all_gather(hidden_in, "tp", axis=1, tiled=True)
    widened = gathered.astype(jnp.float32)
    normed = (
        widened * lax.rsqrt(jnp.mean(widened * widened, -1, keepdims=True) + norm_eps) * norm_gain
    ).astype(jnp.bfloat16)
    positions = length + local_part * tok_rows + jnp.arange(tok_rows, dtype=jnp.int32)
    query_raw = jnp.dot(normed, w_query, preferred_element_type=jnp.float32).reshape(
        tok_rows, kv_local, group_size, head_dim
    )
    queries = rotate(head_norm(query_raw, q_gain), positions).astype(jnp.bfloat16)
    key_raw = jnp.dot(normed, w_key, preferred_element_type=jnp.float32).reshape(
        tok_rows, kv_local, head_dim
    )
    keys_new = rotate(head_norm(key_raw, k_gain), positions).astype(jnp.bfloat16)
    values_new = (
        jnp.dot(normed, w_value, preferred_element_type=jnp.float32)
        .astype(jnp.bfloat16)
        .reshape(tok_rows, kv_local, head_dim)
    )
    gates = jax.nn.sigmoid(jnp.dot(normed, w_headgate, preferred_element_type=jnp.float32)).reshape(
        tok_rows, kv_local, group_size
    )

    partner_pairs = [(z, (z + req_count) % ring_z) for z in range(ring_z)]
    partner_kv = lax.ppermute(jnp.stack([keys_new, values_new]), "sz", partner_pairs)
    partner_part = x_index * pair + (pair - 1 - parity)
    all_queries = lax.all_gather(queries, "sx", axis=0, tiled=True)
    query_tok = (
        (jnp.arange(ring_x, dtype=jnp.int32) * pair + parity)[:, None] * tok_rows
        + jnp.arange(tok_rows, dtype=jnp.int32)[None, :]
    ).reshape(-1)
    row_ids = jnp.arange(tok_rows, dtype=jnp.int32)
    key_tok = jnp.concatenate([local_part * tok_rows + row_ids, partner_part * tok_rows + row_ids])
    keys_two = jnp.concatenate([keys_new, partner_kv[0]], 0).reshape(-1, head_dim)
    values_two = jnp.concatenate([values_new, partner_kv[1]], 0).reshape(-1, head_dim)
    query_count = query_tok.shape[0]
    scalars = jnp.stack([length, x_index * cache_rows]).astype(jnp.int32)
    packed = attention(
        scalars,
        all_queries.reshape(-1, head_dim),
        jnp.repeat(query_tok, heads_local)[:, None],
        incoming,
        keys_new.reshape(-1, head_dim),
        partner_kv[0].reshape(-1, head_dim),
        values_new.reshape(-1, head_dim),
        partner_kv[1].reshape(-1, head_dim),
        key_tok[None, :],
    )
    slot_rows = tok_rows * heads_local
    packed_in = lax.all_to_all(packed, "sx", 0, 0, tiled=True)
    acc_in = packed_in[:, :slot_rows].reshape(ring_x, tok_rows, kv_local, group_size, head_dim)
    stats_in = packed_in[:, slot_rows:].reshape(ring_x, 2, tok_rows, kv_local, group_size)
    stats_in = jnp.moveaxis(stats_in, 1, -1)
    best = jnp.max(stats_in[..., 0], 0)
    factor = jnp.exp(stats_in[..., 0] - best[None])
    total = jnp.sum(stats_in[..., 1] * factor, 0)
    summed_acc = jnp.sum(acc_in * factor[..., None], 0)
    mixed = (
        (summed_acc / total[..., None] * gates[..., None])
        .astype(jnp.bfloat16)
        .reshape(tok_rows, heads_local * head_dim)
    )
    partial_out = jnp.dot(mixed, w_out, preferred_element_type=jnp.float32)
    tp_size = lax.axis_size("tp")
    pieces = partial_out.astype(jnp.bfloat16).reshape(tok_rows, tp_size, -1)
    arrived = lax.all_to_all(pieces, "tp", 1, 1, tiled=True)
    summed = jnp.sum(arrived.astype(jnp.float32), 1)
    return (hidden_in.astype(jnp.float32) + summed).astype(jnp.bfloat16)


def solution(mesh):
    seq_size = mesh.shape["seq"]
    tp_size = mesh.shape["tp"]
    req_count = seq_size // (SPAN // 128)
    ring_z = 2 * req_count
    ring_x = seq_size // ring_z
    split_mesh = Mesh(mesh.devices.reshape(ring_x, ring_z, tp_size), ("sx", "sz", "tp"))
    seq = ("sx", "sz")
    in_specs = (
        P(seq, "tp"),
        P(),
        P(None, "tp"),
        P(None, "tp"),
        P(None, "tp"),
        P(None, "tp"),
        P("tp", None),
        P(),
        P(),
        P(None, seq, "tp"),
        P(None, seq, "tp"),
        P(),
        P(),
    )
    out_specs = P(seq, "tp")
    return jax.shard_map(
        per_device, mesh=split_mesh, in_specs=in_specs, out_specs=out_specs, check_vma=False
    )
```

```python
import math

import jax
import jax.numpy as jnp
from jax import lax
from jax.experimental import pallas as pl
from jax.experimental.pallas import tpu as pltpu
from jax.sharding import Mesh, PartitionSpec as P

SPAN = 1024


norm_eps = 1e-06
rope_base = 1000000.0
masked_score = -1e30


def shifted(value, axis, by):
    peers = lax.axis_size(axis)
    pairs = [(i, i + by) for i in range(peers) if 0 <= i + by < peers]
    return lax.ppermute(value, axis, pairs)


def head_norm(vec, gain):
    return vec * lax.rsqrt(jnp.mean(vec * vec, -1, keepdims=True) + norm_eps) * gain


def rotate(vec, positions):
    half = vec.shape[-1] // 2
    freq = jnp.exp(
        jnp.arange(half, dtype=jnp.float32) * (-2.0 * math.log(rope_base) / vec.shape[-1])
    )
    angle = positions.astype(jnp.float32)[:, None] * freq[None, :]
    shape_out = (vec.shape[0],) + (1,) * (vec.ndim - 2) + (half,)
    cosine = jnp.cos(angle).reshape(shape_out)
    sine = jnp.sin(angle).reshape(shape_out)
    first = vec[..., :half]
    second = vec[..., half:]
    return jnp.concatenate([first * cosine - second * sine, second * cosine + first * sine], -1)


def attend(state_now, queries, keys_block, values_block, visible):
    running_max, running_sum, running_acc = state_now
    scores = jnp.einsum(
        "tcgd,kcd->tcgk", queries, keys_block, preferred_element_type=jnp.float32
    ) * queries.shape[-1] ** (-0.5)
    scores = jnp.where(visible[:, None, None, :], scores, masked_score)
    new_max = jnp.maximum(running_max, jnp.max(scores, -1))
    rescale = jnp.exp(running_max - new_max)
    expo = jnp.exp(scores - new_max[..., None])
    new_sum = running_sum * rescale + jnp.sum(expo, -1)
    update = jnp.einsum(
        "tcgk,kcd->tcgd",
        expo.astype(jnp.bfloat16),
        values_block,
        preferred_element_type=jnp.float32,
    )
    return (new_max, new_sum, running_acc * rescale[..., None] + update)


def attention_kernel(
    scalars, q_ref, qtok_ref, cache_hbm, kn_ref, kp_ref, vn_ref, vp_ref, ktok_ref, out_ref, cache_ref, sems
):
    first = pl.program_id(0) == 0
    key_copy = pltpu.make_async_copy(cache_hbm.at[:, 0], cache_ref.at[:, 0], sems.at[0])
    value_copy = pltpu.make_async_copy(cache_hbm.at[:, 1], cache_ref.at[:, 1], sems.at[1])

    @pl.when(first)
    def _():
        key_copy.start()
        value_copy.start()
        key_copy.wait()

    scale = q_ref.shape[-1] ** (-0.5)
    dims = (((1,), (1,)), ((), ()))
    q = q_ref[...]
    sources, _, depth, width = cache_ref.shape
    keys_cache = cache_ref[:, 0].reshape(sources * depth, width)
    cache_scores = lax.dot_general(q, keys_cache, dims, preferred_element_type=jnp.float32) * scale
    cache_pos = scalars[1] + lax.broadcasted_iota(jnp.int32, (1, sources * depth), 1)
    cache_seen = cache_pos < scalars[0]
    cache_scores = jnp.where(cache_seen, cache_scores, masked_score)
    keys_new = jnp.concatenate([kn_ref[...], kp_ref[...]], 0)
    values_new = jnp.concatenate([vn_ref[...], vp_ref[...]], 0)
    new_scores = lax.dot_general(q, keys_new, dims, preferred_element_type=jnp.float32) * scale
    new_seen = ktok_ref[...] <= qtok_ref[...]
    new_scores = jnp.where(new_seen, new_scores, masked_score)
    top = jnp.maximum(
        jnp.max(cache_scores, 1, keepdims=True), jnp.max(new_scores, 1, keepdims=True)
    )
    cache_expo = jnp.where(cache_seen, jnp.exp(cache_scores - top), 0.0)
    new_expo = jnp.where(new_seen, jnp.exp(new_scores - top), 0.0)
    total = jnp.sum(cache_expo, 1, keepdims=True) + jnp.sum(new_expo, 1, keepdims=True)

    @pl.when(first)
    def _():
        value_copy.wait()

    values_cache = cache_ref[:, 1].reshape(sources * depth, width)
    acc = jnp.dot(
        cache_expo.astype(jnp.bfloat16), values_cache, preferred_element_type=jnp.float32
    ) + jnp.dot(new_expo.astype(jnp.bfloat16), values_new, preferred_element_type=jnp.float32)
    rows, width = acc.shape
    top_t = jnp.transpose(jnp.broadcast_to(top, (rows, width)))[0:1]
    total_t = jnp.transpose(jnp.broadcast_to(total, (rows, width)))[0:1]
    out_ref[0, :rows, :] = acc
    for half in range(rows // width):
        cols = slice(half * width, (half + 1) * width)
        out_ref[0, rows + half : rows + half + 1, :] = top_t[:, cols]
        out_ref[0, rows + rows // width + half : rows + rows // width + half + 1, :] = total_t[:, cols]


def attention(scalars, q_rows, q_tok, cache_both, keys_new, keys_partner, values_new, values_partner, key_tok):
    rows, width = q_rows.shape
    cache_rows = cache_both.shape[0] * cache_both.shape[2]
    new_rows = 2 * keys_new.shape[0]
    block = 256
    packed_rows = block + 2 * (block // width)
    full = lambda shape: pl.BlockSpec(shape, lambda i, s: (0, 0))
    row_block = lambda cols: pl.BlockSpec((block, cols), lambda i, s: (i, 0))
    flops = 4 * rows * (cache_rows + new_rows) * width
    return pl.pallas_call(
        attention_kernel,
        out_shape=jax.ShapeDtypeStruct((rows // block, packed_rows, width), jnp.float32),
        grid_spec=pltpu.PrefetchScalarGridSpec(
            num_scalar_prefetch=1,
            grid=(rows // block,),
            in_specs=[
                row_block(width),
                row_block(1),
                pl.BlockSpec(memory_space=pl.ANY),
                full((new_rows // 2, width)),
                full((new_rows // 2, width)),
                full((new_rows // 2, width)),
                full((new_rows // 2, width)),
                full((1, new_rows)),
            ],
            out_specs=pl.BlockSpec((1, packed_rows, width), lambda i, s: (i, 0, 0)),
            scratch_shapes=[
                pltpu.VMEM(cache_both.shape, cache_both.dtype),
                pltpu.SemaphoreType.DMA((2,)),
            ],
        ),
        cost_estimate=pl.CostEstimate(
            flops=flops,
            transcendentals=rows * (cache_rows + new_rows),
            bytes_accessed=2 * (rows + 2 * cache_rows + 2 * new_rows) * width + 4 * rows * width,
        ),
    )(scalars, q_rows, q_tok, cache_both, keys_new, keys_partner, values_new, values_partner, key_tok)


def per_device(
    hidden_in,
    norm_gain,
    w_query,
    w_key,
    w_value,
    w_headgate,
    w_out,
    q_gain,
    k_gain,
    cache_keys,
    cache_values,
    cached_len,
    group_of,
):
    tok_rows = hidden_in.shape[0]
    head_dim = q_gain.shape[0]
    kv_local = w_key.shape[1] // head_dim
    heads_local = w_query.shape[1] // head_dim
    group_size = heads_local // kv_local
    per_request = SPAN // tok_rows
    ring_x = lax.axis_size("sx")
    ring_z = lax.axis_size("sz")
    req_count = ring_x * ring_z // per_request
    pair = ring_z // req_count
    x_index = lax.axis_index("sx")
    z_index = lax.axis_index("sz")
    seq_index = x_index * ring_z + z_index
    request = seq_index % req_count
    local_part = seq_index // req_count
    parity = z_index // req_count
    length = cached_len[request]

    peer_groups = group_of[jnp.arange(ring_z, dtype=jnp.int32) % req_count]
    cache_both = jnp.stack([cache_keys, cache_values], 1)
    incoming = lax.all_to_all(cache_both[peer_groups], "sz", 0, 0, tiled=True)
    cache_rows = ring_z * cache_keys.shape[1]
    keys_cache = incoming[:, 0].reshape(cache_rows, kv_local, head_dim)
    values_cache = incoming[:, 1].reshape(cache_rows, kv_local, head_dim)
    cache_pos = x_index * cache_rows + jnp.arange(cache_rows, dtype=jnp.int32)

    gathered = lax.all_gather(hidden_in, "tp", axis=1, tiled=True)
    widened = gathered.astype(jnp.float32)
    normed = (
        widened * lax.rsqrt(jnp.mean(widened * widened, -1, keepdims=True) + norm_eps) * norm_gain
    ).astype(jnp.bfloat16)
    positions = length + local_part * tok_rows + jnp.arange(tok_rows, dtype=jnp.int32)
    query_raw = jnp.dot(normed, w_query, preferred_element_type=jnp.float32).reshape(
        tok_rows, kv_local, group_size, head_dim
    )
    queries = rotate(head_norm(query_raw, q_gain), positions).astype(jnp.bfloat16)
    key_raw = jnp.dot(normed, w_key, preferred_element_type=jnp.float32).reshape(
        tok_rows, kv_local, head_dim
    )
    keys_new = rotate(head_norm(key_raw, k_gain), positions).astype(jnp.bfloat16)
    values_new = (
        jnp.dot(normed, w_value, preferred_element_type=jnp.float32)
        .astype(jnp.bfloat16)
        .reshape(tok_rows, kv_local, head_dim)
    )
    gates = jax.nn.sigmoid(jnp.dot(normed, w_headgate, preferred_element_type=jnp.float32)).reshape(
        tok_rows, kv_local, group_size
    )

    partner_pairs = [(z, (z + req_count) % ring_z) for z in range(ring_z)]
    partner_kv = lax.ppermute(jnp.stack([keys_new, values_new]), "sz", partner_pairs)
    partner_part = x_index * pair + (pair - 1 - parity)
    all_queries = lax.all_gather(queries, "sx", axis=0, tiled=True)
    query_tok = (
        (jnp.arange(ring_x, dtype=jnp.int32) * pair + parity)[:, None] * tok_rows
        + jnp.arange(tok_rows, dtype=jnp.int32)[None, :]
    ).reshape(-1)
    row_ids = jnp.arange(tok_rows, dtype=jnp.int32)
    key_tok = jnp.concatenate([local_part * tok_rows + row_ids, partner_part * tok_rows + row_ids])
    keys_two = jnp.concatenate([keys_new, partner_kv[0]], 0).reshape(-1, head_dim)
    values_two = jnp.concatenate([values_new, partner_kv[1]], 0).reshape(-1, head_dim)
    query_count = query_tok.shape[0]
    scalars = jnp.stack([length, x_index * cache_rows]).astype(jnp.int32)
    packed = attention(
        scalars,
        all_queries.reshape(-1, head_dim),
        jnp.repeat(query_tok, heads_local)[:, None],
        incoming,
        keys_new.reshape(-1, head_dim),
        partner_kv[0].reshape(-1, head_dim),
        values_new.reshape(-1, head_dim),
        partner_kv[1].reshape(-1, head_dim),
        key_tok[None, :],
    )
    slot_rows = tok_rows * heads_local
    packed_in = lax.all_to_all(packed, "sx", 0, 0, tiled=True)
    acc_in = packed_in[:, :slot_rows].reshape(ring_x, tok_rows, kv_local, group_size, head_dim)
    stats_in = packed_in[:, slot_rows:].reshape(ring_x, 2, tok_rows, kv_local, group_size)
    stats_in = jnp.moveaxis(stats_in, 1, -1)
    best = jnp.max(stats_in[..., 0], 0)
    factor = jnp.exp(stats_in[..., 0] - best[None])
    total = jnp.sum(stats_in[..., 1] * factor, 0)
    summed_acc = jnp.sum(acc_in * factor[..., None], 0)
    mixed = (
        (summed_acc / total[..., None] * gates[..., None])
        .astype(jnp.bfloat16)
        .reshape(tok_rows, heads_local * head_dim)
    )
    partial_out = jnp.dot(mixed, w_out, preferred_element_type=jnp.float32)
    tp_size = lax.axis_size("tp")
    pieces = partial_out.astype(jnp.bfloat16).reshape(tok_rows, tp_size, -1)
    arrived = lax.all_to_all(pieces, "tp", 1, 1, tiled=True)
    summed = jnp.sum(arrived.astype(jnp.float32), 1)
    return (hidden_in.astype(jnp.float32) + summed).astype(jnp.bfloat16)


def solution(mesh):
    seq_size = mesh.shape["seq"]
    tp_size = mesh.shape["tp"]
    req_count = seq_size // (SPAN // 128)
    ring_z = 2 * req_count
    ring_x = seq_size // ring_z
    split_mesh = Mesh(mesh.devices.reshape(ring_x, ring_z, tp_size), ("sx", "sz", "tp"))
    seq = ("sx", "sz")
    in_specs = (
        P(seq, "tp"),
        P(),
        P(None, "tp"),
        P(None, "tp"),
        P(None, "tp"),
        P(None, "tp"),
        P("tp", None),
        P(),
        P(),
        P(None, seq, "tp"),
        P(None, seq, "tp"),
        P(),
        P(),
    )
    out_specs = P(seq, "tp")
    return jax.shard_map(
        per_device, mesh=split_mesh, in_specs=in_specs, out_specs=out_specs, check_vma=False
    )
```

```python
import math

import jax
import jax.numpy as jnp
from jax import lax
from jax.experimental import pallas as pl
from jax.experimental.pallas import tpu as pltpu
from jax.sharding import Mesh, PartitionSpec as P

SPAN = 1024


norm_eps = 1e-06
rope_base = 1000000.0
masked_score = -1e30


def shifted(value, axis, by):
    peers = lax.axis_size(axis)
    pairs = [(i, i + by) for i in range(peers) if 0 <= i + by < peers]
    return lax.ppermute(value, axis, pairs)


def head_norm(vec, gain):
    return vec * lax.rsqrt(jnp.mean(vec * vec, -1, keepdims=True) + norm_eps) * gain


def rotate(vec, positions):
    half = vec.shape[-1] // 2
    freq = jnp.exp(
        jnp.arange(half, dtype=jnp.float32) * (-2.0 * math.log(rope_base) / vec.shape[-1])
    )
    angle = positions.astype(jnp.float32)[:, None] * freq[None, :]
    shape_out = (vec.shape[0],) + (1,) * (vec.ndim - 2) + (half,)
    cosine = jnp.cos(angle).reshape(shape_out)
    sine = jnp.sin(angle).reshape(shape_out)
    first = vec[..., :half]
    second = vec[..., half:]
    return jnp.concatenate([first * cosine - second * sine, second * cosine + first * sine], -1)


def attend(state_now, queries, keys_block, values_block, visible):
    running_max, running_sum, running_acc = state_now
    scores = jnp.einsum(
        "tcgd,kcd->tcgk", queries, keys_block, preferred_element_type=jnp.float32
    ) * queries.shape[-1] ** (-0.5)
    scores = jnp.where(visible[:, None, None, :], scores, masked_score)
    new_max = jnp.maximum(running_max, jnp.max(scores, -1))
    rescale = jnp.exp(running_max - new_max)
    expo = jnp.exp(scores - new_max[..., None])
    new_sum = running_sum * rescale + jnp.sum(expo, -1)
    update = jnp.einsum(
        "tcgk,kcd->tcgd",
        expo.astype(jnp.bfloat16),
        values_block,
        preferred_element_type=jnp.float32,
    )
    return (new_max, new_sum, running_acc * rescale[..., None] + update)


def attention_kernel(scalars, q_ref, qtok_ref, cache_ref, kn_ref, kp_ref, vn_ref, vp_ref, ktok_ref, out_ref):
    scale = q_ref.shape[-1] ** (-0.5)
    dims = (((1,), (1,)), ((), ()))
    q = q_ref[...]
    sources, _, depth, width = cache_ref.shape
    keys_cache = cache_ref[:, 0].reshape(sources * depth, width)
    values_cache = cache_ref[:, 1].reshape(sources * depth, width)
    cache_scores = lax.dot_general(q, keys_cache, dims, preferred_element_type=jnp.float32) * scale
    cache_pos = scalars[1] + lax.broadcasted_iota(jnp.int32, (1, sources * depth), 1)
    cache_seen = cache_pos < scalars[0]
    cache_scores = jnp.where(cache_seen, cache_scores, masked_score)
    keys_new = jnp.concatenate([kn_ref[...], kp_ref[...]], 0)
    values_new = jnp.concatenate([vn_ref[...], vp_ref[...]], 0)
    new_scores = lax.dot_general(q, keys_new, dims, preferred_element_type=jnp.float32) * scale
    new_seen = ktok_ref[...] <= qtok_ref[...]
    new_scores = jnp.where(new_seen, new_scores, masked_score)
    top = jnp.maximum(
        jnp.max(cache_scores, 1, keepdims=True), jnp.max(new_scores, 1, keepdims=True)
    )
    cache_expo = jnp.where(cache_seen, jnp.exp(cache_scores - top), 0.0)
    new_expo = jnp.where(new_seen, jnp.exp(new_scores - top), 0.0)
    total = jnp.sum(cache_expo, 1, keepdims=True) + jnp.sum(new_expo, 1, keepdims=True)
    acc = jnp.dot(
        cache_expo.astype(jnp.bfloat16), values_cache, preferred_element_type=jnp.float32
    ) + jnp.dot(new_expo.astype(jnp.bfloat16), values_new, preferred_element_type=jnp.float32)
    rows, width = acc.shape
    top_t = jnp.transpose(jnp.broadcast_to(top, (rows, width)))[0:1]
    total_t = jnp.transpose(jnp.broadcast_to(total, (rows, width)))[0:1]
    out_ref[0, :rows, :] = acc
    for half in range(rows // width):
        cols = slice(half * width, (half + 1) * width)
        out_ref[0, rows + half : rows + half + 1, :] = top_t[:, cols]
        out_ref[0, rows + rows // width + half : rows + rows // width + half + 1, :] = total_t[:, cols]


def attention(scalars, q_rows, q_tok, cache_both, keys_new, keys_partner, values_new, values_partner, key_tok):
    rows, width = q_rows.shape
    cache_rows = cache_both.shape[0] * cache_both.shape[2]
    new_rows = 2 * keys_new.shape[0]
    block = 256
    packed_rows = block + 2 * (block // width)
    full = lambda shape: pl.BlockSpec(shape, lambda i, s: (0, 0))
    row_block = lambda cols: pl.BlockSpec((block, cols), lambda i, s: (i, 0))
    flops = 4 * rows * (cache_rows + new_rows) * width
    return pl.pallas_call(
        attention_kernel,
        out_shape=jax.ShapeDtypeStruct((rows // block, packed_rows, width), jnp.float32),
        grid_spec=pltpu.PrefetchScalarGridSpec(
            num_scalar_prefetch=1,
            grid=(rows // block,),
            in_specs=[
                row_block(width),
                row_block(1),
                pl.BlockSpec(cache_both.shape, lambda i, s: (0, 0, 0, 0)),
                full((new_rows // 2, width)),
                full((new_rows // 2, width)),
                full((new_rows // 2, width)),
                full((new_rows // 2, width)),
                full((1, new_rows)),
            ],
            out_specs=pl.BlockSpec((1, packed_rows, width), lambda i, s: (i, 0, 0)),
        ),
        cost_estimate=pl.CostEstimate(
            flops=flops,
            transcendentals=rows * (cache_rows + new_rows),
            bytes_accessed=2 * (rows + 2 * cache_rows + 2 * new_rows) * width + 4 * rows * width,
        ),
    )(scalars, q_rows, q_tok, cache_both, keys_new, keys_partner, values_new, values_partner, key_tok)


def per_device(
    hidden_in,
    norm_gain,
    w_query,
    w_key,
    w_value,
    w_headgate,
    w_out,
    q_gain,
    k_gain,
    cache_keys,
    cache_values,
    cached_len,
    group_of,
):
    tok_rows = hidden_in.shape[0]
    head_dim = q_gain.shape[0]
    kv_local = w_key.shape[1] // head_dim
    heads_local = w_query.shape[1] // head_dim
    group_size = heads_local // kv_local
    per_request = SPAN // tok_rows
    ring_x = lax.axis_size("sx")
    ring_z = lax.axis_size("sz")
    req_count = ring_x * ring_z // per_request
    pair = ring_z // req_count
    x_index = lax.axis_index("sx")
    z_index = lax.axis_index("sz")
    seq_index = x_index * ring_z + z_index
    request = seq_index % req_count
    local_part = seq_index // req_count
    parity = z_index // req_count
    length = cached_len[request]

    peer_groups = group_of[jnp.arange(ring_z, dtype=jnp.int32) % req_count]
    cache_both = jnp.stack([cache_keys, cache_values], 1)
    outgoing = jnp.where((peer_groups == 0)[:, None, None, None], cache_both[0], cache_both[1])
    incoming = lax.all_to_all(outgoing, "sz", 0, 0, tiled=True)
    cache_rows = ring_z * cache_keys.shape[1]
    keys_cache = incoming[:, 0].reshape(cache_rows, kv_local, head_dim)
    values_cache = incoming[:, 1].reshape(cache_rows, kv_local, head_dim)
    cache_pos = x_index * cache_rows + jnp.arange(cache_rows, dtype=jnp.int32)

    gathered = lax.all_gather(hidden_in, "tp", axis=1, tiled=True)
    widened = gathered.astype(jnp.float32)
    normed = (
        widened * lax.rsqrt(jnp.mean(widened * widened, -1, keepdims=True) + norm_eps) * norm_gain
    ).astype(jnp.bfloat16)
    positions = length + local_part * tok_rows + jnp.arange(tok_rows, dtype=jnp.int32)
    query_raw = jnp.dot(normed, w_query, preferred_element_type=jnp.float32).reshape(
        tok_rows, kv_local, group_size, head_dim
    )
    queries = rotate(head_norm(query_raw, q_gain), positions).astype(jnp.bfloat16)
    key_raw = jnp.dot(normed, w_key, preferred_element_type=jnp.float32).reshape(
        tok_rows, kv_local, head_dim
    )
    keys_new = rotate(head_norm(key_raw, k_gain), positions).astype(jnp.bfloat16)
    values_new = (
        jnp.dot(normed, w_value, preferred_element_type=jnp.float32)
        .astype(jnp.bfloat16)
        .reshape(tok_rows, kv_local, head_dim)
    )
    gates = jax.nn.sigmoid(jnp.dot(normed, w_headgate, preferred_element_type=jnp.float32)).reshape(
        tok_rows, kv_local, group_size
    )

    partner_pairs = [(z, (z + req_count) % ring_z) for z in range(ring_z)]
    partner_kv = lax.ppermute(jnp.stack([keys_new, values_new]), "sz", partner_pairs)
    partner_part = x_index * pair + (pair - 1 - parity)
    all_queries = lax.all_gather(queries, "sx", axis=0, tiled=True)
    query_tok = (
        (jnp.arange(ring_x, dtype=jnp.int32) * pair + parity)[:, None] * tok_rows
        + jnp.arange(tok_rows, dtype=jnp.int32)[None, :]
    ).reshape(-1)
    row_ids = jnp.arange(tok_rows, dtype=jnp.int32)
    key_tok = jnp.concatenate([local_part * tok_rows + row_ids, partner_part * tok_rows + row_ids])
    keys_two = jnp.concatenate([keys_new, partner_kv[0]], 0).reshape(-1, head_dim)
    values_two = jnp.concatenate([values_new, partner_kv[1]], 0).reshape(-1, head_dim)
    query_count = query_tok.shape[0]
    scalars = jnp.stack([length, x_index * cache_rows]).astype(jnp.int32)
    packed = attention(
        scalars,
        all_queries.reshape(-1, head_dim),
        jnp.repeat(query_tok, heads_local)[:, None],
        incoming,
        keys_new.reshape(-1, head_dim),
        partner_kv[0].reshape(-1, head_dim),
        values_new.reshape(-1, head_dim),
        partner_kv[1].reshape(-1, head_dim),
        key_tok[None, :],
    )
    slot_rows = tok_rows * heads_local
    packed_in = lax.all_to_all(packed, "sx", 0, 0, tiled=True)
    acc_in = packed_in[:, :slot_rows].reshape(ring_x, tok_rows, kv_local, group_size, head_dim)
    stats_in = packed_in[:, slot_rows:].reshape(ring_x, 2, tok_rows, kv_local, group_size)
    stats_in = jnp.moveaxis(stats_in, 1, -1)
    best = jnp.max(stats_in[..., 0], 0)
    factor = jnp.exp(stats_in[..., 0] - best[None])
    total = jnp.sum(stats_in[..., 1] * factor, 0)
    summed_acc = jnp.sum(acc_in * factor[..., None], 0)
    mixed = (
        (summed_acc / total[..., None] * gates[..., None])
        .astype(jnp.bfloat16)
        .reshape(tok_rows, heads_local * head_dim)
    )
    partial_out = jnp.dot(mixed, w_out, preferred_element_type=jnp.float32)
    tp_size = lax.axis_size("tp")
    pieces = partial_out.astype(jnp.bfloat16).reshape(tok_rows, tp_size, -1)
    arrived = lax.all_to_all(pieces, "tp", 1, 1, tiled=True)
    summed = jnp.sum(arrived.astype(jnp.float32), 1)
    return (hidden_in.astype(jnp.float32) + summed).astype(jnp.bfloat16)


def solution(mesh):
    seq_size = mesh.shape["seq"]
    tp_size = mesh.shape["tp"]
    req_count = seq_size // (SPAN // 128)
    ring_z = 2 * req_count
    ring_x = seq_size // ring_z
    split_mesh = Mesh(mesh.devices.reshape(ring_x, ring_z, tp_size), ("sx", "sz", "tp"))
    seq = ("sx", "sz")
    in_specs = (
        P(seq, "tp"),
        P(),
        P(None, "tp"),
        P(None, "tp"),
        P(None, "tp"),
        P(None, "tp"),
        P("tp", None),
        P(),
        P(),
        P(None, seq, "tp"),
        P(None, seq, "tp"),
        P(),
        P(),
    )
    out_specs = P(seq, "tp")
    return jax.shard_map(
        per_device, mesh=split_mesh, in_specs=in_specs, out_specs=out_specs, check_vma=False
    )
```
